32 devices in a mesh: pole: 2 (over x), row: 8 (over z, y), col: 2 (over core).
Axes of the slice: x: 2, y: 2, z: 4, core: 2. Of those that a mesh axis runs over, the one named last changes fastest.
Arguments:
- anc_inverse: bfloat16 [2048, 1024], P(('pole', 'row')), parts along dimension 0, as said below
- parent_pivinv: float32 [2048, 1024], P(('pole', 'row')), parts along dimension 0, as said below
- parent_lower: bfloat16 [2048, 1024], P(('pole', 'row')), parts along dimension 0, may hold values from -0.1875 to 0.1875
- parent_mask: int32 [4], replicated, may hold values 0 or 1
- leaf_lower_par: bfloat16 [2048, 1024], P(('pole', 'row')), parts along dimension 0, may hold values from -0.125 to 0.125
- leaf_lower_anc: bfloat16 [2048, 1024], P(('pole', 'row')), parts along dimension 0, may hold values from -0.125 to 0.125
- leaf_mask: int32 [8], replicated, may hold values 0 or 1
- leaf_pivots: float32 [2048], P(('pole', 'col')), parts along dimension 0, may hold values from 0.5 to 2
Outputs:
- parent_block: float32 [2048, 1024], P(('pole', 'row')), parts along dimension 0
- parent_offdiag: bfloat16 [2048, 1024], P(('pole', 'row'), 'col'), parts along dimension 0
- leaf_par_block: bfloat16 [2048, 1024], P(('pole', 'row'), 'col'), parts along dimension 0
- leaf_anc_block: bfloat16 [2048, 1024], P(('pole', 'row'), 'col'), parts along dimension 0
- density: float32 [2048], P(('pole', 'col')), parts along dimension 0
The draws below stay inside these ranges and needn't reach their ends.
There are 2 independent parts, one for each index of `pole`. The reference program is written for one: setup_inputs(seed, part) draws one part's arguments, and reference() takes and returns one part's arrays. A program takes and returns all parts, laid end to end along the dimension named above; an argument that names none is the same for every part. Nothing has to cross between parts.
Inputs may be any that keep to these rules, and one draw needn't show every extreme that they name: `anc_inverse`: symmetric. `parent_pivinv`: symmetric. `parent_mask`: 1 marks a structurally nonzero block of 256 rows. `leaf_mask`: 1 marks a structurally nonzero block of 256 rows.
All inputs are finite; a program needn't handle non-finite values.
Results may differ from the reference program's by a relative error of at most 0.0095.
Values may be sent and summed in bfloat16 or wider, within the bound.
No kernel may reach another device: no remote copies, remote signals or barrier semaphores. Data moves between devices by JAX's collectives and lax.ppermute only.
A program may use at most 64 MiB of HBM per device.

```python
import math
import jax
import jax.numpy as jnp
from jax import lax

BLOCK = 256
ORDER = 1024
ANC_ROWS = 1024


def symmetric_draw(key, order_size):
    base = jax.random.normal(key, (order_size, order_size), jnp.float32)
    result = (base + base.T) * 0.7071
    return result + 2.0 * jnp.eye(order_size, dtype=jnp.float32)


def draw_anc_inverse(key, part):
    return symmetric_draw(jax.random.fold_in(key, 11), ANC_ROWS).astype(jnp.bfloat16)


def draw_parent_pivinv(key, part):
    return symmetric_draw(jax.random.fold_in(key, 23), ORDER)


def place_ends(values, key, least, top_value):
    shape = values.shape
    spot = [jax.random.randint(jax.random.fold_in(key, axis), (), 0, shape[axis]) for axis in range(len(shape))]
    values = values.at[tuple(spot)].set(least)
    longest = shape.index(max(shape))
    spot[longest] = (spot[longest] + 1) % shape[longest]
    return values.at[tuple(spot)].set(top_value)


def shard_levels(key, extent, shards, least, largest):
    gain, own = 1.0, jax.random.fold_in(key, 6)
    for axis_at, blocks in shards:
        heights = jnp.exp(jax.random.uniform(jax.random.fold_in(own, axis_at), (blocks,), jnp.float32, least / len(shards), largest / len(shards)))
        gain = gain * jnp.repeat(heights, extent[axis_at] // blocks).reshape([-1 if axis == axis_at else 1 for axis in range(len(extent))])
    return gain


def normal_values(rng, shape, deviation, reach, pieces=(), kind=jnp.bfloat16):
    loudness = shard_levels(rng, shape, pieces, -0.22, 0.18) if pieces else 1.0
    drawn = jax.random.normal(rng, shape, jnp.float32) * deviation * loudness
    return jnp.minimum(jnp.maximum(drawn, -reach), reach).astype(kind)


def setup_inputs(seed: int = 0, part: int = 0) -> dict:
    key_of = jax.random.split(jax.random.key(seed), 9)
    part_keys = jax.random.split(jax.random.fold_in(key_of[8], part), 9)
    anc_inverse = draw_anc_inverse(jax.random.fold_in(jax.random.fold_in(key_of[8], part), 71), part)
    parent_pivinv = draw_parent_pivinv(jax.random.fold_in(jax.random.fold_in(key_of[8], part), 71), part)
    parent_lower = normal_values(part_keys[2], (ANC_ROWS, ORDER), ANC_ROWS ** -0.5, 0.1875, ((0, 8),))
    parent_mask = place_ends((jax.random.randint(key_of[3], (ANC_ROWS // BLOCK,), 0, 4) < 3).astype(jnp.int32), jax.random.fold_in(key_of[3], 1), 0, 1)
    leaf_lower_par = normal_values(part_keys[4], (ORDER, ORDER), (ANC_ROWS + ORDER) ** -0.5, 0.125, ((0, 8),))
    leaf_lower_anc = normal_values(part_keys[5], (ANC_ROWS, ORDER), (ANC_ROWS + ORDER) ** -0.5, 0.125, ((0, 8),))
    leaf_mask = place_ends((jax.random.randint(key_of[6], ((ORDER + ANC_ROWS) // BLOCK,), 0, 4) < 3).astype(jnp.int32), jax.random.fold_in(key_of[6], 1), 0, 1)
    leaf_pivots = jnp.clip(jnp.exp(math.log(2.0) - 1.3862944 * jax.random.uniform(part_keys[7], (ORDER,), jnp.float32) ** shard_levels(part_keys[7], (ORDER,), ((0, 2),), -0.2, 0.2)), 0.5, 2.0)
    return dict(anc_inverse=anc_inverse, parent_pivinv=parent_pivinv, parent_lower=parent_lower, parent_mask=parent_mask, leaf_lower_par=leaf_lower_par, leaf_lower_anc=leaf_lower_anc, leaf_mask=leaf_mask, leaf_pivots=leaf_pivots)


def reference(anc_inverse, parent_pivinv, parent_lower, parent_mask, leaf_lower_par, leaf_lower_anc, leaf_mask, leaf_pivots):
    parent_gate = jnp.repeat(parent_mask, BLOCK).astype(parent_lower.dtype)
    lower_one = parent_lower * parent_gate[:, None]
    ancestor = anc_inverse.astype(jnp.float32)
    lower_full = lower_one.astype(jnp.float32)
    product = jnp.dot(ancestor, lower_full, preferred_element_type=jnp.float32)
    parent_offdiag = (-product).astype(jnp.bfloat16)
    offdiag_full = parent_offdiag.astype(jnp.float32)
    parent_block = parent_pivinv - jnp.dot(lower_full.T, offdiag_full, preferred_element_type=jnp.float32)
    parent_round = lax.optimization_barrier(parent_block.astype(jnp.bfloat16))
    round_full = parent_round.astype(jnp.float32)
    leaf_gate = jnp.repeat(leaf_mask, BLOCK)
    par_masked = leaf_lower_par * leaf_gate[:ORDER, None].astype(leaf_lower_par.dtype)
    anc_masked = leaf_lower_anc * leaf_gate[ORDER:, None].astype(leaf_lower_anc.dtype)
    par_full = par_masked.astype(jnp.float32)
    anc_full = anc_masked.astype(jnp.float32)
    upper_sum = jnp.dot(round_full, par_full, preferred_element_type=jnp.float32) + jnp.dot(offdiag_full.T, anc_full, preferred_element_type=jnp.float32)
    lower_sum = jnp.dot(offdiag_full, par_full, preferred_element_type=jnp.float32) + jnp.dot(ancestor, anc_full, preferred_element_type=jnp.float32)
    leaf_par_block = (-upper_sum).astype(jnp.bfloat16)
    leaf_anc_block = (-lower_sum).astype(jnp.bfloat16)
    column_sums = jnp.sum(par_full * leaf_par_block.astype(jnp.float32), axis=0) + jnp.sum(anc_full * leaf_anc_block.astype(jnp.float32), axis=0)
    density = leaf_pivots - column_sums
    return parent_block, parent_offdiag, leaf_par_block, leaf_anc_block, density
```

```python
import jax
import jax.numpy as jnp
from jax import lax
from jax.sharding import PartitionSpec as P

BLOCK = 256
ORDER = 1024


def local(
    anc_inverse,
    parent_pivinv,
    parent_lower,
    parent_mask,
    leaf_lower_par,
    leaf_lower_anc,
    leaf_mask,
    leaf_pivots,
):
    row_index = lax.axis_index("row")
    row_devices = lax.axis_size("row")
    col_index = lax.axis_index("col")
    anc_rows = anc_inverse.shape[0]
    order_rows = parent_pivinv.shape[0]
    col_width = leaf_pivots.shape[0]
    parent_gate = lax.dynamic_slice_in_dim(
        jnp.repeat(parent_mask, BLOCK), row_index * anc_rows, anc_rows
    )
    lower_one = parent_lower * parent_gate[:, None].astype(jnp.bfloat16)
    lower_half = lax.dynamic_slice_in_dim(lower_one, col_index * col_width, col_width, 1)
    leaf_gate = jnp.repeat(leaf_mask, BLOCK)
    gate_par = lax.dynamic_slice_in_dim(leaf_gate[:ORDER], row_index * order_rows, order_rows)
    gate_anc = lax.dynamic_slice_in_dim(leaf_gate[ORDER:], row_index * anc_rows, anc_rows)
    leaf_local = jnp.concatenate(
        [
            leaf_lower_par * gate_par[:, None].astype(jnp.bfloat16),
            leaf_lower_anc * gate_anc[:, None].astype(jnp.bfloat16),
        ],
        axis=0,
    )
    leaf_half = lax.dynamic_slice_in_dim(leaf_local, col_index * col_width, col_width, 1)
    columns = anc_inverse
    product = jnp.dot(
        columns,
        lax.all_gather(lower_half, "row", axis=0, tiled=True),
        preferred_element_type=jnp.float32,
    )
    parent_offdiag = (-product).astype(jnp.bfloat16)
    offdiag_rows = lax.all_gather(parent_offdiag, "col", axis=1, tiled=True)
    columns = lower_one
    diag_sums = lax.psum_scatter(
        lax.dot_general(
            columns, offdiag_rows, (((0,), (0,)), ((), ())), preferred_element_type=jnp.float32
        ),
        "row",
        scatter_dimension=0,
        tiled=True,
    )
    parent_block = parent_pivinv - diag_sums
    parent_round = parent_block.astype(jnp.bfloat16)
    mirrored = lax.all_to_all(offdiag_rows, "row", split_axis=1, concat_axis=0, tiled=True).T
    upper_rows = jnp.concatenate(
        [
            parent_round.reshape(order_rows, row_devices, order_rows),
            mirrored.reshape(order_rows, row_devices, anc_rows),
        ],
        axis=2,
    )
    lower_rows = jnp.concatenate(
        [
            offdiag_rows.reshape(anc_rows, row_devices, order_rows),
            anc_inverse.reshape(anc_rows, row_devices, anc_rows),
        ],
        axis=2,
    )
    inverse_rows = jnp.concatenate(
        [upper_rows.reshape(order_rows, -1), lower_rows.reshape(anc_rows, -1)], axis=0
    )
    columns = inverse_rows
    leaf_product = jnp.dot(
        columns,
        lax.all_gather(leaf_half, "row", axis=0, tiled=True),
        preferred_element_type=jnp.float32,
    )
    leaf_result = (-leaf_product).astype(jnp.bfloat16)
    partial_sums = jnp.sum(leaf_half.astype(jnp.float32) * leaf_result.astype(jnp.float32), axis=0)
    density = leaf_pivots - lax.psum(partial_sums, "row")
    return (
        parent_block,
        parent_offdiag,
        leaf_result[:order_rows],
        leaf_result[order_rows:],
        density,
    )


def gathered_rows(pieces):
    widths = [p.shape[1] for p in pieces]
    full = lax.all_gather(jnp.concatenate(pieces, axis=1), ("row", "col"), axis=0, tiled=True)
    out, at = [], 0
    for w in widths:
        out.append(full[:, at : at + w])
        at += w
    return out


def local_whole(
    anc_inverse,
    parent_pivinv,
    parent_lower,
    parent_mask,
    leaf_lower_par,
    leaf_lower_anc,
    leaf_mask,
    leaf_pivots,
):
    row_index = lax.axis_index("row")
    row_devices = lax.axis_size("row")
    col_index = lax.axis_index("col")
    anc_rows = anc_inverse.shape[0]
    order_rows = parent_pivinv.shape[0]
    col_width = leaf_pivots.shape[0]
    off_width = parent_lower.shape[1] // 2
    half = anc_rows // 2

    def mine(x):
        return lax.dynamic_slice_in_dim(x, col_index * half, half, 0)

    anc_full, lower_full, par_full, anc_leaf_full = gathered_rows(
        [mine(anc_inverse), mine(parent_lower), mine(leaf_lower_par), mine(leaf_lower_anc)]
    )
    order_all = order_rows * row_devices
    parent_gate = jnp.repeat(parent_mask, BLOCK).astype(jnp.bfloat16)
    leaf_gate = jnp.repeat(leaf_mask, BLOCK).astype(jnp.bfloat16)
    lower_m = lower_full * parent_gate[:, None]
    par_m = par_full * leaf_gate[:order_all, None]
    anc_m = anc_leaf_full * leaf_gate[order_all:, None]

    offdiag_all = (-jnp.dot(anc_full, lower_m, preferred_element_type=jnp.float32)).astype(jnp.bfloat16)
    lower_cols = lax.dynamic_slice_in_dim(lower_m, row_index * order_rows, order_rows, 1)
    parent_block = parent_pivinv - lax.dot_general(
        lower_cols, offdiag_all, (((0,), (0,)), ((), ())), preferred_element_type=jnp.float32
    )
    parent_round = parent_block.astype(jnp.bfloat16)

    par_half = lax.dynamic_slice_in_dim(par_m, col_index * col_width, col_width, 1)
    anc_half = lax.dynamic_slice_in_dim(anc_m, col_index * col_width, col_width, 1)
    offdiag_cols = lax.dynamic_slice_in_dim(offdiag_all, row_index * order_rows, order_rows, 1)
    offdiag_rows = lax.dynamic_slice_in_dim(offdiag_all, row_index * anc_rows, anc_rows, 0)
    upper_sum = jnp.dot(parent_round, par_half, preferred_element_type=jnp.float32) + lax.dot_general(
        offdiag_cols, anc_half, (((0,), (0,)), ((), ())), preferred_element_type=jnp.float32
    )
    lower_sum = jnp.dot(offdiag_rows, par_half, preferred_element_type=jnp.float32) + jnp.dot(
        anc_inverse, anc_half, preferred_element_type=jnp.float32
    )
    leaf_par_block = (-upper_sum).astype(jnp.bfloat16)
    leaf_anc_block = (-lower_sum).astype(jnp.bfloat16)

    par_own = lax.dynamic_slice_in_dim(par_half, row_index * order_rows, order_rows, 0)
    anc_own = lax.dynamic_slice_in_dim(anc_half, row_index * anc_rows, anc_rows, 0)
    partial_sums = jnp.sum(
        par_own.astype(jnp.float32) * leaf_par_block.astype(jnp.float32), axis=0
    ) + jnp.sum(anc_own.astype(jnp.float32) * leaf_anc_block.astype(jnp.float32), axis=0)
    spread = jnp.broadcast_to(partial_sums[None], (row_devices, col_width))
    column_sums = jnp.sum(lax.all_to_all(spread, "row", 0, 0, tiled=True), axis=0)
    density = leaf_pivots - column_sums
    offdiag_own = lax.dynamic_slice_in_dim(offdiag_rows, col_index * off_width, off_width, 1)
    return parent_block, offdiag_own, leaf_par_block, leaf_anc_block, density


def fits_whole(mesh, anc_rows, order_rows):
    anc_all = anc_rows * mesh.shape["row"]
    return (
        anc_rows == order_rows
        and anc_rows % 2 == 0
        and anc_all * anc_all * 2 <= 16 * 1024 * 1024
    )


def solution(mesh):
    placed = (
        P(("pole", "row"), None),
        P(("pole", "row"), None),
        P(("pole", "row"), None),
        P(),
        P(("pole", "row"), None),
        P(("pole", "row"), None),
        P(),
        P(("pole", "col")),
    )
    placed_out = (
        P(("pole", "row"), None),
        P(("pole", "row"), "col"),
        P(("pole", "row"), "col"),
        P(("pole", "row"), "col"),
        P(("pole", "col")),
    )
    shards = mesh.shape["pole"] * mesh.shape["row"]

    def run(*args):
        anc_rows = args[0].shape[0] // shards
        order_rows = args[1].shape[0] // shards
        body = local_whole if fits_whole(mesh, anc_rows, order_rows) else local
        return jax.shard_map(
            body, mesh=mesh, in_specs=placed, out_specs=placed_out, check_vma=False
        )(*args)

    return run
```

```python
import jax
import jax.numpy as jnp
from jax import lax
from jax.sharding import PartitionSpec as P

BLOCK = 256
ORDER = 1024


def local(
    anc_inverse,
    parent_pivinv,
    parent_lower,
    parent_mask,
    leaf_lower_par,
    leaf_lower_anc,
    leaf_mask,
    leaf_pivots,
):
    row_index = lax.axis_index("row")
    row_devices = lax.axis_size("row")
    col_index = lax.axis_index("col")
    anc_rows = anc_inverse.shape[0]
    order_rows = parent_pivinv.shape[0]
    col_width = leaf_pivots.shape[0]
    parent_gate = lax.dynamic_slice_in_dim(
        jnp.repeat(parent_mask, BLOCK), row_index * anc_rows, anc_rows
    )
    lower_one = parent_lower * parent_gate[:, None].astype(jnp.bfloat16)
    lower_half = lax.dynamic_slice_in_dim(lower_one, col_index * col_width, col_width, 1)
    leaf_gate = jnp.repeat(leaf_mask, BLOCK)
    gate_par = lax.dynamic_slice_in_dim(leaf_gate[:ORDER], row_index * order_rows, order_rows)
    gate_anc = lax.dynamic_slice_in_dim(leaf_gate[ORDER:], row_index * anc_rows, anc_rows)
    leaf_local = jnp.concatenate(
        [
            leaf_lower_par * gate_par[:, None].astype(jnp.bfloat16),
            leaf_lower_anc * gate_anc[:, None].astype(jnp.bfloat16),
        ],
        axis=0,
    )
    leaf_half = lax.dynamic_slice_in_dim(leaf_local, col_index * col_width, col_width, 1)
    columns = anc_inverse
    product = jnp.dot(
        columns,
        lax.all_gather(lower_half, "row", axis=0, tiled=True),
        preferred_element_type=jnp.float32,
    )
    parent_offdiag = (-product).astype(jnp.bfloat16)
    offdiag_rows = lax.all_gather(parent_offdiag, "col", axis=1, tiled=True)
    columns = lower_one
    diag_sums = lax.psum_scatter(
        lax.dot_general(
            columns, offdiag_rows, (((0,), (0,)), ((), ())), preferred_element_type=jnp.float32
        ),
        "row",
        scatter_dimension=0,
        tiled=True,
    )
    parent_block = parent_pivinv - diag_sums
    parent_round = parent_block.astype(jnp.bfloat16)
    mirrored = lax.all_to_all(offdiag_rows, "row", split_axis=1, concat_axis=0, tiled=True).T
    upper_rows = jnp.concatenate(
        [
            parent_round.reshape(order_rows, row_devices, order_rows),
            mirrored.reshape(order_rows, row_devices, anc_rows),
        ],
        axis=2,
    )
    lower_rows = jnp.concatenate(
        [
            offdiag_rows.reshape(anc_rows, row_devices, order_rows),
            anc_inverse.reshape(anc_rows, row_devices, anc_rows),
        ],
        axis=2,
    )
    inverse_rows = jnp.concatenate(
        [upper_rows.reshape(order_rows, -1), lower_rows.reshape(anc_rows, -1)], axis=0
    )
    columns = inverse_rows
    leaf_product = jnp.dot(
        columns,
        lax.all_gather(leaf_half, "row", axis=0, tiled=True),
        preferred_element_type=jnp.float32,
    )
    leaf_result = (-leaf_product).astype(jnp.bfloat16)
    partial_sums = jnp.sum(leaf_half.astype(jnp.float32) * leaf_result.astype(jnp.float32), axis=0)
    density = leaf_pivots - lax.psum(partial_sums, "row")
    return (
        parent_block,
        parent_offdiag,
        leaf_result[:order_rows],
        leaf_result[order_rows:],
        density,
    )


def local_whole(
    anc_inverse,
    parent_pivinv,
    parent_lower,
    parent_mask,
    leaf_lower_par,
    leaf_lower_anc,
    leaf_mask,
    leaf_pivots,
):
    row_index = lax.axis_index("row")
    row_devices = lax.axis_size("row")
    col_index = lax.axis_index("col")
    anc_rows = anc_inverse.shape[0]
    order_rows = parent_pivinv.shape[0]
    col_width = leaf_pivots.shape[0]
    off_width = parent_lower.shape[1] // 2
    half = anc_rows // 2

    def mine(x):
        return lax.dynamic_slice_in_dim(x, col_index * half, half, 0)

    order_all = order_rows * row_devices
    parent_gate = jnp.repeat(parent_mask, BLOCK).astype(jnp.bfloat16)
    leaf_gate = jnp.repeat(leaf_mask, BLOCK).astype(jnp.bfloat16)
    anc_start = row_index * anc_rows + col_index * half
    order_start = row_index * order_rows + col_index * half
    lower_gate = lax.dynamic_slice_in_dim(parent_gate, anc_start, half)
    par_gate = lax.dynamic_slice_in_dim(leaf_gate[:order_all], order_start, half)
    anc_gate = lax.dynamic_slice_in_dim(leaf_gate[order_all:], anc_start, half)
    stacked = jnp.stack(
        [
            mine(anc_inverse),
            mine(parent_lower) * lower_gate[:, None],
            mine(leaf_lower_par) * par_gate[:, None],
            mine(leaf_lower_anc) * anc_gate[:, None],
        ]
    )
    full = lax.all_gather(stacked, ("row", "col"), axis=1, tiled=True)
    anc_full, lower_m, par_m, anc_m = full[0], full[1], full[2], full[3]

    offdiag_all = (-jnp.dot(anc_full, lower_m, preferred_element_type=jnp.float32)).astype(jnp.bfloat16)
    lower_cols = lax.dynamic_slice_in_dim(lower_m, row_index * order_rows, order_rows, 1)
    parent_block = parent_pivinv - lax.dot_general(
        lower_cols, offdiag_all, (((0,), (0,)), ((), ())), preferred_element_type=jnp.float32
    )
    parent_round = parent_block.astype(jnp.bfloat16)

    par_half = lax.dynamic_slice_in_dim(par_m, col_index * col_width, col_width, 1)
    anc_half = lax.dynamic_slice_in_dim(anc_m, col_index * col_width, col_width, 1)
    offdiag_cols = lax.dynamic_slice_in_dim(offdiag_all, row_index * order_rows, order_rows, 1)
    offdiag_rows = lax.dynamic_slice_in_dim(offdiag_all, row_index * anc_rows, anc_rows, 0)
    upper_sum = jnp.dot(parent_round, par_half, preferred_element_type=jnp.float32) + lax.dot_general(
        offdiag_cols, anc_half, (((0,), (0,)), ((), ())), preferred_element_type=jnp.float32
    )
    lower_sum = jnp.dot(offdiag_rows, par_half, preferred_element_type=jnp.float32) + jnp.dot(
        anc_inverse, anc_half, preferred_element_type=jnp.float32
    )
    leaf_par_block = (-upper_sum).astype(jnp.bfloat16)
    leaf_anc_block = (-lower_sum).astype(jnp.bfloat16)

    par_own = lax.dynamic_slice_in_dim(par_half, row_index * order_rows, order_rows, 0)
    anc_own = lax.dynamic_slice_in_dim(anc_half, row_index * anc_rows, anc_rows, 0)
    partial_sums = jnp.sum(
        par_own.astype(jnp.float32) * leaf_par_block.astype(jnp.float32), axis=0
    ) + jnp.sum(anc_own.astype(jnp.float32) * leaf_anc_block.astype(jnp.float32), axis=0)
    spread = jnp.broadcast_to(partial_sums[None], (row_devices, col_width))
    column_sums = jnp.sum(lax.all_to_all(spread, "row", 0, 0, tiled=True), axis=0)
    density = leaf_pivots - column_sums
    offdiag_own = lax.dynamic_slice_in_dim(offdiag_rows, col_index * off_width, off_width, 1)
    return parent_block, offdiag_own, leaf_par_block, leaf_anc_block, density


def fits_whole(mesh, anc_rows, order_rows, order_cols, leaf_cols):
    anc_all = anc_rows * mesh.shape["row"]
    return (
        anc_rows == order_rows
        and anc_rows % 2 == 0
        and len({anc_all, order_cols, leaf_cols}) == 1
        and anc_all * anc_all * 2 <= 16 * 1024 * 1024
    )


def solution(mesh):
    placed = (
        P(("pole", "row"), None),
        P(("pole", "row"), None),
        P(("pole", "row"), None),
        P(),
        P(("pole", "row"), None),
        P(("pole", "row"), None),
        P(),
        P(("pole", "col")),
    )
    placed_out = (
        P(("pole", "row"), None),
        P(("pole", "row"), "col"),
        P(("pole", "row"), "col"),
        P(("pole", "row"), "col"),
        P(("pole", "col")),
    )
    shards = mesh.shape["pole"] * mesh.shape["row"]

    def run(*args):
        anc_rows = args[0].shape[0] // shards
        order_rows = args[1].shape[0] // shards
        body = local_whole if fits_whole(mesh, anc_rows, order_rows, args[2].shape[1], args[4].shape[1]) else local
        return jax.shard_map(
            body, mesh=mesh, in_specs=placed, out_specs=placed_out, check_vma=False
        )(*args)

    return run
```

```python
import jax
import jax.numpy as jnp
from jax import lax
from jax.sharding import PartitionSpec as P

BLOCK = 256
ORDER = 1024


def local(
    anc_inverse,
    parent_pivinv,
    parent_lower,
    parent_mask,
    leaf_lower_par,
    leaf_lower_anc,
    leaf_mask,
    leaf_pivots,
):
    row_index = lax.axis_index("row")
    row_devices = lax.axis_size("row")
    col_index = lax.axis_index("col")
    anc_rows = anc_inverse.shape[0]
    order_rows = parent_pivinv.shape[0]
    col_width = leaf_pivots.shape[0]
    parent_gate = lax.dynamic_slice_in_dim(
        jnp.repeat(parent_mask, BLOCK), row_index * anc_rows, anc_rows
    )
    lower_one = parent_lower * parent_gate[:, None].astype(jnp.bfloat16)
    lower_half = lax.dynamic_slice_in_dim(lower_one, col_index * col_width, col_width, 1)
    leaf_gate = jnp.repeat(leaf_mask, BLOCK)
    gate_par = lax.dynamic_slice_in_dim(leaf_gate[:ORDER], row_index * order_rows, order_rows)
    gate_anc = lax.dynamic_slice_in_dim(leaf_gate[ORDER:], row_index * anc_rows, anc_rows)
    leaf_local = jnp.concatenate(
        [
            leaf_lower_par * gate_par[:, None].astype(jnp.bfloat16),
            leaf_lower_anc * gate_anc[:, None].astype(jnp.bfloat16),
        ],
        axis=0,
    )
    leaf_half = lax.dynamic_slice_in_dim(leaf_local, col_index * col_width, col_width, 1)
    columns = anc_inverse
    product = jnp.dot(
        columns,
        lax.all_gather(lower_half, "row", axis=0, tiled=True),
        preferred_element_type=jnp.float32,
    )
    parent_offdiag = (-product).astype(jnp.bfloat16)
    offdiag_rows = lax.all_gather(parent_offdiag, "col", axis=1, tiled=True)
    columns = lower_one
    diag_sums = lax.psum_scatter(
        lax.dot_general(
            columns, offdiag_rows, (((0,), (0,)), ((), ())), preferred_element_type=jnp.float32
        ),
        "row",
        scatter_dimension=0,
        tiled=True,
    )
    parent_block = parent_pivinv - diag_sums
    parent_round = parent_block.astype(jnp.bfloat16)
    mirrored = lax.all_to_all(offdiag_rows, "row", split_axis=1, concat_axis=0, tiled=True).T
    upper_rows = jnp.concatenate(
        [
            parent_round.reshape(order_rows, row_devices, order_rows),
            mirrored.reshape(order_rows, row_devices, anc_rows),
        ],
        axis=2,
    )
    lower_rows = jnp.concatenate(
        [
            offdiag_rows.reshape(anc_rows, row_devices, order_rows),
            anc_inverse.reshape(anc_rows, row_devices, anc_rows),
        ],
        axis=2,
    )
    inverse_rows = jnp.concatenate(
        [upper_rows.reshape(order_rows, -1), lower_rows.reshape(anc_rows, -1)], axis=0
    )
    columns = inverse_rows
    leaf_product = jnp.dot(
        columns,
        lax.all_gather(leaf_half, "row", axis=0, tiled=True),
        preferred_element_type=jnp.float32,
    )
    leaf_result = (-leaf_product).astype(jnp.bfloat16)
    partial_sums = jnp.sum(leaf_half.astype(jnp.float32) * leaf_result.astype(jnp.float32), axis=0)
    density = leaf_pivots - lax.psum(partial_sums, "row")
    return (
        parent_block,
        parent_offdiag,
        leaf_result[:order_rows],
        leaf_result[order_rows:],
        density,
    )


def local_whole(
    anc_inverse,
    parent_pivinv,
    parent_lower,
    parent_mask,
    leaf_lower_par,
    leaf_lower_anc,
    leaf_mask,
    leaf_pivots,
):
    row_index = lax.axis_index("row")
    row_devices = lax.axis_size("row")
    col_index = lax.axis_index("col")
    anc_rows = anc_inverse.shape[0]
    order_rows = parent_pivinv.shape[0]
    col_width = leaf_pivots.shape[0]
    off_width = parent_lower.shape[1] // 2
    half = anc_rows // 2

    def mine(x):
        return lax.dynamic_slice_in_dim(x, col_index * half, half, 0)

    order_all = order_rows * row_devices
    parent_gate = jnp.repeat(parent_mask, BLOCK).astype(jnp.bfloat16)
    leaf_gate = jnp.repeat(leaf_mask, BLOCK).astype(jnp.bfloat16)
    anc_start = row_index * anc_rows + col_index * half
    order_start = row_index * order_rows + col_index * half
    lower_gate = lax.dynamic_slice_in_dim(parent_gate, anc_start, half)
    par_gate = lax.dynamic_slice_in_dim(leaf_gate[:order_all], order_start, half)
    anc_gate = lax.dynamic_slice_in_dim(leaf_gate[order_all:], anc_start, half)
    stacked = jnp.stack(
        [
            mine(anc_inverse),
            mine(parent_lower) * lower_gate[:, None],
            mine(leaf_lower_par) * par_gate[:, None],
            mine(leaf_lower_anc) * anc_gate[:, None],
        ]
    )
    full = lax.all_gather(stacked, ("row", "col"), axis=1, tiled=True)
    anc_full, lower_m, par_m, anc_m = full[0], full[1], full[2], full[3]

    lower_cols = lax.dynamic_slice_in_dim(lower_m, row_index * order_rows, order_rows, 1)
    offdiag_cols = (-jnp.dot(anc_full, lower_cols, preferred_element_type=jnp.float32)).astype(
        jnp.bfloat16
    )
    offdiag_rows = (-jnp.dot(anc_inverse, lower_m, preferred_element_type=jnp.float32)).astype(
        jnp.bfloat16
    )
    parent_block = parent_pivinv - lax.dot_general(
        offdiag_cols, lower_m, (((0,), (0,)), ((), ())), preferred_element_type=jnp.float32
    )
    parent_round = parent_block.astype(jnp.bfloat16)

    par_half = lax.dynamic_slice_in_dim(par_m, col_index * col_width, col_width, 1)
    anc_half = lax.dynamic_slice_in_dim(anc_m, col_index * col_width, col_width, 1)
    upper_sum = jnp.dot(parent_round, par_half, preferred_element_type=jnp.float32) + lax.dot_general(
        offdiag_cols, anc_half, (((0,), (0,)), ((), ())), preferred_element_type=jnp.float32
    )
    lower_sum = jnp.dot(offdiag_rows, par_half, preferred_element_type=jnp.float32) + jnp.dot(
        anc_inverse, anc_half, preferred_element_type=jnp.float32
    )
    leaf_par_block = (-upper_sum).astype(jnp.bfloat16)
    leaf_anc_block = (-lower_sum).astype(jnp.bfloat16)

    par_own = lax.dynamic_slice_in_dim(par_half, row_index * order_rows, order_rows, 0)
    anc_own = lax.dynamic_slice_in_dim(anc_half, row_index * anc_rows, anc_rows, 0)
    partial_sums = jnp.sum(
        par_own.astype(jnp.float32) * leaf_par_block.astype(jnp.float32), axis=0
    ) + jnp.sum(anc_own.astype(jnp.float32) * leaf_anc_block.astype(jnp.float32), axis=0)
    spread = jnp.broadcast_to(partial_sums[None], (row_devices, col_width))
    column_sums = jnp.sum(lax.all_to_all(spread, "row", 0, 0, tiled=True), axis=0)
    density = leaf_pivots - column_sums
    offdiag_own = lax.dynamic_slice_in_dim(offdiag_rows, col_index * off_width, off_width, 1)
    return parent_block, offdiag_own, leaf_par_block, leaf_anc_block, density


def fits_whole(mesh, anc_rows, order_rows, order_cols, leaf_cols):
    anc_all = anc_rows * mesh.shape["row"]
    return (
        anc_rows == order_rows
        and anc_rows % 2 == 0
        and len({anc_all, order_cols, leaf_cols}) == 1
        and anc_all * anc_all * 2 <= 16 * 1024 * 1024
    )


def solution(mesh):
    placed = (
        P(("pole", "row"), None),
        P(("pole", "row"), None),
        P(("pole", "row"), None),
        P(),
        P(("pole", "row"), None),
        P(("pole", "row"), None),
        P(),
        P(("pole", "col")),
    )
    placed_out = (
        P(("pole", "row"), None),
        P(("pole", "row"), "col"),
        P(("pole", "row"), "col"),
        P(("pole", "row"), "col"),
        P(("pole", "col")),
    )
    shards = mesh.shape["pole"] * mesh.shape["row"]

    def run(*args):
        anc_rows = args[0].shape[0] // shards
        order_rows = args[1].shape[0] // shards
        body = local_whole if fits_whole(mesh, anc_rows, order_rows, args[2].shape[1], args[4].shape[1]) else local
        return jax.shard_map(
            body, mesh=mesh, in_specs=placed, out_specs=placed_out, check_vma=False
        )(*args)

    return run
```

```python
import jax
import jax.numpy as jnp
from jax import lax
from jax.experimental import pallas as pl
from jax.experimental.pallas import tpu as pltpu
from jax.sharding import PartitionSpec as P

BLOCK = 256
ORDER = 1024


def local(
    anc_inverse,
    parent_pivinv,
    parent_lower,
    parent_mask,
    leaf_lower_par,
    leaf_lower_anc,
    leaf_mask,
    leaf_pivots,
):
    row_index = lax.axis_index("row")
    row_devices = lax.axis_size("row")
    col_index = lax.axis_index("col")
    anc_rows = anc_inverse.shape[0]
    order_rows = parent_pivinv.shape[0]
    col_width = leaf_pivots.shape[0]
    parent_gate = lax.dynamic_slice_in_dim(
        jnp.repeat(parent_mask, BLOCK), row_index * anc_rows, anc_rows
    )
    lower_one = parent_lower * parent_gate[:, None].astype(jnp.bfloat16)
    lower_half = lax.dynamic_slice_in_dim(lower_one, col_index * col_width, col_width, 1)
    leaf_gate = jnp.repeat(leaf_mask, BLOCK)
    gate_par = lax.dynamic_slice_in_dim(leaf_gate[:ORDER], row_index * order_rows, order_rows)
    gate_anc = lax.dynamic_slice_in_dim(leaf_gate[ORDER:], row_index * anc_rows, anc_rows)
    leaf_local = jnp.concatenate(
        [
            leaf_lower_par * gate_par[:, None].astype(jnp.bfloat16),
            leaf_lower_anc * gate_anc[:, None].astype(jnp.bfloat16),
        ],
        axis=0,
    )
    leaf_half = lax.dynamic_slice_in_dim(leaf_local, col_index * col_width, col_width, 1)
    columns = anc_inverse
    product = jnp.dot(
        columns,
        lax.all_gather(lower_half, "row", axis=0, tiled=True),
        preferred_element_type=jnp.float32,
    )
    parent_offdiag = (-product).astype(jnp.bfloat16)
    offdiag_rows = lax.all_gather(parent_offdiag, "col", axis=1, tiled=True)
    columns = lower_one
    diag_sums = lax.psum_scatter(
        lax.dot_general(
            columns, offdiag_rows, (((0,), (0,)), ((), ())), preferred_element_type=jnp.float32
        ),
        "row",
        scatter_dimension=0,
        tiled=True,
    )
    parent_block = parent_pivinv - diag_sums
    parent_round = parent_block.astype(jnp.bfloat16)
    mirrored = lax.all_to_all(offdiag_rows, "row", split_axis=1, concat_axis=0, tiled=True).T
    upper_rows = jnp.concatenate(
        [
            parent_round.reshape(order_rows, row_devices, order_rows),
            mirrored.reshape(order_rows, row_devices, anc_rows),
        ],
        axis=2,
    )
    lower_rows = jnp.concatenate(
        [
            offdiag_rows.reshape(anc_rows, row_devices, order_rows),
            anc_inverse.reshape(anc_rows, row_devices, anc_rows),
        ],
        axis=2,
    )
    inverse_rows = jnp.concatenate(
        [upper_rows.reshape(order_rows, -1), lower_rows.reshape(anc_rows, -1)], axis=0
    )
    columns = inverse_rows
    leaf_product = jnp.dot(
        columns,
        lax.all_gather(leaf_half, "row", axis=0, tiled=True),
        preferred_element_type=jnp.float32,
    )
    leaf_result = (-leaf_product).astype(jnp.bfloat16)
    partial_sums = jnp.sum(leaf_half.astype(jnp.float32) * leaf_result.astype(jnp.float32), axis=0)
    density = leaf_pivots - lax.psum(partial_sums, "row")
    return (
        parent_block,
        parent_offdiag,
        leaf_result[:order_rows],
        leaf_result[order_rows:],
        density,
    )


def leaf_kernel(
    idx_ref, lower_gate, par_gate, anc_gate, full_hbm, anc_local, pivinv,
    block_ref, offdiag_ref, par_ref, anc_ref, part_ref,
    anc_v, lower_v, par_v, ancl_v, rows_v, sem,
):
    row, col = idx_ref[0], idx_ref[1]
    anc_all, order_all = anc_v.shape[0], lower_v.shape[1]
    width = par_v.shape[1]
    order_rows, anc_rows = block_ref.shape[0], anc_local.shape[0]
    off_width = offdiag_ref.shape[1]
    leaf_at = anc_all + order_all
    copies = [
        pltpu.make_async_copy(full_hbm.at[:, pl.ds(0, anc_all)], anc_v, sem.at[0]),
        pltpu.make_async_copy(full_hbm.at[:, pl.ds(anc_all, order_all)], lower_v, sem.at[1]),
        pltpu.make_async_copy(
            full_hbm.at[:, pl.ds(pl.multiple_of(leaf_at + col * width, 128), width)], par_v, sem.at[2]
        ),
        pltpu.make_async_copy(
            full_hbm.at[:, pl.ds(pl.multiple_of(leaf_at + order_all + col * width, 128), width)],
            ancl_v,
            sem.at[3],
        ),
    ]
    for copy in copies:
        copy.start()
    copies[0].wait()
    copies[1].wait()
    lower_v[...] = lower_v[...] * lower_gate[...]
    lower = lower_v[...]
    lower_cols = lower_v[:, pl.ds(pl.multiple_of(row * order_rows, 128), order_rows)]
    offdiag_t = (
        -jnp.dot(lower_cols.T, anc_v[...], preferred_element_type=jnp.float32)
    ).astype(jnp.bfloat16)
    block = pivinv[...] - jnp.dot(offdiag_t, lower, preferred_element_type=jnp.float32)
    block_ref[...] = block
    rows = (-jnp.dot(anc_local[...], lower, preferred_element_type=jnp.float32)).astype(jnp.bfloat16)
    rows_v[...] = rows
    offdiag_ref[...] = rows_v[:, pl.ds(pl.multiple_of(col * off_width, 128), off_width)]
    copies[2].wait()
    copies[3].wait()
    par_v[...] = par_v[...] * par_gate[...]
    ancl_v[...] = ancl_v[...] * anc_gate[...]
    par, ancl = par_v[...], ancl_v[...]
    upper = jnp.dot(
        block.astype(jnp.bfloat16), par, preferred_element_type=jnp.float32
    ) + jnp.dot(offdiag_t, ancl, preferred_element_type=jnp.float32)
    par_block = (-upper).astype(jnp.bfloat16)
    lower_sum = jnp.dot(rows, par, preferred_element_type=jnp.float32) + jnp.dot(
        anc_local[...], ancl, preferred_element_type=jnp.float32
    )
    anc_block = (-lower_sum).astype(jnp.bfloat16)
    par_ref[...] = par_block
    anc_ref[...] = anc_block
    par_own = par_v[pl.ds(pl.multiple_of(row * order_rows, 8), order_rows), :]
    ancl_own = ancl_v[pl.ds(pl.multiple_of(row * anc_rows, 8), anc_rows), :]
    part = jnp.sum(
        par_own.astype(jnp.float32) * par_block.astype(jnp.float32), axis=0, keepdims=True
    ) + jnp.sum(ancl_own.astype(jnp.float32) * anc_block.astype(jnp.float32), axis=0, keepdims=True)
    part_ref[...] = jnp.broadcast_to(part, part_ref.shape)


def local_whole(
    anc_inverse,
    parent_pivinv,
    parent_lower,
    parent_mask,
    leaf_lower_par,
    leaf_lower_anc,
    leaf_mask,
    leaf_pivots,
):
    row_index = lax.axis_index("row")
    row_devices = lax.axis_size("row")
    col_index = lax.axis_index("col")
    anc_rows = anc_inverse.shape[0]
    order_rows = parent_pivinv.shape[0]
    col_width = leaf_pivots.shape[0]
    off_width = parent_lower.shape[1] // 2
    half = anc_rows // 2
    anc_all = anc_rows * row_devices
    order_all = order_rows * row_devices

    def mine(x):
        return lax.dynamic_slice_in_dim(x, col_index * half, half, 0)

    full = lax.all_gather(
        jnp.concatenate(
            [mine(anc_inverse), mine(parent_lower), mine(leaf_lower_par), mine(leaf_lower_anc)], axis=1
        ),
        ("row", "col"),
        axis=0,
        tiled=True,
    )
    parent_gate = jnp.repeat(parent_mask, BLOCK).astype(jnp.bfloat16)[:, None]
    leaf_gate = jnp.repeat(leaf_mask, BLOCK).astype(jnp.bfloat16)[:, None]
    idx = jnp.stack([row_index, col_index]).astype(jnp.int32)
    vmem = pl.BlockSpec(memory_space=pltpu.VMEM)
    flops = 2 * (3 * order_rows * anc_all * order_all + 4 * order_rows * anc_all * col_width)
    block, offdiag_own, par_block, anc_block, parts = pl.pallas_call(
        leaf_kernel,
        out_shape=(
            jax.ShapeDtypeStruct((order_rows, order_all), jnp.float32),
            jax.ShapeDtypeStruct((anc_rows, off_width), jnp.bfloat16),
            jax.ShapeDtypeStruct((order_rows, col_width), jnp.bfloat16),
            jax.ShapeDtypeStruct((anc_rows, col_width), jnp.bfloat16),
            jax.ShapeDtypeStruct((row_devices, col_width), jnp.float32),
        ),
        in_specs=[pl.BlockSpec(memory_space=pltpu.SMEM)]
        + [vmem] * 3
        + [pl.BlockSpec(memory_space=pl.ANY)]
        + [vmem] * 2,
        out_specs=(vmem,) * 5,
        scratch_shapes=[
            pltpu.VMEM((anc_all, anc_all), jnp.bfloat16),
            pltpu.VMEM((anc_all, order_all), jnp.bfloat16),
            pltpu.VMEM((order_all, col_width), jnp.bfloat16),
            pltpu.VMEM((anc_all, col_width), jnp.bfloat16),
            pltpu.VMEM((anc_rows, order_all), jnp.bfloat16),
            pltpu.SemaphoreType.DMA((4,)),
        ],
        cost_estimate=pl.CostEstimate(
            flops=flops, transcendentals=0, bytes_accessed=full.size + 8 * anc_rows * order_all
        ),
    )(
        idx,
        parent_gate,
        leaf_gate[:order_all],
        leaf_gate[order_all:],
        full,
        anc_inverse,
        parent_pivinv,
    )
    column_sums = jnp.sum(lax.all_to_all(parts, "row", 0, 0, tiled=True), axis=0)
    density = leaf_pivots - column_sums
    return block, offdiag_own, par_block, anc_block, density


def fits_whole(mesh, anc_rows, order_rows):
    anc_all = anc_rows * mesh.shape["row"]
    return (
        anc_rows == order_rows
        and anc_rows % 128 == 0
        and anc_all * anc_all * 2 <= 16 * 1024 * 1024
    )


def solution(mesh):
    placed = (
        P(("pole", "row"), None),
        P(("pole", "row"), None),
        P(("pole", "row"), None),
        P(),
        P(("pole", "row"), None),
        P(("pole", "row"), None),
        P(),
        P(("pole", "col")),
    )
    placed_out = (
        P(("pole", "row"), None),
        P(("pole", "row"), "col"),
        P(("pole", "row"), "col"),
        P(("pole", "row"), "col"),
        P(("pole", "col")),
    )
    shards = mesh.shape["pole"] * mesh.shape["row"]

    def run(*args):
        anc_rows = args[0].shape[0] // shards
        order_rows = args[1].shape[0] // shards
        body = local_whole if fits_whole(mesh, anc_rows, order_rows) else local
        return jax.shard_map(
            body, mesh=mesh, in_specs=placed, out_specs=placed_out, check_vma=False
        )(*args)

    return run
```

```python
import jax
import jax.numpy as jnp
from jax import lax
from jax.experimental import pallas as pl
from jax.experimental.pallas import tpu as pltpu
from jax.sharding import PartitionSpec as P

BLOCK = 256
ORDER = 1024


def local(
    anc_inverse,
    parent_pivinv,
    parent_lower,
    parent_mask,
    leaf_lower_par,
    leaf_lower_anc,
    leaf_mask,
    leaf_pivots,
):
    row_index = lax.axis_index("row")
    row_devices = lax.axis_size("row")
    col_index = lax.axis_index("col")
    anc_rows = anc_inverse.shape[0]
    order_rows = parent_pivinv.shape[0]
    col_width = leaf_pivots.shape[0]
    parent_gate = lax.dynamic_slice_in_dim(
        jnp.repeat(parent_mask, BLOCK), row_index * anc_rows, anc_rows
    )
    lower_one = parent_lower * parent_gate[:, None].astype(jnp.bfloat16)
    lower_half = lax.dynamic_slice_in_dim(lower_one, col_index * col_width, col_width, 1)
    leaf_gate = jnp.repeat(leaf_mask, BLOCK)
    gate_par = lax.dynamic_slice_in_dim(leaf_gate[:ORDER], row_index * order_rows, order_rows)
    gate_anc = lax.dynamic_slice_in_dim(leaf_gate[ORDER:], row_index * anc_rows, anc_rows)
    leaf_local = jnp.concatenate(
        [
            leaf_lower_par * gate_par[:, None].astype(jnp.bfloat16),
            leaf_lower_anc * gate_anc[:, None].astype(jnp.bfloat16),
        ],
        axis=0,
    )
    leaf_half = lax.dynamic_slice_in_dim(leaf_local, col_index * col_width, col_width, 1)
    columns = anc_inverse
    product = jnp.dot(
        columns,
        lax.all_gather(lower_half, "row", axis=0, tiled=True),
        preferred_element_type=jnp.float32,
    )
    parent_offdiag = (-product).astype(jnp.bfloat16)
    offdiag_rows = lax.all_gather(parent_offdiag, "col", axis=1, tiled=True)
    columns = lower_one
    diag_sums = lax.psum_scatter(
        lax.dot_general(
            columns, offdiag_rows, (((0,), (0,)), ((), ())), preferred_element_type=jnp.float32
        ),
        "row",
        scatter_dimension=0,
        tiled=True,
    )
    parent_block = parent_pivinv - diag_sums
    parent_round = parent_block.astype(jnp.bfloat16)
    mirrored = lax.all_to_all(offdiag_rows, "row", split_axis=1, concat_axis=0, tiled=True).T
    upper_rows = jnp.concatenate(
        [
            parent_round.reshape(order_rows, row_devices, order_rows),
            mirrored.reshape(order_rows, row_devices, anc_rows),
        ],
        axis=2,
    )
    lower_rows = jnp.concatenate(
        [
            offdiag_rows.reshape(anc_rows, row_devices, order_rows),
            anc_inverse.reshape(anc_rows, row_devices, anc_rows),
        ],
        axis=2,
    )
    inverse_rows = jnp.concatenate(
        [upper_rows.reshape(order_rows, -1), lower_rows.reshape(anc_rows, -1)], axis=0
    )
    columns = inverse_rows
    leaf_product = jnp.dot(
        columns,
        lax.all_gather(leaf_half, "row", axis=0, tiled=True),
        preferred_element_type=jnp.float32,
    )
    leaf_result = (-leaf_product).astype(jnp.bfloat16)
    partial_sums = jnp.sum(leaf_half.astype(jnp.float32) * leaf_result.astype(jnp.float32), axis=0)
    density = leaf_pivots - lax.psum(partial_sums, "row")
    return (
        parent_block,
        parent_offdiag,
        leaf_result[:order_rows],
        leaf_result[order_rows:],
        density,
    )


def piece_kernel(idx_ref, anc_hbm, lower_hbm, par_hbm, ancl_hbm, out_ref, sem):
    row, col = idx_ref[0], idx_ref[1]
    half = out_ref.shape[0]
    blk = anc_hbm.shape[0]
    blocks = anc_hbm.shape[1] // blk
    sent = blocks // 2 + 1
    rows = pl.ds(pl.multiple_of(col * half, 8), half)
    copies = []
    for k in range(sent):
        start = pl.multiple_of(lax.rem(row + k, blocks) * blk, 128)
        copies.append(
            pltpu.make_async_copy(
                anc_hbm.at[rows, pl.ds(start, blk)], out_ref.at[:, pl.ds(k * blk, blk)], sem.at[k]
            )
        )
    at = sent * blk
    for j, source in enumerate((lower_hbm, par_hbm, ancl_hbm)):
        width = source.shape[1]
        copies.append(
            pltpu.make_async_copy(
                source.at[rows, :], out_ref.at[:, pl.ds(at, width)], sem.at[sent + j]
            )
        )
        at += width
    for copy in copies:
        copy.start()
    for copy in copies:
        copy.wait()


def leaf_kernel(
    idx_ref, lower_gate, par_gate, anc_gate, full_hbm, anc_local, pivinv,
    block_ref, offdiag_ref, par_ref, anc_ref, part_ref,
    sent_v, anc_v, lower_v, par_v, ancl_v, rows_v, sem,
):
    row, col = idx_ref[0], idx_ref[1]
    anc_all, order_all = anc_v.shape[0], lower_v.shape[1]
    width = par_v.shape[1]
    order_rows, anc_rows = block_ref.shape[0], anc_local.shape[0]
    off_width = offdiag_ref.shape[1]
    sent_width = sent_v.shape[1]
    leaf_at = sent_width + order_all
    leaf_width = (full_hbm.shape[1] - leaf_at) // 2
    copies = [
        pltpu.make_async_copy(full_hbm.at[:, pl.ds(0, sent_width)], sent_v, sem.at[0]),
        pltpu.make_async_copy(full_hbm.at[:, pl.ds(sent_width, order_all)], lower_v, sem.at[1]),
        pltpu.make_async_copy(
            full_hbm.at[:, pl.ds(pl.multiple_of(leaf_at + col * width, 128), width)], par_v, sem.at[2]
        ),
        pltpu.make_async_copy(
            full_hbm.at[:, pl.ds(pl.multiple_of(leaf_at + leaf_width + col * width, 128), width)],
            ancl_v,
            sem.at[3],
        ),
    ]
    for copy in copies:
        copy.start()
    copies[0].wait()
    blocks = anc_all // anc_rows
    for p in range(blocks):
        for q in range(blocks):
            k = (q - p) % blocks
            if k * anc_rows < sent_width:
                part = sent_v[p * anc_rows : (p + 1) * anc_rows, k * anc_rows : (k + 1) * anc_rows]
            else:
                k = (p - q) % blocks
                part = sent_v[q * anc_rows : (q + 1) * anc_rows, k * anc_rows : (k + 1) * anc_rows]
                part = part.astype(jnp.float32).T.astype(jnp.bfloat16)
            anc_v[p * anc_rows : (p + 1) * anc_rows, q * anc_rows : (q + 1) * anc_rows] = part
    copies[1].wait()
    lower_v[...] = lower_v[...] * lower_gate[...]
    lower = lower_v[...]
    lower_cols = lower_v[:, pl.ds(pl.multiple_of(row * order_rows, 128), order_rows)]
    offdiag_t = (
        -jnp.dot(lower_cols.T, anc_v[...], preferred_element_type=jnp.float32)
    ).astype(jnp.bfloat16)
    block = pivinv[...] - jnp.dot(offdiag_t, lower, preferred_element_type=jnp.float32)
    block_ref[...] = block
    rows = (-jnp.dot(anc_local[...], lower, preferred_element_type=jnp.float32)).astype(jnp.bfloat16)
    rows_v[...] = rows
    offdiag_ref[...] = rows_v[:, pl.ds(pl.multiple_of(col * off_width, 128), off_width)]
    copies[2].wait()
    copies[3].wait()
    par_v[...] = par_v[...] * par_gate[...]
    ancl_v[...] = ancl_v[...] * anc_gate[...]
    par, ancl = par_v[...], ancl_v[...]
    upper = jnp.dot(
        block.astype(jnp.bfloat16), par, preferred_element_type=jnp.float32
    ) + jnp.dot(offdiag_t, ancl, preferred_element_type=jnp.float32)
    par_block = (-upper).astype(jnp.bfloat16)
    lower_sum = jnp.dot(rows, par, preferred_element_type=jnp.float32) + jnp.dot(
        anc_local[...], ancl, preferred_element_type=jnp.float32
    )
    anc_block = (-lower_sum).astype(jnp.bfloat16)
    par_ref[...] = par_block
    anc_ref[...] = anc_block
    par_own = par_v[pl.ds(pl.multiple_of(row * order_rows, 8), order_rows), :]
    ancl_own = ancl_v[pl.ds(pl.multiple_of(row * anc_rows, 8), anc_rows), :]
    part = jnp.sum(
        par_own.astype(jnp.float32) * par_block.astype(jnp.float32), axis=0, keepdims=True
    ) + jnp.sum(ancl_own.astype(jnp.float32) * anc_block.astype(jnp.float32), axis=0, keepdims=True)
    part_ref[...] = jnp.broadcast_to(part, part_ref.shape)


def local_whole(
    anc_inverse,
    parent_pivinv,
    parent_lower,
    parent_mask,
    leaf_lower_par,
    leaf_lower_anc,
    leaf_mask,
    leaf_pivots,
):
    row_index = lax.axis_index("row")
    row_devices = lax.axis_size("row")
    col_index = lax.axis_index("col")
    anc_rows = anc_inverse.shape[0]
    order_rows = parent_pivinv.shape[0]
    col_width = leaf_pivots.shape[0]
    off_width = parent_lower.shape[1] // 2
    half = anc_rows // 2
    anc_all = anc_rows * row_devices
    order_all = order_rows * row_devices

    idx = jnp.stack([row_index, col_index]).astype(jnp.int32)
    sent_width = (row_devices // 2 + 1) * anc_rows
    piece_width = sent_width + order_all + 2 * leaf_lower_par.shape[1]
    hbm = pl.BlockSpec(memory_space=pl.ANY)
    piece = pl.pallas_call(
        piece_kernel,
        out_shape=jax.ShapeDtypeStruct((half, piece_width), jnp.bfloat16),
        in_specs=[pl.BlockSpec(memory_space=pltpu.SMEM)] + [hbm] * 4,
        out_specs=pl.BlockSpec(memory_space=pltpu.VMEM),
        scratch_shapes=[pltpu.SemaphoreType.DMA((row_devices // 2 + 4,))],
    )(idx, anc_inverse, parent_lower, leaf_lower_par, leaf_lower_anc)
    full = lax.all_gather(piece, ("row", "col"), axis=0, tiled=True)
    parent_gate = jnp.repeat(parent_mask, BLOCK).astype(jnp.bfloat16)[:, None]
    leaf_gate = jnp.repeat(leaf_mask, BLOCK).astype(jnp.bfloat16)[:, None]
    vmem = pl.BlockSpec(memory_space=pltpu.VMEM)
    flops = 2 * (3 * order_rows * anc_all * order_all + 4 * order_rows * anc_all * col_width)
    block, offdiag_own, par_block, anc_block, parts = pl.pallas_call(
        leaf_kernel,
        out_shape=(
            jax.ShapeDtypeStruct((order_rows, order_all), jnp.float32),
            jax.ShapeDtypeStruct((anc_rows, off_width), jnp.bfloat16),
            jax.ShapeDtypeStruct((order_rows, col_width), jnp.bfloat16),
            jax.ShapeDtypeStruct((anc_rows, col_width), jnp.bfloat16),
            jax.ShapeDtypeStruct((row_devices, col_width), jnp.float32),
        ),
        in_specs=[pl.BlockSpec(memory_space=pltpu.SMEM)]
        + [vmem] * 3
        + [pl.BlockSpec(memory_space=pl.ANY)]
        + [vmem] * 2,
        out_specs=(vmem,) * 5,
        scratch_shapes=[
            pltpu.VMEM((anc_all, sent_width), jnp.bfloat16),
            pltpu.VMEM((anc_all, anc_all), jnp.bfloat16),
            pltpu.VMEM((anc_all, order_all), jnp.bfloat16),
            pltpu.VMEM((order_all, col_width), jnp.bfloat16),
            pltpu.VMEM((anc_all, col_width), jnp.bfloat16),
            pltpu.VMEM((anc_rows, order_all), jnp.bfloat16),
            pltpu.SemaphoreType.DMA((4,)),
        ],
        cost_estimate=pl.CostEstimate(
            flops=flops, transcendentals=0, bytes_accessed=full.size + 8 * anc_rows * order_all
        ),
    )(
        idx,
        parent_gate,
        leaf_gate[:order_all],
        leaf_gate[order_all:],
        full,
        anc_inverse,
        parent_pivinv,
    )
    column_sums = jnp.sum(lax.all_to_all(parts, "row", 0, 0, tiled=True), axis=0)
    density = leaf_pivots - column_sums
    return block, offdiag_own, par_block, anc_block, density


def fits_whole(mesh, anc_rows, order_rows):
    anc_all = anc_rows * mesh.shape["row"]
    return (
        anc_rows == order_rows
        and anc_rows % 128 == 0
        and anc_all * anc_all * 2 <= 16 * 1024 * 1024
    )


def solution(mesh):
    placed = (
        P(("pole", "row"), None),
        P(("pole", "row"), None),
        P(("pole", "row"), None),
        P(),
        P(("pole", "row"), None),
        P(("pole", "row"), None),
        P(),
        P(("pole", "col")),
    )
    placed_out = (
        P(("pole", "row"), None),
        P(("pole", "row"), "col"),
        P(("pole", "row"), "col"),
        P(("pole", "row"), "col"),
        P(("pole", "col")),
    )
    shards = mesh.shape["pole"] * mesh.shape["row"]

    def run(*args):
        anc_rows = args[0].shape[0] // shards
        order_rows = args[1].shape[0] // shards
        body = local_whole if fits_whole(mesh, anc_rows, order_rows) else local
        return jax.shard_map(
            body, mesh=mesh, in_specs=placed, out_specs=placed_out, check_vma=False
        )(*args)

    return run
```

```python
import jax
import jax.numpy as jnp
from jax import lax
from jax.experimental import pallas as pl
from jax.experimental.pallas import tpu as pltpu
from jax.sharding import PartitionSpec as P

BLOCK = 256
ORDER = 1024


def local(
    anc_inverse,
    parent_pivinv,
    parent_lower,
    parent_mask,
    leaf_lower_par,
    leaf_lower_anc,
    leaf_mask,
    leaf_pivots,
):
    row_index = lax.axis_index("row")
    row_devices = lax.axis_size("row")
    col_index = lax.axis_index("col")
    anc_rows = anc_inverse.shape[0]
    order_rows = parent_pivinv.shape[0]
    col_width = leaf_pivots.shape[0]
    parent_gate = lax.dynamic_slice_in_dim(
        jnp.repeat(parent_mask, BLOCK), row_index * anc_rows, anc_rows
    )
    lower_one = parent_lower * parent_gate[:, None].astype(jnp.bfloat16)
    lower_half = lax.dynamic_slice_in_dim(lower_one, col_index * col_width, col_width, 1)
    leaf_gate = jnp.repeat(leaf_mask, BLOCK)
    gate_par = lax.dynamic_slice_in_dim(leaf_gate[:ORDER], row_index * order_rows, order_rows)
    gate_anc = lax.dynamic_slice_in_dim(leaf_gate[ORDER:], row_index * anc_rows, anc_rows)
    leaf_local = jnp.concatenate(
        [
            leaf_lower_par * gate_par[:, None].astype(jnp.bfloat16),
            leaf_lower_anc * gate_anc[:, None].astype(jnp.bfloat16),
        ],
        axis=0,
    )
    leaf_half = lax.dynamic_slice_in_dim(leaf_local, col_index * col_width, col_width, 1)
    columns = anc_inverse
    product = jnp.dot(
        columns,
        lax.all_gather(lower_half, "row", axis=0, tiled=True),
        preferred_element_type=jnp.float32,
    )
    parent_offdiag = (-product).astype(jnp.bfloat16)
    offdiag_rows = lax.all_gather(parent_offdiag, "col", axis=1, tiled=True)
    columns = lower_one
    diag_sums = lax.psum_scatter(
        lax.dot_general(
            columns, offdiag_rows, (((0,), (0,)), ((), ())), preferred_element_type=jnp.float32
        ),
        "row",
        scatter_dimension=0,
        tiled=True,
    )
    parent_block = parent_pivinv - diag_sums
    parent_round = parent_block.astype(jnp.bfloat16)
    mirrored = lax.all_to_all(offdiag_rows, "row", split_axis=1, concat_axis=0, tiled=True).T
    upper_rows = jnp.concatenate(
        [
            parent_round.reshape(order_rows, row_devices, order_rows),
            mirrored.reshape(order_rows, row_devices, anc_rows),
        ],
        axis=2,
    )
    lower_rows = jnp.concatenate(
        [
            offdiag_rows.reshape(anc_rows, row_devices, order_rows),
            anc_inverse.reshape(anc_rows, row_devices, anc_rows),
        ],
        axis=2,
    )
    inverse_rows = jnp.concatenate(
        [upper_rows.reshape(order_rows, -1), lower_rows.reshape(anc_rows, -1)], axis=0
    )
    columns = inverse_rows
    leaf_product = jnp.dot(
        columns,
        lax.all_gather(leaf_half, "row", axis=0, tiled=True),
        preferred_element_type=jnp.float32,
    )
    leaf_result = (-leaf_product).astype(jnp.bfloat16)
    partial_sums = jnp.sum(leaf_half.astype(jnp.float32) * leaf_result.astype(jnp.float32), axis=0)
    density = leaf_pivots - lax.psum(partial_sums, "row")
    return (
        parent_block,
        parent_offdiag,
        leaf_result[:order_rows],
        leaf_result[order_rows:],
        density,
    )


def piece_kernel(anc_hbm, lower_hbm, par_hbm, ancl_hbm, out_ref):
    row, col = lax.axis_index("row"), lax.axis_index("col")
    half = out_ref.shape[0]
    blk = anc_hbm.shape[0]
    blocks = anc_hbm.shape[1] // blk
    sent = blocks // 2 + 1
    rows = pl.ds(pl.multiple_of(col * half, 8), half)
    for k in range(sent):
        start = pl.multiple_of(lax.rem(row + k, blocks) * blk, 128)
        out_ref[:, k * blk : (k + 1) * blk] = anc_hbm[rows, pl.ds(start, blk)]
    at = sent * blk
    for source in (lower_hbm, par_hbm, ancl_hbm):
        width = source.shape[1]
        out_ref[:, at : at + width] = source[rows, :]
        at += width


def leaf_kernel(
    lower_gate, par_gate, anc_gate, pivots, full_hbm, anc_local, pivinv,
    block_ref, offdiag_ref, par_ref, anc_ref, part_ref,
    sent_v, anc_v, lower_v, par_v, ancl_v, rows_v, sem,
):
    row, col = lax.axis_index("row"), lax.axis_index("col")
    anc_all, order_all = anc_v.shape[0], lower_v.shape[1]
    width = par_v.shape[1]
    order_rows, anc_rows = block_ref.shape[0], anc_local.shape[0]
    off_width = offdiag_ref.shape[1]
    sent_width = sent_v.shape[1]
    leaf_at = sent_width + order_all
    leaf_width = (full_hbm.shape[1] - leaf_at) // 2
    copies = [
        pltpu.make_async_copy(full_hbm.at[:, pl.ds(0, sent_width)], sent_v, sem.at[0]),
        pltpu.make_async_copy(full_hbm.at[:, pl.ds(sent_width, order_all)], lower_v, sem.at[1]),
        pltpu.make_async_copy(
            full_hbm.at[:, pl.ds(pl.multiple_of(leaf_at + col * width, 128), width)], par_v, sem.at[2]
        ),
        pltpu.make_async_copy(
            full_hbm.at[:, pl.ds(pl.multiple_of(leaf_at + leaf_width + col * width, 128), width)],
            ancl_v,
            sem.at[3],
        ),
    ]
    for copy in copies:
        copy.start()
    copies[0].wait()
    blocks = anc_all // anc_rows
    for p in range(blocks):
        for q in range(blocks):
            k = (q - p) % blocks
            if k * anc_rows < sent_width:
                part = sent_v[p * anc_rows : (p + 1) * anc_rows, k * anc_rows : (k + 1) * anc_rows]
            else:
                k = (p - q) % blocks
                part = sent_v[q * anc_rows : (q + 1) * anc_rows, k * anc_rows : (k + 1) * anc_rows]
                part = part.astype(jnp.float32).T.astype(jnp.bfloat16)
            anc_v[p * anc_rows : (p + 1) * anc_rows, q * anc_rows : (q + 1) * anc_rows] = part
    copies[1].wait()
    lower_v[...] = lower_v[...] * lower_gate[...]
    lower = lower_v[...]
    lower_cols = lower_v[:, pl.ds(pl.multiple_of(row * order_rows, 128), order_rows)]
    offdiag_t = (
        -jnp.dot(lower_cols.T, anc_v[...], preferred_element_type=jnp.float32)
    ).astype(jnp.bfloat16)
    block = pivinv[...] - jnp.dot(offdiag_t, lower, preferred_element_type=jnp.float32)
    block_ref[...] = block
    rows = (-jnp.dot(anc_local[...], lower, preferred_element_type=jnp.float32)).astype(jnp.bfloat16)
    rows_v[...] = rows
    offdiag_ref[...] = rows_v[:, pl.ds(pl.multiple_of(col * off_width, 128), off_width)]
    copies[2].wait()
    copies[3].wait()
    par_v[...] = par_v[...] * par_gate[...]
    ancl_v[...] = ancl_v[...] * anc_gate[...]
    par, ancl = par_v[...], ancl_v[...]
    upper = jnp.dot(
        block.astype(jnp.bfloat16), par, preferred_element_type=jnp.float32
    ) + jnp.dot(offdiag_t, ancl, preferred_element_type=jnp.float32)
    par_block = (-upper).astype(jnp.bfloat16)
    lower_sum = jnp.dot(rows, par, preferred_element_type=jnp.float32) + jnp.dot(
        anc_local[...], ancl, preferred_element_type=jnp.float32
    )
    anc_block = (-lower_sum).astype(jnp.bfloat16)
    par_ref[...] = par_block
    anc_ref[...] = anc_block
    par_own = par_v[pl.ds(pl.multiple_of(row * order_rows, 8), order_rows), :]
    ancl_own = ancl_v[pl.ds(pl.multiple_of(row * anc_rows, 8), anc_rows), :]
    part = jnp.sum(
        par_own.astype(jnp.float32) * par_block.astype(jnp.float32), axis=0, keepdims=True
    ) + jnp.sum(ancl_own.astype(jnp.float32) * anc_block.astype(jnp.float32), axis=0, keepdims=True)
    part = jnp.where(row == 0, pivots[...] - part, -part)
    part_ref[...] = jnp.broadcast_to(part, part_ref.shape)


def local_whole(
    anc_inverse,
    parent_pivinv,
    parent_lower,
    parent_mask,
    leaf_lower_par,
    leaf_lower_anc,
    leaf_mask,
    leaf_pivots,
):
    row_index = lax.axis_index("row")
    row_devices = lax.axis_size("row")
    col_index = lax.axis_index("col")
    anc_rows = anc_inverse.shape[0]
    order_rows = parent_pivinv.shape[0]
    col_width = leaf_pivots.shape[0]
    off_width = parent_lower.shape[1] // 2
    half = anc_rows // 2
    anc_all = anc_rows * row_devices
    order_all = order_rows * row_devices

    sent_width = (row_devices // 2 + 1) * anc_rows
    piece_width = sent_width + order_all + 2 * leaf_lower_par.shape[1]
    piece = pl.pallas_call(
        piece_kernel,
        out_shape=jax.ShapeDtypeStruct((half, piece_width), jnp.bfloat16),
        in_specs=[pl.BlockSpec(memory_space=pltpu.VMEM)] * 4,
        out_specs=pl.BlockSpec(memory_space=pltpu.VMEM),
    )(anc_inverse, parent_lower, leaf_lower_par, leaf_lower_anc)
    full = lax.all_gather(piece, ("row", "col"), axis=0, tiled=True)
    parent_gate = jnp.repeat(parent_mask, BLOCK).astype(jnp.bfloat16)[:, None]
    leaf_gate = jnp.repeat(leaf_mask, BLOCK).astype(jnp.bfloat16)[:, None]
    vmem = pl.BlockSpec(memory_space=pltpu.VMEM)
    flops = 2 * (3 * order_rows * anc_all * order_all + 4 * order_rows * anc_all * col_width)
    block, offdiag_own, par_block, anc_block, parts = pl.pallas_call(
        leaf_kernel,
        out_shape=(
            jax.ShapeDtypeStruct((order_rows, order_all), jnp.float32),
            jax.ShapeDtypeStruct((anc_rows, off_width), jnp.bfloat16),
            jax.ShapeDtypeStruct((order_rows, col_width), jnp.bfloat16),
            jax.ShapeDtypeStruct((anc_rows, col_width), jnp.bfloat16),
            jax.ShapeDtypeStruct((row_devices, col_width), jnp.float32),
        ),
        in_specs=[vmem] * 4
        + [pl.BlockSpec(memory_space=pl.ANY)]
        + [vmem] * 2,
        out_specs=(vmem,) * 5,
        scratch_shapes=[
            pltpu.VMEM((anc_all, sent_width), jnp.bfloat16),
            pltpu.VMEM((anc_all, anc_all), jnp.bfloat16),
            pltpu.VMEM((anc_all, order_all), jnp.bfloat16),
            pltpu.VMEM((order_all, col_width), jnp.bfloat16),
            pltpu.VMEM((anc_all, col_width), jnp.bfloat16),
            pltpu.VMEM((anc_rows, order_all), jnp.bfloat16),
            pltpu.SemaphoreType.DMA((4,)),
        ],
        cost_estimate=pl.CostEstimate(
            flops=flops, transcendentals=0, bytes_accessed=full.size + 8 * anc_rows * order_all
        ),
    )(
        parent_gate,
        leaf_gate[:order_all],
        leaf_gate[order_all:],
        leaf_pivots[None, :],
        full,
        anc_inverse,
        parent_pivinv,
    )
    density = jnp.sum(lax.all_to_all(parts, "row", 0, 0), axis=0)
    return block, offdiag_own, par_block, anc_block, density


def fits_whole(mesh, anc_rows, order_rows):
    anc_all = anc_rows * mesh.shape["row"]
    return (
        anc_rows == order_rows
        and anc_rows % 128 == 0
        and anc_all * anc_all * 2 <= 16 * 1024 * 1024
    )


def solution(mesh):
    placed = (
        P(("pole", "row"), None),
        P(("pole", "row"), None),
        P(("pole", "row"), None),
        P(),
        P(("pole", "row"), None),
        P(("pole", "row"), None),
        P(),
        P(("pole", "col")),
    )
    placed_out = (
        P(("pole", "row"), None),
        P(("pole", "row"), "col"),
        P(("pole", "row"), "col"),
        P(("pole", "row"), "col"),
        P(("pole", "col")),
    )
    shards = mesh.shape["pole"] * mesh.shape["row"]

    def run(*args):
        anc_rows = args[0].shape[0] // shards
        order_rows = args[1].shape[0] // shards
        body = local_whole if fits_whole(mesh, anc_rows, order_rows) else local
        return jax.shard_map(
            body, mesh=mesh, in_specs=placed, out_specs=placed_out, check_vma=False
        )(*args)

    return run
```

```python
import jax
import jax.numpy as jnp
from jax import lax
from jax.experimental import pallas as pl
from jax.experimental.pallas import tpu as pltpu
from jax.sharding import PartitionSpec as P

BLOCK = 256
ORDER = 1024


def local(
    anc_inverse,
    parent_pivinv,
    parent_lower,
    parent_mask,
    leaf_lower_par,
    leaf_lower_anc,
    leaf_mask,
    leaf_pivots,
):
    row_index = lax.axis_index("row")
    row_devices = lax.axis_size("row")
    col_index = lax.axis_index("col")
    anc_rows = anc_inverse.shape[0]
    order_rows = parent_pivinv.shape[0]
    col_width = leaf_pivots.shape[0]
    parent_gate = lax.dynamic_slice_in_dim(
        jnp.repeat(parent_mask, BLOCK), row_index * anc_rows, anc_rows
    )
    lower_one = parent_lower * parent_gate[:, None].astype(jnp.bfloat16)
    lower_half = lax.dynamic_slice_in_dim(lower_one, col_index * col_width, col_width, 1)
    leaf_gate = jnp.repeat(leaf_mask, BLOCK)
    gate_par = lax.dynamic_slice_in_dim(leaf_gate[:ORDER], row_index * order_rows, order_rows)
    gate_anc = lax.dynamic_slice_in_dim(leaf_gate[ORDER:], row_index * anc_rows, anc_rows)
    leaf_local = jnp.concatenate(
        [
            leaf_lower_par * gate_par[:, None].astype(jnp.bfloat16),
            leaf_lower_anc * gate_anc[:, None].astype(jnp.bfloat16),
        ],
        axis=0,
    )
    leaf_half = lax.dynamic_slice_in_dim(leaf_local, col_index * col_width, col_width, 1)
    columns = anc_inverse
    product = jnp.dot(
        columns,
        lax.all_gather(lower_half, "row", axis=0, tiled=True),
        preferred_element_type=jnp.float32,
    )
    parent_offdiag = (-product).astype(jnp.bfloat16)
    offdiag_rows = lax.all_gather(parent_offdiag, "col", axis=1, tiled=True)
    columns = lower_one
    diag_sums = lax.psum_scatter(
        lax.dot_general(
            columns, offdiag_rows, (((0,), (0,)), ((), ())), preferred_element_type=jnp.float32
        ),
        "row",
        scatter_dimension=0,
        tiled=True,
    )
    parent_block = parent_pivinv - diag_sums
    parent_round = parent_block.astype(jnp.bfloat16)
    mirrored = lax.all_to_all(offdiag_rows, "row", split_axis=1, concat_axis=0, tiled=True).T
    upper_rows = jnp.concatenate(
        [
            parent_round.reshape(order_rows, row_devices, order_rows),
            mirrored.reshape(order_rows, row_devices, anc_rows),
        ],
        axis=2,
    )
    lower_rows = jnp.concatenate(
        [
            offdiag_rows.reshape(anc_rows, row_devices, order_rows),
            anc_inverse.reshape(anc_rows, row_devices, anc_rows),
        ],
        axis=2,
    )
    inverse_rows = jnp.concatenate(
        [upper_rows.reshape(order_rows, -1), lower_rows.reshape(anc_rows, -1)], axis=0
    )
    columns = inverse_rows
    leaf_product = jnp.dot(
        columns,
        lax.all_gather(leaf_half, "row", axis=0, tiled=True),
        preferred_element_type=jnp.float32,
    )
    leaf_result = (-leaf_product).astype(jnp.bfloat16)
    partial_sums = jnp.sum(leaf_half.astype(jnp.float32) * leaf_result.astype(jnp.float32), axis=0)
    density = leaf_pivots - lax.psum(partial_sums, "row")
    return (
        parent_block,
        parent_offdiag,
        leaf_result[:order_rows],
        leaf_result[order_rows:],
        density,
    )


def piece_kernel(anc_hbm, lower_hbm, par_hbm, ancl_hbm, out_ref):
    row, col = lax.axis_index("row"), lax.axis_index("col")
    half = out_ref.shape[0]
    blk = anc_hbm.shape[0]
    blocks = anc_hbm.shape[1] // blk
    sent = blocks // 2 + 1
    rows = pl.ds(pl.multiple_of(col * half, 8), half)
    for k in range(sent):
        start = pl.multiple_of(lax.rem(row + k, blocks) * blk, 128)
        out_ref[:, k * blk : (k + 1) * blk] = anc_hbm[rows, pl.ds(start, blk)]
    at = sent * blk
    for source in (lower_hbm, par_hbm, ancl_hbm):
        width = source.shape[1]
        out_ref[:, at : at + width] = source[rows, :]
        at += width


def leaf_kernel(
    lower_gate, par_gate, anc_gate, pivots, full_hbm, anc_local, pivinv,
    block_ref, offdiag_ref, par_ref, anc_ref, part_ref,
    sent_v, anc_v, lower_v, par_v, ancl_v, rows_v, sem,
):
    row, col = lax.axis_index("row"), lax.axis_index("col")
    anc_all, order_all = anc_v.shape[0], lower_v.shape[1]
    width = par_v.shape[1]
    order_rows, anc_rows = block_ref.shape[0], anc_local.shape[0]
    off_width = offdiag_ref.shape[1]
    sent_width = sent_v.shape[1]
    leaf_at = sent_width + order_all
    leaf_width = (full_hbm.shape[1] - leaf_at) // 2
    copies = [
        pltpu.make_async_copy(full_hbm.at[:, pl.ds(0, sent_width)], sent_v, sem.at[0]),
        pltpu.make_async_copy(full_hbm.at[:, pl.ds(sent_width, order_all)], lower_v, sem.at[1]),
        pltpu.make_async_copy(
            full_hbm.at[:, pl.ds(pl.multiple_of(leaf_at + col * width, 128), width)], par_v, sem.at[2]
        ),
        pltpu.make_async_copy(
            full_hbm.at[:, pl.ds(pl.multiple_of(leaf_at + leaf_width + col * width, 128), width)],
            ancl_v,
            sem.at[3],
        ),
    ]
    for copy in copies:
        copy.start()
    copies[0].wait()
    blocks = anc_all // anc_rows
    for p in range(blocks):
        for q in range(blocks):
            k = (q - p) % blocks
            if k * anc_rows < sent_width:
                part = sent_v[p * anc_rows : (p + 1) * anc_rows, k * anc_rows : (k + 1) * anc_rows]
            else:
                k = (p - q) % blocks
                part = sent_v[q * anc_rows : (q + 1) * anc_rows, k * anc_rows : (k + 1) * anc_rows]
                part = part.astype(jnp.float32).T.astype(jnp.bfloat16)
            anc_v[p * anc_rows : (p + 1) * anc_rows, q * anc_rows : (q + 1) * anc_rows] = part
    copies[1].wait()
    lower = lower_v[...]
    gate_row = lower_gate[...]
    lower_cols = lower_v[:, pl.ds(pl.multiple_of(row * order_rows, 128), order_rows)] * gate_row
    offdiag_t = (
        -jnp.dot(lower_cols.T, anc_v[...], preferred_element_type=jnp.float32)
    ).astype(jnp.bfloat16)
    gate_col = gate_row.T
    block = pivinv[...] - jnp.dot(offdiag_t * gate_col, lower, preferred_element_type=jnp.float32)
    block_ref[...] = block
    anc_here = anc_local[...]
    rows = (-jnp.dot(anc_here * gate_col, lower, preferred_element_type=jnp.float32)).astype(
        jnp.bfloat16
    )
    rows_v[...] = rows
    offdiag_ref[...] = rows_v[:, pl.ds(pl.multiple_of(col * off_width, 128), off_width)]
    copies[2].wait()
    copies[3].wait()
    par_col = par_gate[...].T
    anc_col = anc_gate[...].T
    par, ancl = par_v[...], ancl_v[...]
    upper = jnp.dot(
        block.astype(jnp.bfloat16) * par_col, par, preferred_element_type=jnp.float32
    ) + jnp.dot(offdiag_t * anc_col, ancl, preferred_element_type=jnp.float32)
    par_block = (-upper).astype(jnp.bfloat16)
    lower_sum = jnp.dot(rows * par_col, par, preferred_element_type=jnp.float32) + jnp.dot(
        anc_here * anc_col, ancl, preferred_element_type=jnp.float32
    )
    anc_block = (-lower_sum).astype(jnp.bfloat16)
    par_ref[...] = par_block
    anc_ref[...] = anc_block
    par_own = par_v[pl.ds(pl.multiple_of(row * order_rows, 8), order_rows), :] * par_gate[
        pl.ds(pl.multiple_of(row * order_rows, 8), order_rows), :
    ]
    ancl_own = ancl_v[pl.ds(pl.multiple_of(row * anc_rows, 8), anc_rows), :] * anc_gate[
        pl.ds(pl.multiple_of(row * anc_rows, 8), anc_rows), :
    ]
    part = jnp.sum(
        par_own.astype(jnp.float32) * par_block.astype(jnp.float32), axis=0, keepdims=True
    ) + jnp.sum(ancl_own.astype(jnp.float32) * anc_block.astype(jnp.float32), axis=0, keepdims=True)
    part = jnp.where(row == 0, pivots[...] - part, -part)
    part_ref[...] = jnp.broadcast_to(part, part_ref.shape)


def local_whole(
    anc_inverse,
    parent_pivinv,
    parent_lower,
    parent_mask,
    leaf_lower_par,
    leaf_lower_anc,
    leaf_mask,
    leaf_pivots,
):
    row_index = lax.axis_index("row")
    row_devices = lax.axis_size("row")
    col_index = lax.axis_index("col")
    anc_rows = anc_inverse.shape[0]
    order_rows = parent_pivinv.shape[0]
    col_width = leaf_pivots.shape[0]
    off_width = parent_lower.shape[1] // 2
    half = anc_rows // 2
    anc_all = anc_rows * row_devices
    order_all = order_rows * row_devices

    sent_width = (row_devices // 2 + 1) * anc_rows
    piece_width = sent_width + order_all + 2 * leaf_lower_par.shape[1]
    piece = pl.pallas_call(
        piece_kernel,
        out_shape=jax.ShapeDtypeStruct((half, piece_width), jnp.bfloat16),
        in_specs=[pl.BlockSpec(memory_space=pltpu.VMEM)] * 4,
        out_specs=pl.BlockSpec(memory_space=pltpu.VMEM),
    )(anc_inverse, parent_lower, leaf_lower_par, leaf_lower_anc)
    full = lax.all_gather(piece, ("row", "col"), axis=0, tiled=True)
    parent_gate = jnp.repeat(parent_mask, BLOCK).astype(jnp.bfloat16)[:, None]
    leaf_gate = jnp.repeat(leaf_mask, BLOCK).astype(jnp.bfloat16)[:, None]
    vmem = pl.BlockSpec(memory_space=pltpu.VMEM)
    flops = 2 * (3 * order_rows * anc_all * order_all + 4 * order_rows * anc_all * col_width)
    block, offdiag_own, par_block, anc_block, parts = pl.pallas_call(
        leaf_kernel,
        out_shape=(
            jax.ShapeDtypeStruct((order_rows, order_all), jnp.float32),
            jax.ShapeDtypeStruct((anc_rows, off_width), jnp.bfloat16),
            jax.ShapeDtypeStruct((order_rows, col_width), jnp.bfloat16),
            jax.ShapeDtypeStruct((anc_rows, col_width), jnp.bfloat16),
            jax.ShapeDtypeStruct((1, col_width), jnp.float32),
        ),
        in_specs=[vmem] * 4
        + [pl.BlockSpec(memory_space=pl.ANY)]
        + [vmem] * 2,
        out_specs=(vmem,) * 5,
        scratch_shapes=[
            pltpu.VMEM((anc_all, sent_width), jnp.bfloat16),
            pltpu.VMEM((anc_all, anc_all), jnp.bfloat16),
            pltpu.VMEM((anc_all, order_all), jnp.bfloat16),
            pltpu.VMEM((order_all, col_width), jnp.bfloat16),
            pltpu.VMEM((anc_all, col_width), jnp.bfloat16),
            pltpu.VMEM((anc_rows, order_all), jnp.bfloat16),
            pltpu.SemaphoreType.DMA((4,)),
        ],
        cost_estimate=pl.CostEstimate(
            flops=flops, transcendentals=0, bytes_accessed=full.size + 8 * anc_rows * order_all
        ),
    )(
        parent_gate,
        leaf_gate[:order_all],
        leaf_gate[order_all:],
        leaf_pivots[None, :],
        full,
        anc_inverse,
        parent_pivinv,
    )
    step = 1
    while step < row_devices:
        pairs = [(i, i ^ step) for i in range(row_devices)]
        parts = parts + lax.ppermute(parts, "row", pairs)
        step *= 2
    density = parts[0]
    return block, offdiag_own, par_block, anc_block, density


def fits_whole(mesh, anc_rows, order_rows):
    anc_all = anc_rows * mesh.shape["row"]
    return (
        anc_rows == order_rows
        and anc_rows % 128 == 0
        and mesh.shape["row"] & (mesh.shape["row"] - 1) == 0
        and anc_all * anc_all * 2 <= 16 * 1024 * 1024
    )


def solution(mesh):
    placed = (
        P(("pole", "row"), None),
        P(("pole", "row"), None),
        P(("pole", "row"), None),
        P(),
        P(("pole", "row"), None),
        P(("pole", "row"), None),
        P(),
        P(("pole", "col")),
    )
    placed_out = (
        P(("pole", "row"), None),
        P(("pole", "row"), "col"),
        P(("pole", "row"), "col"),
        P(("pole", "row"), "col"),
        P(("pole", "col")),
    )
    shards = mesh.shape["pole"] * mesh.shape["row"]

    def run(*args):
        anc_rows = args[0].shape[0] // shards
        order_rows = args[1].shape[0] // shards
        body = local_whole if fits_whole(mesh, anc_rows, order_rows) else local
        return jax.shard_map(
            body, mesh=mesh, in_specs=placed, out_specs=placed_out, check_vma=False
        )(*args)

    return run
```

```python
import jax
import jax.numpy as jnp
from jax import lax
from jax.experimental import pallas as pl
from jax.experimental.pallas import tpu as pltpu
from jax.sharding import PartitionSpec as P

BLOCK = 256
ORDER = 1024


def local(
    anc_inverse,
    parent_pivinv,
    parent_lower,
    parent_mask,
    leaf_lower_par,
    leaf_lower_anc,
    leaf_mask,
    leaf_pivots,
):
    row_index = lax.axis_index("row")
    row_devices = lax.axis_size("row")
    col_index = lax.axis_index("col")
    anc_rows = anc_inverse.shape[0]
    order_rows = parent_pivinv.shape[0]
    col_width = leaf_pivots.shape[0]
    parent_gate = lax.dynamic_slice_in_dim(
        jnp.repeat(parent_mask, BLOCK), row_index * anc_rows, anc_rows
    )
    lower_one = parent_lower * parent_gate[:, None].astype(jnp.bfloat16)
    lower_half = lax.dynamic_slice_in_dim(lower_one, col_index * col_width, col_width, 1)
    leaf_gate = jnp.repeat(leaf_mask, BLOCK)
    gate_par = lax.dynamic_slice_in_dim(leaf_gate[:ORDER], row_index * order_rows, order_rows)
    gate_anc = lax.dynamic_slice_in_dim(leaf_gate[ORDER:], row_index * anc_rows, anc_rows)
    leaf_local = jnp.concatenate(
        [
            leaf_lower_par * gate_par[:, None].astype(jnp.bfloat16),
            leaf_lower_anc * gate_anc[:, None].astype(jnp.bfloat16),
        ],
        axis=0,
    )
    leaf_half = lax.dynamic_slice_in_dim(leaf_local, col_index * col_width, col_width, 1)
    columns = anc_inverse
    product = jnp.dot(
        columns,
        lax.all_gather(lower_half, "row", axis=0, tiled=True),
        preferred_element_type=jnp.float32,
    )
    parent_offdiag = (-product).astype(jnp.bfloat16)
    offdiag_rows = lax.all_gather(parent_offdiag, "col", axis=1, tiled=True)
    columns = lower_one
    diag_sums = lax.psum_scatter(
        lax.dot_general(
            columns, offdiag_rows, (((0,), (0,)), ((), ())), preferred_element_type=jnp.float32
        ),
        "row",
        scatter_dimension=0,
        tiled=True,
    )
    parent_block = parent_pivinv - diag_sums
    parent_round = parent_block.astype(jnp.bfloat16)
    mirrored = lax.all_to_all(offdiag_rows, "row", split_axis=1, concat_axis=0, tiled=True).T
    upper_rows = jnp.concatenate(
        [
            parent_round.reshape(order_rows, row_devices, order_rows),
            mirrored.reshape(order_rows, row_devices, anc_rows),
        ],
        axis=2,
    )
    lower_rows = jnp.concatenate(
        [
            offdiag_rows.reshape(anc_rows, row_devices, order_rows),
            anc_inverse.reshape(anc_rows, row_devices, anc_rows),
        ],
        axis=2,
    )
    inverse_rows = jnp.concatenate(
        [upper_rows.reshape(order_rows, -1), lower_rows.reshape(anc_rows, -1)], axis=0
    )
    columns = inverse_rows
    leaf_product = jnp.dot(
        columns,
        lax.all_gather(leaf_half, "row", axis=0, tiled=True),
        preferred_element_type=jnp.float32,
    )
    leaf_result = (-leaf_product).astype(jnp.bfloat16)
    partial_sums = jnp.sum(leaf_half.astype(jnp.float32) * leaf_result.astype(jnp.float32), axis=0)
    density = leaf_pivots - lax.psum(partial_sums, "row")
    return (
        parent_block,
        parent_offdiag,
        leaf_result[:order_rows],
        leaf_result[order_rows:],
        density,
    )


def piece_kernel(anc_hbm, lower_hbm, par_hbm, ancl_hbm, out_ref):
    row, col = lax.axis_index("row"), lax.axis_index("col")
    half = out_ref.shape[0]
    blk = anc_hbm.shape[0]
    blocks = anc_hbm.shape[1] // blk
    sent = blocks // 2 + 1
    rows = pl.ds(pl.multiple_of(col * half, 8), half)
    for k in range(sent):
        start = pl.multiple_of(lax.rem(row + k, blocks) * blk, 128)
        out_ref[:, k * blk : (k + 1) * blk] = anc_hbm[rows, pl.ds(start, blk)]
    at = sent * blk
    for source in (lower_hbm, par_hbm, ancl_hbm):
        width = source.shape[1]
        out_ref[:, at : at + width] = source[rows, :]
        at += width


def leaf_kernel(
    lower_gate, par_gate, anc_gate, pivots, full_hbm, anc_local, pivinv,
    block_ref, offdiag_ref, par_ref, anc_ref, part_ref,
    anc_v, lower_v, par_v, ancl_v, rows_v, sem, anc_sem,
):
    row, col = lax.axis_index("row"), lax.axis_index("col")
    anc_all, order_all = anc_v.shape[0], lower_v.shape[1]
    width = par_v.shape[1]
    order_rows, anc_rows = block_ref.shape[0], anc_local.shape[0]
    off_width = offdiag_ref.shape[1]
    blocks = anc_all // anc_rows
    sent = blocks // 2 + 1
    sent_width = sent * anc_rows
    leaf_at = sent_width + order_all
    leaf_width = (full_hbm.shape[1] - leaf_at) // 2
    anc_copies = []
    for p in range(blocks):
        rows_p = pl.ds(p * anc_rows, anc_rows)
        first = min(sent, blocks - p)
        pieces = [(0, p, first)]
        if first < sent:
            pieces.append((first, 0, sent - first))
        for src_block, dst_block, count in pieces:
            anc_copies.append(
                pltpu.make_async_copy(
                    full_hbm.at[rows_p, pl.ds(src_block * anc_rows, count * anc_rows)],
                    anc_v.at[rows_p, pl.ds(dst_block * anc_rows, count * anc_rows)],
                    anc_sem.at[len(anc_copies)],
                )
            )
    copies = [
        pltpu.make_async_copy(full_hbm.at[:, pl.ds(sent_width, order_all)], lower_v, sem.at[0]),
        pltpu.make_async_copy(
            full_hbm.at[:, pl.ds(pl.multiple_of(leaf_at + col * width, 128), width)], par_v, sem.at[1]
        ),
        pltpu.make_async_copy(
            full_hbm.at[:, pl.ds(pl.multiple_of(leaf_at + leaf_width + col * width, 128), width)],
            ancl_v,
            sem.at[2],
        ),
    ]
    for copy in anc_copies + copies:
        copy.start()
    for copy in anc_copies:
        copy.wait()
    for p in range(blocks):
        for q in range(blocks):
            if (q - p) % blocks >= sent:
                part = anc_v[q * anc_rows : (q + 1) * anc_rows, p * anc_rows : (p + 1) * anc_rows]
                anc_v[p * anc_rows : (p + 1) * anc_rows, q * anc_rows : (q + 1) * anc_rows] = (
                    part.astype(jnp.float32).T.astype(jnp.bfloat16)
                )
    copies[0].wait()
    lower_v[...] = lower_v[...] * lower_gate[...]
    lower = lower_v[...]
    lower_cols = lower_v[:, pl.ds(pl.multiple_of(row * order_rows, 128), order_rows)]
    offdiag_t = (
        -jnp.dot(lower_cols.T, anc_v[...], preferred_element_type=jnp.float32)
    ).astype(jnp.bfloat16)
    block = pivinv[...] - jnp.dot(offdiag_t, lower, preferred_element_type=jnp.float32)
    block_ref[...] = block
    rows = (-jnp.dot(anc_local[...], lower, preferred_element_type=jnp.float32)).astype(jnp.bfloat16)
    rows_v[...] = rows
    offdiag_ref[...] = rows_v[:, pl.ds(pl.multiple_of(col * off_width, 128), off_width)]
    copies[1].wait()
    copies[2].wait()
    par_v[...] = par_v[...] * par_gate[...]
    ancl_v[...] = ancl_v[...] * anc_gate[...]
    par, ancl = par_v[...], ancl_v[...]
    upper = jnp.dot(
        block.astype(jnp.bfloat16), par, preferred_element_type=jnp.float32
    ) + jnp.dot(offdiag_t, ancl, preferred_element_type=jnp.float32)
    par_block = (-upper).astype(jnp.bfloat16)
    lower_sum = jnp.dot(rows, par, preferred_element_type=jnp.float32) + jnp.dot(
        anc_local[...], ancl, preferred_element_type=jnp.float32
    )
    anc_block = (-lower_sum).astype(jnp.bfloat16)
    par_ref[...] = par_block
    anc_ref[...] = anc_block
    par_own = par_v[pl.ds(pl.multiple_of(row * order_rows, 8), order_rows), :]
    ancl_own = ancl_v[pl.ds(pl.multiple_of(row * anc_rows, 8), anc_rows), :]
    part = jnp.sum(
        par_own.astype(jnp.float32) * par_block.astype(jnp.float32), axis=0, keepdims=True
    ) + jnp.sum(ancl_own.astype(jnp.float32) * anc_block.astype(jnp.float32), axis=0, keepdims=True)
    part = jnp.where(row == 0, pivots[...] - part, -part)
    for i in range(part_ref.shape[0]):
        part_ref[i] = part


def local_whole(
    anc_inverse,
    parent_pivinv,
    parent_lower,
    parent_mask,
    leaf_lower_par,
    leaf_lower_anc,
    leaf_mask,
    leaf_pivots,
):
    row_index = lax.axis_index("row")
    row_devices = lax.axis_size("row")
    col_index = lax.axis_index("col")
    anc_rows = anc_inverse.shape[0]
    order_rows = parent_pivinv.shape[0]
    col_width = leaf_pivots.shape[0]
    off_width = parent_lower.shape[1] // 2
    half = anc_rows // 2
    anc_all = anc_rows * row_devices
    order_all = order_rows * row_devices

    sent_width = (row_devices // 2 + 1) * anc_rows
    piece_width = sent_width + order_all + 2 * leaf_lower_par.shape[1]
    piece = pl.pallas_call(
        piece_kernel,
        out_shape=jax.ShapeDtypeStruct((half, piece_width), jnp.bfloat16),
        in_specs=[pl.BlockSpec(memory_space=pltpu.VMEM)] * 4,
        out_specs=pl.BlockSpec(memory_space=pltpu.VMEM),
    )(anc_inverse, parent_lower, leaf_lower_par, leaf_lower_anc)
    full = lax.all_gather(piece, ("row", "col"), axis=0, tiled=True)
    parent_gate = jnp.repeat(parent_mask, BLOCK).astype(jnp.bfloat16)[:, None]
    leaf_gate = jnp.repeat(leaf_mask, BLOCK).astype(jnp.bfloat16)[:, None]
    vmem = pl.BlockSpec(memory_space=pltpu.VMEM)
    flops = 2 * (3 * order_rows * anc_all * order_all + 4 * order_rows * anc_all * col_width)
    block, offdiag_own, par_block, anc_block, parts = pl.pallas_call(
        leaf_kernel,
        out_shape=(
            jax.ShapeDtypeStruct((order_rows, order_all), jnp.float32),
            jax.ShapeDtypeStruct((anc_rows, off_width), jnp.bfloat16),
            jax.ShapeDtypeStruct((order_rows, col_width), jnp.bfloat16),
            jax.ShapeDtypeStruct((anc_rows, col_width), jnp.bfloat16),
            jax.ShapeDtypeStruct((row_devices, 1, col_width), jnp.float32),
        ),
        in_specs=[vmem] * 4
        + [pl.BlockSpec(memory_space=pl.ANY)]
        + [vmem] * 2,
        out_specs=(vmem,) * 5,
        scratch_shapes=[
            pltpu.VMEM((anc_all, anc_all), jnp.bfloat16),
            pltpu.VMEM((anc_all, order_all), jnp.bfloat16),
            pltpu.VMEM((order_all, col_width), jnp.bfloat16),
            pltpu.VMEM((anc_all, col_width), jnp.bfloat16),
            pltpu.VMEM((anc_rows, order_all), jnp.bfloat16),
            pltpu.SemaphoreType.DMA((3,)),
            pltpu.SemaphoreType.DMA((2 * row_devices,)),
        ],
        cost_estimate=pl.CostEstimate(
            flops=flops, transcendentals=0, bytes_accessed=full.size + 8 * anc_rows * order_all
        ),
    )(
        parent_gate,
        leaf_gate[:order_all],
        leaf_gate[order_all:],
        leaf_pivots[None, :],
        full,
        anc_inverse,
        parent_pivinv,
    )
    density = jnp.sum(lax.all_to_all(parts, "row", 0, 0, tiled=True), axis=0)[0]
    return block, offdiag_own, par_block, anc_block, density


def fits_whole(mesh, anc_rows, order_rows):
    anc_all = anc_rows * mesh.shape["row"]
    return (
        anc_rows == order_rows
        and anc_rows % 128 == 0
        and anc_all * anc_all * 2 <= 16 * 1024 * 1024
    )


def solution(mesh):
    placed = (
        P(("pole", "row"), None),
        P(("pole", "row"), None),
        P(("pole", "row"), None),
        P(),
        P(("pole", "row"), None),
        P(("pole", "row"), None),
        P(),
        P(("pole", "col")),
    )
    placed_out = (
        P(("pole", "row"), None),
        P(("pole", "row"), "col"),
        P(("pole", "row"), "col"),
        P(("pole", "row"), "col"),
        P(("pole", "col")),
    )
    shards = mesh.shape["pole"] * mesh.shape["row"]

    def run(*args):
        anc_rows = args[0].shape[0] // shards
        order_rows = args[1].shape[0] // shards
        body = local_whole if fits_whole(mesh, anc_rows, order_rows) else local
        return jax.shard_map(
            body, mesh=mesh, in_specs=placed, out_specs=placed_out, check_vma=False
        )(*args)

    return run
```

```python
import jax
import jax.numpy as jnp
from jax import lax
from jax.experimental import pallas as pl
from jax.experimental.pallas import tpu as pltpu
from jax.sharding import PartitionSpec as P

BLOCK = 256
ORDER = 1024


def local(
    anc_inverse,
    parent_pivinv,
    parent_lower,
    parent_mask,
    leaf_lower_par,
    leaf_lower_anc,
    leaf_mask,
    leaf_pivots,
):
    row_index = lax.axis_index("row")
    row_devices = lax.axis_size("row")
    col_index = lax.axis_index("col")
    anc_rows = anc_inverse.shape[0]
    order_rows = parent_pivinv.shape[0]
    col_width = leaf_pivots.shape[0]
    parent_gate = lax.dynamic_slice_in_dim(
        jnp.repeat(parent_mask, BLOCK), row_index * anc_rows, anc_rows
    )
    lower_one = parent_lower * parent_gate[:, None].astype(jnp.bfloat16)
    lower_half = lax.dynamic_slice_in_dim(lower_one, col_index * col_width, col_width, 1)
    leaf_gate = jnp.repeat(leaf_mask, BLOCK)
    gate_par = lax.dynamic_slice_in_dim(leaf_gate[:ORDER], row_index * order_rows, order_rows)
    gate_anc = lax.dynamic_slice_in_dim(leaf_gate[ORDER:], row_index * anc_rows, anc_rows)
    leaf_local = jnp.concatenate(
        [
            leaf_lower_par * gate_par[:, None].astype(jnp.bfloat16),
            leaf_lower_anc * gate_anc[:, None].astype(jnp.bfloat16),
        ],
        axis=0,
    )
    leaf_half = lax.dynamic_slice_in_dim(leaf_local, col_index * col_width, col_width, 1)
    columns = anc_inverse
    product = jnp.dot(
        columns,
        lax.all_gather(lower_half, "row", axis=0, tiled=True),
        preferred_element_type=jnp.float32,
    )
    parent_offdiag = (-product).astype(jnp.bfloat16)
    offdiag_rows = lax.all_gather(parent_offdiag, "col", axis=1, tiled=True)
    columns = lower_one
    diag_sums = lax.psum_scatter(
        lax.dot_general(
            columns, offdiag_rows, (((0,), (0,)), ((), ())), preferred_element_type=jnp.float32
        ),
        "row",
        scatter_dimension=0,
        tiled=True,
    )
    parent_block = parent_pivinv - diag_sums
    parent_round = parent_block.astype(jnp.bfloat16)
    mirrored = lax.all_to_all(offdiag_rows, "row", split_axis=1, concat_axis=0, tiled=True).T
    upper_rows = jnp.concatenate(
        [
            parent_round.reshape(order_rows, row_devices, order_rows),
            mirrored.reshape(order_rows, row_devices, anc_rows),
        ],
        axis=2,
    )
    lower_rows = jnp.concatenate(
        [
            offdiag_rows.reshape(anc_rows, row_devices, order_rows),
            anc_inverse.reshape(anc_rows, row_devices, anc_rows),
        ],
        axis=2,
    )
    inverse_rows = jnp.concatenate(
        [upper_rows.reshape(order_rows, -1), lower_rows.reshape(anc_rows, -1)], axis=0
    )
    columns = inverse_rows
    leaf_product = jnp.dot(
        columns,
        lax.all_gather(leaf_half, "row", axis=0, tiled=True),
        preferred_element_type=jnp.float32,
    )
    leaf_result = (-leaf_product).astype(jnp.bfloat16)
    partial_sums = jnp.sum(leaf_half.astype(jnp.float32) * leaf_result.astype(jnp.float32), axis=0)
    density = leaf_pivots - lax.psum(partial_sums, "row")
    return (
        parent_block,
        parent_offdiag,
        leaf_result[:order_rows],
        leaf_result[order_rows:],
        density,
    )


def piece_kernel(anc_hbm, lower_hbm, par_hbm, ancl_hbm, out_ref):
    row, col = lax.axis_index("row"), lax.axis_index("col")
    half = out_ref.shape[0]
    blk = anc_hbm.shape[0]
    blocks = anc_hbm.shape[1] // blk
    sent = blocks // 2 + 1
    rows = pl.ds(pl.multiple_of(col * half, 8), half)
    for k in range(sent):
        start = pl.multiple_of(lax.rem(row + k, blocks) * blk, 128)
        out_ref[:, k * blk : (k + 1) * blk] = anc_hbm[rows, pl.ds(start, blk)]
    at = sent * blk
    for source in (lower_hbm, par_hbm, ancl_hbm):
        width = source.shape[1]
        out_ref[:, at : at + width] = source[rows, :]
        at += width


def leaf_kernel(
    lower_gate, par_gate, anc_gate, pivots, full_hbm, anc_local, pivinv,
    block_ref, offdiag_ref, par_ref, anc_ref, part_ref,
    sent_v, anc_v, lower_v, par_v, ancl_v, rows_v, sem,
):
    row, col = lax.axis_index("row"), lax.axis_index("col")
    anc_all, order_all = anc_v.shape[0], lower_v.shape[1]
    width = par_v.shape[1]
    order_rows, anc_rows = block_ref.shape[0], anc_local.shape[0]
    off_width = offdiag_ref.shape[1]
    sent_width = sent_v.shape[1]
    leaf_at = sent_width + order_all
    leaf_width = (full_hbm.shape[1] - leaf_at) // 2
    copies = [
        pltpu.make_async_copy(full_hbm.at[:, pl.ds(0, sent_width)], sent_v, sem.at[0]),
        pltpu.make_async_copy(full_hbm.at[:, pl.ds(sent_width, order_all)], lower_v, sem.at[1]),
        pltpu.make_async_copy(
            full_hbm.at[:, pl.ds(pl.multiple_of(leaf_at + col * width, 128), width)], par_v, sem.at[2]
        ),
        pltpu.make_async_copy(
            full_hbm.at[:, pl.ds(pl.multiple_of(leaf_at + leaf_width + col * width, 128), width)],
            ancl_v,
            sem.at[3],
        ),
    ]
    for copy in copies:
        copy.start()
    copies[0].wait()
    blocks = anc_all // anc_rows
    for p in range(blocks):
        for q in range(blocks):
            k = (q - p) % blocks
            if k * anc_rows < sent_width:
                part = sent_v[p * anc_rows : (p + 1) * anc_rows, k * anc_rows : (k + 1) * anc_rows]
            else:
                k = (p - q) % blocks
                part = sent_v[q * anc_rows : (q + 1) * anc_rows, k * anc_rows : (k + 1) * anc_rows]
                part = part.astype(jnp.float32).T.astype(jnp.bfloat16)
            anc_v[p * anc_rows : (p + 1) * anc_rows, q * anc_rows : (q + 1) * anc_rows] = part
    copies[1].wait()
    lower_v[...] = lower_v[...] * lower_gate[...]
    lower = lower_v[...]
    lower_cols = lower_v[:, pl.ds(pl.multiple_of(row * order_rows, 128), order_rows)]
    offdiag_t = (
        -jnp.dot(lower_cols.T, anc_v[...], preferred_element_type=jnp.float32)
    ).astype(jnp.bfloat16)
    block = pivinv[...] - jnp.dot(offdiag_t, lower, preferred_element_type=jnp.float32)
    block_ref[...] = block
    rows = (-jnp.dot(anc_local[...], lower, preferred_element_type=jnp.float32)).astype(jnp.bfloat16)
    rows_v[...] = rows
    offdiag_ref[...] = rows_v[:, pl.ds(pl.multiple_of(col * off_width, 128), off_width)]
    copies[2].wait()
    copies[3].wait()
    par_v[...] = par_v[...] * par_gate[...]
    ancl_v[...] = ancl_v[...] * anc_gate[...]
    par, ancl = par_v[...], ancl_v[...]
    upper = jnp.dot(
        block.astype(jnp.bfloat16), par, preferred_element_type=jnp.float32
    ) + jnp.dot(offdiag_t, ancl, preferred_element_type=jnp.float32)
    par_block = (-upper).astype(jnp.bfloat16)
    lower_sum = jnp.dot(rows, par, preferred_element_type=jnp.float32) + jnp.dot(
        anc_local[...], ancl, preferred_element_type=jnp.float32
    )
    anc_block = (-lower_sum).astype(jnp.bfloat16)
    par_ref[...] = par_block
    anc_ref[...] = anc_block
    par_own = par_v[pl.ds(pl.multiple_of(row * order_rows, 8), order_rows), :]
    ancl_own = ancl_v[pl.ds(pl.multiple_of(row * anc_rows, 8), anc_rows), :]
    part = jnp.sum(
        par_own.astype(jnp.float32) * par_block.astype(jnp.float32), axis=0, keepdims=True
    ) + jnp.sum(ancl_own.astype(jnp.float32) * anc_block.astype(jnp.float32), axis=0, keepdims=True)
    part = jnp.where(row == 0, pivots[...] - part, -part)
    for i in range(part_ref.shape[0]):
        part_ref[i] = part


def local_whole(
    anc_inverse,
    parent_pivinv,
    parent_lower,
    parent_mask,
    leaf_lower_par,
    leaf_lower_anc,
    leaf_mask,
    leaf_pivots,
):
    row_index = lax.axis_index("row")
    row_devices = lax.axis_size("row")
    col_index = lax.axis_index("col")
    anc_rows = anc_inverse.shape[0]
    order_rows = parent_pivinv.shape[0]
    col_width = leaf_pivots.shape[0]
    off_width = parent_lower.shape[1] // 2
    half = anc_rows // 2
    anc_all = anc_rows * row_devices
    order_all = order_rows * row_devices

    sent_width = (row_devices // 2 + 1) * anc_rows
    piece_width = sent_width + order_all + 2 * leaf_lower_par.shape[1]
    piece = pl.pallas_call(
        piece_kernel,
        out_shape=jax.ShapeDtypeStruct((half, piece_width), jnp.bfloat16),
        in_specs=[pl.BlockSpec(memory_space=pltpu.VMEM)] * 4,
        out_specs=pl.BlockSpec(memory_space=pltpu.VMEM),
    )(anc_inverse, parent_lower, leaf_lower_par, leaf_lower_anc)
    full = lax.all_gather(piece, ("row", "col"), axis=0, tiled=True)
    parent_gate = jnp.repeat(parent_mask, BLOCK).astype(jnp.bfloat16)[:, None]
    leaf_gate = jnp.repeat(leaf_mask, BLOCK).astype(jnp.bfloat16)[:, None]
    vmem = pl.BlockSpec(memory_space=pltpu.VMEM)
    flops = 2 * (3 * order_rows * anc_all * order_all + 4 * order_rows * anc_all * col_width)
    block, offdiag_own, par_block, anc_block, parts = pl.pallas_call(
        leaf_kernel,
        out_shape=(
            jax.ShapeDtypeStruct((order_rows, order_all), jnp.float32),
            jax.ShapeDtypeStruct((anc_rows, off_width), jnp.bfloat16),
            jax.ShapeDtypeStruct((order_rows, col_width), jnp.bfloat16),
            jax.ShapeDtypeStruct((anc_rows, col_width), jnp.bfloat16),
            jax.ShapeDtypeStruct((row_devices, 1, col_width), jnp.float32),
        ),
        in_specs=[vmem] * 4
        + [pl.BlockSpec(memory_space=pl.ANY)]
        + [vmem] * 2,
        out_specs=(vmem,) * 5,
        scratch_shapes=[
            pltpu.VMEM((anc_all, sent_width), jnp.bfloat16),
            pltpu.VMEM((anc_all, anc_all), jnp.bfloat16),
            pltpu.VMEM((anc_all, order_all), jnp.bfloat16),
            pltpu.VMEM((order_all, col_width), jnp.bfloat16),
            pltpu.VMEM((anc_all, col_width), jnp.bfloat16),
            pltpu.VMEM((anc_rows, order_all), jnp.bfloat16),
            pltpu.SemaphoreType.DMA((4,)),
        ],
        cost_estimate=pl.CostEstimate(
            flops=flops, transcendentals=0, bytes_accessed=full.size + 8 * anc_rows * order_all
        ),
    )(
        parent_gate,
        leaf_gate[:order_all],
        leaf_gate[order_all:],
        leaf_pivots[None, :],
        full,
        anc_inverse,
        parent_pivinv,
    )
    density = jnp.sum(lax.all_to_all(parts, "row", 0, 0, tiled=True), axis=0)[0]
    return block, offdiag_own, par_block, anc_block, density


def fits_whole(mesh, anc_rows, order_rows):
    anc_all = anc_rows * mesh.shape["row"]
    return (
        anc_rows == order_rows
        and anc_rows % 128 == 0
        and anc_all * anc_all * 2 <= 16 * 1024 * 1024
    )


def solution(mesh):
    placed = (
        P(("pole", "row"), None),
        P(("pole", "row"), None),
        P(("pole", "row"), None),
        P(),
        P(("pole", "row"), None),
        P(("pole", "row"), None),
        P(),
        P(("pole", "col")),
    )
    placed_out = (
        P(("pole", "row"), None),
        P(("pole", "row"), "col"),
        P(("pole", "row"), "col"),
        P(("pole", "row"), "col"),
        P(("pole", "col")),
    )
    shards = mesh.shape["pole"] * mesh.shape["row"]

    def run(*args):
        anc_rows = args[0].shape[0] // shards
        order_rows = args[1].shape[0] // shards
        body = local_whole if fits_whole(mesh, anc_rows, order_rows) else local
        return jax.shard_map(
            body, mesh=mesh, in_specs=placed, out_specs=placed_out, check_vma=False
        )(*args)

    return run
```

```python
import jax
import jax.numpy as jnp
from jax import lax
from jax.experimental import pallas as pl
from jax.experimental.pallas import tpu as pltpu
from jax.sharding import PartitionSpec as P

BLOCK = 256
ORDER = 1024


def local(
    anc_inverse,
    parent_pivinv,
    parent_lower,
    parent_mask,
    leaf_lower_par,
    leaf_lower_anc,
    leaf_mask,
    leaf_pivots,
):
    row_index = lax.axis_index("row")
    row_devices = lax.axis_size("row")
    col_index = lax.axis_index("col")
    anc_rows = anc_inverse.shape[0]
    order_rows = parent_pivinv.shape[0]
    col_width = leaf_pivots.shape[0]
    parent_gate = lax.dynamic_slice_in_dim(
        jnp.repeat(parent_mask, BLOCK), row_index * anc_rows, anc_rows
    )
    lower_one = parent_lower * parent_gate[:, None].astype(jnp.bfloat16)
    lower_half = lax.dynamic_slice_in_dim(lower_one, col_index * col_width, col_width, 1)
    leaf_gate = jnp.repeat(leaf_mask, BLOCK)
    gate_par = lax.dynamic_slice_in_dim(leaf_gate[:ORDER], row_index * order_rows, order_rows)
    gate_anc = lax.dynamic_slice_in_dim(leaf_gate[ORDER:], row_index * anc_rows, anc_rows)
    leaf_local = jnp.concatenate(
        [
            leaf_lower_par * gate_par[:, None].astype(jnp.bfloat16),
            leaf_lower_anc * gate_anc[:, None].astype(jnp.bfloat16),
        ],
        axis=0,
    )
    leaf_half = lax.dynamic_slice_in_dim(leaf_local, col_index * col_width, col_width, 1)
    columns = anc_inverse
    product = jnp.dot(
        columns,
        lax.all_gather(lower_half, "row", axis=0, tiled=True),
        preferred_element_type=jnp.float32,
    )
    parent_offdiag = (-product).astype(jnp.bfloat16)
    offdiag_rows = lax.all_gather(parent_offdiag, "col", axis=1, tiled=True)
    columns = lower_one
    diag_sums = lax.psum_scatter(
        lax.dot_general(
            columns, offdiag_rows, (((0,), (0,)), ((), ())), preferred_element_type=jnp.float32
        ),
        "row",
        scatter_dimension=0,
        tiled=True,
    )
    parent_block = parent_pivinv - diag_sums
    parent_round = parent_block.astype(jnp.bfloat16)
    mirrored = lax.all_to_all(offdiag_rows, "row", split_axis=1, concat_axis=0, tiled=True).T
    upper_rows = jnp.concatenate(
        [
            parent_round.reshape(order_rows, row_devices, order_rows),
            mirrored.reshape(order_rows, row_devices, anc_rows),
        ],
        axis=2,
    )
    lower_rows = jnp.concatenate(
        [
            offdiag_rows.reshape(anc_rows, row_devices, order_rows),
            anc_inverse.reshape(anc_rows, row_devices, anc_rows),
        ],
        axis=2,
    )
    inverse_rows = jnp.concatenate(
        [upper_rows.reshape(order_rows, -1), lower_rows.reshape(anc_rows, -1)], axis=0
    )
    columns = inverse_rows
    leaf_product = jnp.dot(
        columns,
        lax.all_gather(leaf_half, "row", axis=0, tiled=True),
        preferred_element_type=jnp.float32,
    )
    leaf_result = (-leaf_product).astype(jnp.bfloat16)
    partial_sums = jnp.sum(leaf_half.astype(jnp.float32) * leaf_result.astype(jnp.float32), axis=0)
    density = leaf_pivots - lax.psum(partial_sums, "row")
    return (
        parent_block,
        parent_offdiag,
        leaf_result[:order_rows],
        leaf_result[order_rows:],
        density,
    )


def piece_kernel(anc_hbm, lower_hbm, par_hbm, ancl_hbm, out_ref):
    row, col = lax.axis_index("row"), lax.axis_index("col")
    half = out_ref.shape[0]
    blk = anc_hbm.shape[0]
    blocks = anc_hbm.shape[1] // blk
    sent = blocks // 2 + 1
    rows = pl.ds(pl.multiple_of(col * half, 8), half)
    for k in range(sent):
        start = pl.multiple_of(lax.rem(row + k, blocks) * blk, 128)
        out_ref[:, k * blk : (k + 1) * blk] = anc_hbm[rows, pl.ds(start, blk)]
    at = sent * blk
    for source in (lower_hbm, par_hbm, ancl_hbm):
        width = source.shape[1]
        out_ref[:, at : at + width] = source[rows, :]
        at += width


def leaf_kernel(
    lower_gate, par_gate, anc_gate, pivots, full_hbm, anc_local, pivinv,
    block_ref, offdiag_ref, par_ref, anc_ref, part_ref,
    sent_v, anc_v, lower_v, par_v, ancl_v, rows_v, sem,
):
    row, col = lax.axis_index("row"), lax.axis_index("col")
    anc_all, order_all = anc_v.shape[0], lower_v.shape[1]
    width = par_v.shape[1]
    order_rows, anc_rows = block_ref.shape[0], anc_local.shape[0]
    off_width = offdiag_ref.shape[1]
    sent_width = sent_v.shape[1]
    leaf_at = sent_width + order_all
    leaf_width = (full_hbm.shape[1] - leaf_at) // 2
    copies = [
        pltpu.make_async_copy(full_hbm.at[:, pl.ds(sent_width, order_all)], lower_v, sem.at[1]),
        pltpu.make_async_copy(full_hbm.at[:, pl.ds(0, sent_width)], sent_v, sem.at[0]),
        pltpu.make_async_copy(
            full_hbm.at[:, pl.ds(pl.multiple_of(leaf_at + col * width, 128), width)], par_v, sem.at[2]
        ),
        pltpu.make_async_copy(
            full_hbm.at[:, pl.ds(pl.multiple_of(leaf_at + leaf_width + col * width, 128), width)],
            ancl_v,
            sem.at[3],
        ),
    ]
    for copy in copies:
        copy.start()
    gate_row = lower_gate[...]
    gate_col = gate_row.T
    anc_here = anc_local[...]
    copies[0].wait()
    lower = lower_v[...]
    rows = (-jnp.dot(anc_here * gate_col, lower, preferred_element_type=jnp.float32)).astype(
        jnp.bfloat16
    )
    rows_v[...] = rows
    offdiag_ref[...] = rows_v[:, pl.ds(pl.multiple_of(col * off_width, 128), off_width)]
    copies[1].wait()
    blocks = anc_all // anc_rows
    for p in range(blocks):
        for q in range(blocks):
            k = (q - p) % blocks
            if k * anc_rows < sent_width:
                part = sent_v[p * anc_rows : (p + 1) * anc_rows, k * anc_rows : (k + 1) * anc_rows]
            else:
                k = (p - q) % blocks
                part = sent_v[q * anc_rows : (q + 1) * anc_rows, k * anc_rows : (k + 1) * anc_rows]
                part = part.astype(jnp.float32).T.astype(jnp.bfloat16)
            anc_v[p * anc_rows : (p + 1) * anc_rows, q * anc_rows : (q + 1) * anc_rows] = part
    lower_cols = lower_v[:, pl.ds(pl.multiple_of(row * order_rows, 128), order_rows)] * gate_row
    offdiag_t = (
        -jnp.dot(lower_cols.T, anc_v[...], preferred_element_type=jnp.float32)
    ).astype(jnp.bfloat16)
    block = pivinv[...] - jnp.dot(offdiag_t * gate_col, lower, preferred_element_type=jnp.float32)
    block_ref[...] = block
    copies[2].wait()
    copies[3].wait()
    par_v[...] = par_v[...] * par_gate[...]
    ancl_v[...] = ancl_v[...] * anc_gate[...]
    par, ancl = par_v[...], ancl_v[...]
    upper = jnp.dot(
        block.astype(jnp.bfloat16), par, preferred_element_type=jnp.float32
    ) + jnp.dot(offdiag_t, ancl, preferred_element_type=jnp.float32)
    par_block = (-upper).astype(jnp.bfloat16)
    lower_sum = jnp.dot(rows, par, preferred_element_type=jnp.float32) + jnp.dot(
        anc_local[...], ancl, preferred_element_type=jnp.float32
    )
    anc_block = (-lower_sum).astype(jnp.bfloat16)
    par_ref[...] = par_block
    anc_ref[...] = anc_block
    par_own = par_v[pl.ds(pl.multiple_of(row * order_rows, 8), order_rows), :]
    ancl_own = ancl_v[pl.ds(pl.multiple_of(row * anc_rows, 8), anc_rows), :]
    part = jnp.sum(
        par_own.astype(jnp.float32) * par_block.astype(jnp.float32), axis=0, keepdims=True
    ) + jnp.sum(ancl_own.astype(jnp.float32) * anc_block.astype(jnp.float32), axis=0, keepdims=True)
    part = jnp.where(row == 0, pivots[...] - part, -part)
    for i in range(part_ref.shape[0]):
        part_ref[i] = part


def local_whole(
    anc_inverse,
    parent_pivinv,
    parent_lower,
    parent_mask,
    leaf_lower_par,
    leaf_lower_anc,
    leaf_mask,
    leaf_pivots,
):
    row_index = lax.axis_index("row")
    row_devices = lax.axis_size("row")
    col_index = lax.axis_index("col")
    anc_rows = anc_inverse.shape[0]
    order_rows = parent_pivinv.shape[0]
    col_width = leaf_pivots.shape[0]
    off_width = parent_lower.shape[1] // 2
    half = anc_rows // 2
    anc_all = anc_rows * row_devices
    order_all = order_rows * row_devices

    sent_width = (row_devices // 2 + 1) * anc_rows
    piece_width = sent_width + order_all + 2 * leaf_lower_par.shape[1]
    piece = pl.pallas_call(
        piece_kernel,
        out_shape=jax.ShapeDtypeStruct((half, piece_width), jnp.bfloat16),
        in_specs=[pl.BlockSpec(memory_space=pltpu.VMEM)] * 4,
        out_specs=pl.BlockSpec(memory_space=pltpu.VMEM),
    )(anc_inverse, parent_lower, leaf_lower_par, leaf_lower_anc)
    full = lax.all_gather(piece, ("row", "col"), axis=0, tiled=True)
    parent_gate = jnp.repeat(parent_mask, BLOCK).astype(jnp.bfloat16)[:, None]
    leaf_gate = jnp.repeat(leaf_mask, BLOCK).astype(jnp.bfloat16)[:, None]
    vmem = pl.BlockSpec(memory_space=pltpu.VMEM)
    flops = 2 * (3 * order_rows * anc_all * order_all + 4 * order_rows * anc_all * col_width)
    block, offdiag_own, par_block, anc_block, parts = pl.pallas_call(
        leaf_kernel,
        out_shape=(
            jax.ShapeDtypeStruct((order_rows, order_all), jnp.float32),
            jax.ShapeDtypeStruct((anc_rows, off_width), jnp.bfloat16),
            jax.ShapeDtypeStruct((order_rows, col_width), jnp.bfloat16),
            jax.ShapeDtypeStruct((anc_rows, col_width), jnp.bfloat16),
            jax.ShapeDtypeStruct((row_devices, 1, col_width), jnp.float32),
        ),
        in_specs=[vmem] * 4
        + [pl.BlockSpec(memory_space=pl.ANY)]
        + [vmem] * 2,
        out_specs=(vmem,) * 5,
        scratch_shapes=[
            pltpu.VMEM((anc_all, sent_width), jnp.bfloat16),
            pltpu.VMEM((anc_all, anc_all), jnp.bfloat16),
            pltpu.VMEM((anc_all, order_all), jnp.bfloat16),
            pltpu.VMEM((order_all, col_width), jnp.bfloat16),
            pltpu.VMEM((anc_all, col_width), jnp.bfloat16),
            pltpu.VMEM((anc_rows, order_all), jnp.bfloat16),
            pltpu.SemaphoreType.DMA((4,)),
        ],
        cost_estimate=pl.CostEstimate(
            flops=flops, transcendentals=0, bytes_accessed=full.size + 8 * anc_rows * order_all
        ),
    )(
        parent_gate,
        leaf_gate[:order_all],
        leaf_gate[order_all:],
        leaf_pivots[None, :],
        full,
        anc_inverse,
        parent_pivinv,
    )
    density = jnp.sum(lax.all_to_all(parts, "row", 0, 0, tiled=True), axis=0)[0]
    return block, offdiag_own, par_block, anc_block, density


def fits_whole(mesh, anc_rows, order_rows):
    anc_all = anc_rows * mesh.shape["row"]
    return (
        anc_rows == order_rows
        and anc_rows % 128 == 0
        and anc_all * anc_all * 2 <= 16 * 1024 * 1024
    )


def solution(mesh):
    placed = (
        P(("pole", "row"), None),
        P(("pole", "row"), None),
        P(("pole", "row"), None),
        P(),
        P(("pole", "row"), None),
        P(("pole", "row"), None),
        P(),
        P(("pole", "col")),
    )
    placed_out = (
        P(("pole", "row"), None),
        P(("pole", "row"), "col"),
        P(("pole", "row"), "col"),
        P(("pole", "row"), "col"),
        P(("pole", "col")),
    )
    shards = mesh.shape["pole"] * mesh.shape["row"]

    def run(*args):
        anc_rows = args[0].shape[0] // shards
        order_rows = args[1].shape[0] // shards
        body = local_whole if fits_whole(mesh, anc_rows, order_rows) else local
        return jax.shard_map(
            body, mesh=mesh, in_specs=placed, out_specs=placed_out, check_vma=False
        )(*args)

    return run
```

```python
import jax
import jax.numpy as jnp
from jax import lax
from jax.experimental import pallas as pl
from jax.experimental.pallas import tpu as pltpu
from jax.sharding import PartitionSpec as P

BLOCK = 256
ORDER = 1024


def local(
    anc_inverse,
    parent_pivinv,
    parent_lower,
    parent_mask,
    leaf_lower_par,
    leaf_lower_anc,
    leaf_mask,
    leaf_pivots,
):
    row_index = lax.axis_index("row")
    row_devices = lax.axis_size("row")
    col_index = lax.axis_index("col")
    anc_rows = anc_inverse.shape[0]
    order_rows = parent_pivinv.shape[0]
    col_width = leaf_pivots.shape[0]
    parent_gate = lax.dynamic_slice_in_dim(
        jnp.repeat(parent_mask, BLOCK), row_index * anc_rows, anc_rows
    )
    lower_one = parent_lower * parent_gate[:, None].astype(jnp.bfloat16)
    lower_half = lax.dynamic_slice_in_dim(lower_one, col_index * col_width, col_width, 1)
    leaf_gate = jnp.repeat(leaf_mask, BLOCK)
    gate_par = lax.dynamic_slice_in_dim(leaf_gate[:ORDER], row_index * order_rows, order_rows)
    gate_anc = lax.dynamic_slice_in_dim(leaf_gate[ORDER:], row_index * anc_rows, anc_rows)
    leaf_local = jnp.concatenate(
        [
            leaf_lower_par * gate_par[:, None].astype(jnp.bfloat16),
            leaf_lower_anc * gate_anc[:, None].astype(jnp.bfloat16),
        ],
        axis=0,
    )
    leaf_half = lax.dynamic_slice_in_dim(leaf_local, col_index * col_width, col_width, 1)
    columns = anc_inverse
    product = jnp.dot(
        columns,
        lax.all_gather(lower_half, "row", axis=0, tiled=True),
        preferred_element_type=jnp.float32,
    )
    parent_offdiag = (-product).astype(jnp.bfloat16)
    offdiag_rows = lax.all_gather(parent_offdiag, "col", axis=1, tiled=True)
    columns = lower_one
    diag_sums = lax.psum_scatter(
        lax.dot_general(
            columns, offdiag_rows, (((0,), (0,)), ((), ())), preferred_element_type=jnp.float32
        ),
        "row",
        scatter_dimension=0,
        tiled=True,
    )
    parent_block = parent_pivinv - diag_sums
    parent_round = parent_block.astype(jnp.bfloat16)
    mirrored = lax.all_to_all(offdiag_rows, "row", split_axis=1, concat_axis=0, tiled=True).T
    upper_rows = jnp.concatenate(
        [
            parent_round.reshape(order_rows, row_devices, order_rows),
            mirrored.reshape(order_rows, row_devices, anc_rows),
        ],
        axis=2,
    )
    lower_rows = jnp.concatenate(
        [
            offdiag_rows.reshape(anc_rows, row_devices, order_rows),
            anc_inverse.reshape(anc_rows, row_devices, anc_rows),
        ],
        axis=2,
    )
    inverse_rows = jnp.concatenate(
        [upper_rows.reshape(order_rows, -1), lower_rows.reshape(anc_rows, -1)], axis=0
    )
    columns = inverse_rows
    leaf_product = jnp.dot(
        columns,
        lax.all_gather(leaf_half, "row", axis=0, tiled=True),
        preferred_element_type=jnp.float32,
    )
    leaf_result = (-leaf_product).astype(jnp.bfloat16)
    partial_sums = jnp.sum(leaf_half.astype(jnp.float32) * leaf_result.astype(jnp.float32), axis=0)
    density = leaf_pivots - lax.psum(partial_sums, "row")
    return (
        parent_block,
        parent_offdiag,
        leaf_result[:order_rows],
        leaf_result[order_rows:],
        density,
    )


def piece_kernel(anc_hbm, lower_hbm, par_hbm, ancl_hbm, out_ref):
    row, col = lax.axis_index("row"), lax.axis_index("col")
    half = out_ref.shape[0]
    blk = anc_hbm.shape[0]
    blocks = anc_hbm.shape[1] // blk
    sent = blocks // 2 + 1
    rows = pl.ds(pl.multiple_of(col * half, 8), half)
    for k in range(sent):
        start = pl.multiple_of(lax.rem(row + k, blocks) * blk, 128)
        out_ref[:, k * blk : (k + 1) * blk] = anc_hbm[rows, pl.ds(start, blk)]
    at = sent * blk
    for source in (lower_hbm, par_hbm, ancl_hbm):
        width = source.shape[1]
        out_ref[:, at : at + width] = source[rows, :]
        at += width


def leaf_kernel(
    lower_gate, par_gate, anc_gate, pivots, full_hbm, anc_local, pivinv,
    block_ref, offdiag_ref, par_ref, anc_ref, part_ref,
    sent_v, anc_v, lower_v, par_v, ancl_v, rows_v, sem,
):
    row, col = lax.axis_index("row"), lax.axis_index("col")
    anc_all, order_all = anc_v.shape[0], lower_v.shape[1]
    width = par_v.shape[1]
    order_rows, anc_rows = block_ref.shape[0], anc_local.shape[0]
    off_width = offdiag_ref.shape[1]
    sent_width = sent_v.shape[1]
    leaf_at = sent_width + order_all
    leaf_width = (full_hbm.shape[1] - leaf_at) // 2
    copies = [
        pltpu.make_async_copy(full_hbm.at[:, pl.ds(sent_width, order_all)], lower_v, sem.at[1]),
        pltpu.make_async_copy(full_hbm.at[:, pl.ds(0, sent_width)], sent_v, sem.at[0]),
        pltpu.make_async_copy(
            full_hbm.at[:, pl.ds(pl.multiple_of(leaf_at + col * width, 128), width)], par_v, sem.at[2]
        ),
        pltpu.make_async_copy(
            full_hbm.at[:, pl.ds(pl.multiple_of(leaf_at + leaf_width + col * width, 128), width)],
            ancl_v,
            sem.at[3],
        ),
    ]
    copies[0].start()
    copies[1].start()
    gate_row = lower_gate[...]
    gate_col = gate_row.T
    anc_here = anc_local[...]
    copies[0].wait()
    copies[2].start()
    copies[3].start()
    lower = lower_v[...]
    rows = (-jnp.dot(anc_here * gate_col, lower, preferred_element_type=jnp.float32)).astype(
        jnp.bfloat16
    )
    rows_v[...] = rows
    offdiag_ref[...] = rows_v[:, pl.ds(pl.multiple_of(col * off_width, 128), off_width)]
    copies[1].wait()
    blocks = anc_all // anc_rows
    sent = sent_width // anc_rows
    for p in range(blocks):
        rows_p = slice(p * anc_rows, (p + 1) * anc_rows)
        first = min(sent, blocks - p)
        anc_v[rows_p, p * anc_rows : (p + first) * anc_rows] = sent_v[rows_p, : first * anc_rows]
        if first < sent:
            anc_v[rows_p, : (sent - first) * anc_rows] = sent_v[rows_p, first * anc_rows : sent_width]
        for q in range(blocks):
            k = (q - p) % blocks
            if k >= sent:
                k = (p - q) % blocks
                part = sent_v[q * anc_rows : (q + 1) * anc_rows, k * anc_rows : (k + 1) * anc_rows]
                anc_v[rows_p, q * anc_rows : (q + 1) * anc_rows] = (
                    part.astype(jnp.float32).T.astype(jnp.bfloat16)
                )
    lower_cols = lower_v[:, pl.ds(pl.multiple_of(row * order_rows, 128), order_rows)] * gate_row
    offdiag_t = (
        -jnp.dot(lower_cols.T, anc_v[...], preferred_element_type=jnp.float32)
    ).astype(jnp.bfloat16)
    block = pivinv[...] - jnp.dot(offdiag_t * gate_col, lower, preferred_element_type=jnp.float32)
    block_ref[...] = block
    copies[2].wait()
    copies[3].wait()
    par_v[...] = par_v[...] * par_gate[...]
    ancl_v[...] = ancl_v[...] * anc_gate[...]
    par, ancl = par_v[...], ancl_v[...]
    upper = jnp.dot(
        block.astype(jnp.bfloat16), par, preferred_element_type=jnp.float32
    ) + jnp.dot(offdiag_t, ancl, preferred_element_type=jnp.float32)
    par_block = (-upper).astype(jnp.bfloat16)
    lower_sum = jnp.dot(rows, par, preferred_element_type=jnp.float32) + jnp.dot(
        anc_local[...], ancl, preferred_element_type=jnp.float32
    )
    anc_block = (-lower_sum).astype(jnp.bfloat16)
    par_ref[...] = par_block
    anc_ref[...] = anc_block
    par_own = par_v[pl.ds(pl.multiple_of(row * order_rows, 8), order_rows), :]
    ancl_own = ancl_v[pl.ds(pl.multiple_of(row * anc_rows, 8), anc_rows), :]
    part = jnp.sum(
        par_own.astype(jnp.float32) * par_block.astype(jnp.float32), axis=0, keepdims=True
    ) + jnp.sum(ancl_own.astype(jnp.float32) * anc_block.astype(jnp.float32), axis=0, keepdims=True)
    part = jnp.where(row == 0, pivots[...] - part, -part)
    for i in range(part_ref.shape[0]):
        part_ref[i] = part


def local_whole(
    anc_inverse,
    parent_pivinv,
    parent_lower,
    parent_mask,
    leaf_lower_par,
    leaf_lower_anc,
    leaf_mask,
    leaf_pivots,
):
    row_index = lax.axis_index("row")
    row_devices = lax.axis_size("row")
    col_index = lax.axis_index("col")
    anc_rows = anc_inverse.shape[0]
    order_rows = parent_pivinv.shape[0]
    col_width = leaf_pivots.shape[0]
    off_width = parent_lower.shape[1] // 2
    half = anc_rows // 2
    anc_all = anc_rows * row_devices
    order_all = order_rows * row_devices

    sent_width = (row_devices // 2 + 1) * anc_rows
    piece_width = sent_width + order_all + 2 * leaf_lower_par.shape[1]
    piece = pl.pallas_call(
        piece_kernel,
        out_shape=jax.ShapeDtypeStruct((half, piece_width), jnp.bfloat16),
        in_specs=[pl.BlockSpec(memory_space=pltpu.VMEM)] * 4,
        out_specs=pl.BlockSpec(memory_space=pltpu.VMEM),
    )(anc_inverse, parent_lower, leaf_lower_par, leaf_lower_anc)
    full = lax.all_gather(piece, ("row", "col"), axis=0, tiled=True)
    parent_gate = jnp.repeat(parent_mask, BLOCK).astype(jnp.bfloat16)[:, None]
    leaf_gate = jnp.repeat(leaf_mask, BLOCK).astype(jnp.bfloat16)[:, None]
    vmem = pl.BlockSpec(memory_space=pltpu.VMEM)
    flops = 2 * (3 * order_rows * anc_all * order_all + 4 * order_rows * anc_all * col_width)
    block, offdiag_own, par_block, anc_block, parts = pl.pallas_call(
        leaf_kernel,
        out_shape=(
            jax.ShapeDtypeStruct((order_rows, order_all), jnp.float32),
            jax.ShapeDtypeStruct((anc_rows, off_width), jnp.bfloat16),
            jax.ShapeDtypeStruct((order_rows, col_width), jnp.bfloat16),
            jax.ShapeDtypeStruct((anc_rows, col_width), jnp.bfloat16),
            jax.ShapeDtypeStruct((row_devices, 1, col_width), jnp.float32),
        ),
        in_specs=[vmem] * 4
        + [pl.BlockSpec(memory_space=pl.ANY)]
        + [vmem] * 2,
        out_specs=(vmem,) * 5,
        scratch_shapes=[
            pltpu.VMEM((anc_all, sent_width), jnp.bfloat16),
            pltpu.VMEM((anc_all, anc_all), jnp.bfloat16),
            pltpu.VMEM((anc_all, order_all), jnp.bfloat16),
            pltpu.VMEM((order_all, col_width), jnp.bfloat16),
            pltpu.VMEM((anc_all, col_width), jnp.bfloat16),
            pltpu.VMEM((anc_rows, order_all), jnp.bfloat16),
            pltpu.SemaphoreType.DMA((4,)),
        ],
        cost_estimate=pl.CostEstimate(
            flops=flops, transcendentals=0, bytes_accessed=full.size + 8 * anc_rows * order_all
        ),
    )(
        parent_gate,
        leaf_gate[:order_all],
        leaf_gate[order_all:],
        leaf_pivots[None, :],
        full,
        anc_inverse,
        parent_pivinv,
    )
    density = jnp.sum(lax.all_to_all(parts, "row", 0, 0, tiled=True), axis=0)[0]
    return block, offdiag_own, par_block, anc_block, density


def fits_whole(mesh, anc_rows, order_rows):
    anc_all = anc_rows * mesh.shape["row"]
    return (
        anc_rows == order_rows
        and anc_rows % 128 == 0
        and anc_all * anc_all * 2 <= 16 * 1024 * 1024
    )


def solution(mesh):
    placed = (
        P(("pole", "row"), None),
        P(("pole", "row"), None),
        P(("pole", "row"), None),
        P(),
        P(("pole", "row"), None),
        P(("pole", "row"), None),
        P(),
        P(("pole", "col")),
    )
    placed_out = (
        P(("pole", "row"), None),
        P(("pole", "row"), "col"),
        P(("pole", "row"), "col"),
        P(("pole", "row"), "col"),
        P(("pole", "col")),
    )
    shards = mesh.shape["pole"] * mesh.shape["row"]

    def run(*args):
        anc_rows = args[0].shape[0] // shards
        order_rows = args[1].shape[0] // shards
        body = local_whole if fits_whole(mesh, anc_rows, order_rows) else local
        return jax.shard_map(
            body, mesh=mesh, in_specs=placed, out_specs=placed_out, check_vma=False
        )(*args)

    return run
```

```python
import jax
import jax.numpy as jnp
from jax import lax
from jax.experimental import pallas as pl
from jax.experimental.pallas import tpu as pltpu
from jax.sharding import PartitionSpec as P

BLOCK = 256
ORDER = 1024


def local(
    anc_inverse,
    parent_pivinv,
    parent_lower,
    parent_mask,
    leaf_lower_par,
    leaf_lower_anc,
    leaf_mask,
    leaf_pivots,
):
    row_index = lax.axis_index("row")
    row_devices = lax.axis_size("row")
    col_index = lax.axis_index("col")
    anc_rows = anc_inverse.shape[0]
    order_rows = parent_pivinv.shape[0]
    col_width = leaf_pivots.shape[0]
    parent_gate = lax.dynamic_slice_in_dim(
        jnp.repeat(parent_mask, BLOCK), row_index * anc_rows, anc_rows
    )
    lower_one = parent_lower * parent_gate[:, None].astype(jnp.bfloat16)
    lower_half = lax.dynamic_slice_in_dim(lower_one, col_index * col_width, col_width, 1)
    leaf_gate = jnp.repeat(leaf_mask, BLOCK)
    gate_par = lax.dynamic_slice_in_dim(leaf_gate[:ORDER], row_index * order_rows, order_rows)
    gate_anc = lax.dynamic_slice_in_dim(leaf_gate[ORDER:], row_index * anc_rows, anc_rows)
    leaf_local = jnp.concatenate(
        [
            leaf_lower_par * gate_par[:, None].astype(jnp.bfloat16),
            leaf_lower_anc * gate_anc[:, None].astype(jnp.bfloat16),
        ],
        axis=0,
    )
    leaf_half = lax.dynamic_slice_in_dim(leaf_local, col_index * col_width, col_width, 1)
    columns = anc_inverse
    product = jnp.dot(
        columns,
        lax.all_gather(lower_half, "row", axis=0, tiled=True),
        preferred_element_type=jnp.float32,
    )
    parent_offdiag = (-product).astype(jnp.bfloat16)
    offdiag_rows = lax.all_gather(parent_offdiag, "col", axis=1, tiled=True)
    columns = lower_one
    diag_sums = lax.psum_scatter(
        lax.dot_general(
            columns, offdiag_rows, (((0,), (0,)), ((), ())), preferred_element_type=jnp.float32
        ),
        "row",
        scatter_dimension=0,
        tiled=True,
    )
    parent_block = parent_pivinv - diag_sums
    parent_round = parent_block.astype(jnp.bfloat16)
    mirrored = lax.all_to_all(offdiag_rows, "row", split_axis=1, concat_axis=0, tiled=True).T
    upper_rows = jnp.concatenate(
        [
            parent_round.reshape(order_rows, row_devices, order_rows),
            mirrored.reshape(order_rows, row_devices, anc_rows),
        ],
        axis=2,
    )
    lower_rows = jnp.concatenate(
        [
            offdiag_rows.reshape(anc_rows, row_devices, order_rows),
            anc_inverse.reshape(anc_rows, row_devices, anc_rows),
        ],
        axis=2,
    )
    inverse_rows = jnp.concatenate(
        [upper_rows.reshape(order_rows, -1), lower_rows.reshape(anc_rows, -1)], axis=0
    )
    columns = inverse_rows
    leaf_product = jnp.dot(
        columns,
        lax.all_gather(leaf_half, "row", axis=0, tiled=True),
        preferred_element_type=jnp.float32,
    )
    leaf_result = (-leaf_product).astype(jnp.bfloat16)
    partial_sums = jnp.sum(leaf_half.astype(jnp.float32) * leaf_result.astype(jnp.float32), axis=0)
    density = leaf_pivots - lax.psum(partial_sums, "row")
    return (
        parent_block,
        parent_offdiag,
        leaf_result[:order_rows],
        leaf_result[order_rows:],
        density,
    )


def piece_kernel(anc_hbm, lower_hbm, par_hbm, ancl_hbm, out_ref):
    row, col = lax.axis_index("row"), lax.axis_index("col")
    half = out_ref.shape[0]
    blk = anc_hbm.shape[0]
    blocks = anc_hbm.shape[1] // blk
    sent = blocks // 2 + 1
    rows = pl.ds(pl.multiple_of(col * half, 8), half)
    for k in range(sent):
        start = pl.multiple_of(lax.rem(row + k, blocks) * blk, 128)
        out_ref[:, k * blk : (k + 1) * blk] = anc_hbm[rows, pl.ds(start, blk)]
    at = sent * blk
    for source in (lower_hbm, par_hbm, ancl_hbm):
        width = source.shape[1]
        out_ref[:, at : at + width] = source[rows, :]
        at += width


def leaf_kernel(
    lower_gate, par_gate, anc_gate, pivots, full_hbm, anc_local, pivinv,
    block_ref, offdiag_ref, par_ref, anc_ref, part_ref,
    sent_v, anc_v, lower_v, par_v, ancl_v, rows_v, sem,
):
    row, col = lax.axis_index("row"), lax.axis_index("col")
    anc_all, order_all = anc_v.shape[0], lower_v.shape[1]
    width = par_v.shape[1]
    order_rows, anc_rows = block_ref.shape[0], anc_local.shape[0]
    off_width = offdiag_ref.shape[1]
    sent_width = sent_v.shape[1]
    leaf_at = sent_width + order_all
    leaf_width = (full_hbm.shape[1] - leaf_at) // 2
    lower_v[...] = full_hbm[:, sent_width : sent_width + order_all]
    gate_row = lower_gate[...]
    gate_col = gate_row.T
    anc_here = anc_local[...]
    lower = lower_v[...]
    rows = (-jnp.dot(anc_here * gate_col, lower, preferred_element_type=jnp.float32)).astype(
        jnp.bfloat16
    )
    rows_v[...] = rows
    offdiag_ref[...] = rows_v[:, pl.ds(pl.multiple_of(col * off_width, 128), off_width)]
    sent_v[...] = full_hbm[:, :sent_width]
    blocks = anc_all // anc_rows
    sent = sent_width // anc_rows
    for p in range(blocks):
        rows_p = slice(p * anc_rows, (p + 1) * anc_rows)
        first = min(sent, blocks - p)
        anc_v[rows_p, p * anc_rows : (p + first) * anc_rows] = sent_v[rows_p, : first * anc_rows]
        if first < sent:
            anc_v[rows_p, : (sent - first) * anc_rows] = sent_v[rows_p, first * anc_rows : sent_width]
        for q in range(blocks):
            k = (q - p) % blocks
            if k >= sent:
                k = (p - q) % blocks
                part = sent_v[q * anc_rows : (q + 1) * anc_rows, k * anc_rows : (k + 1) * anc_rows]
                anc_v[rows_p, q * anc_rows : (q + 1) * anc_rows] = (
                    part.astype(jnp.float32).T.astype(jnp.bfloat16)
                )
    lower_cols = lower_v[:, pl.ds(pl.multiple_of(row * order_rows, 128), order_rows)] * gate_row
    offdiag_t = (
        -jnp.dot(lower_cols.T, anc_v[...], preferred_element_type=jnp.float32)
    ).astype(jnp.bfloat16)
    block = pivinv[...] - jnp.dot(offdiag_t * gate_col, lower, preferred_element_type=jnp.float32)
    block_ref[...] = block
    par_v[...] = full_hbm[:, pl.ds(pl.multiple_of(leaf_at + col * width, 128), width)] * par_gate[...]
    ancl_v[...] = (
        full_hbm[:, pl.ds(pl.multiple_of(leaf_at + leaf_width + col * width, 128), width)]
        * anc_gate[...]
    )
    par, ancl = par_v[...], ancl_v[...]
    upper = jnp.dot(
        block.astype(jnp.bfloat16), par, preferred_element_type=jnp.float32
    ) + jnp.dot(offdiag_t, ancl, preferred_element_type=jnp.float32)
    par_block = (-upper).astype(jnp.bfloat16)
    lower_sum = jnp.dot(rows, par, preferred_element_type=jnp.float32) + jnp.dot(
        anc_local[...], ancl, preferred_element_type=jnp.float32
    )
    anc_block = (-lower_sum).astype(jnp.bfloat16)
    par_ref[...] = par_block
    anc_ref[...] = anc_block
    par_own = par_v[pl.ds(pl.multiple_of(row * order_rows, 8), order_rows), :]
    ancl_own = ancl_v[pl.ds(pl.multiple_of(row * anc_rows, 8), anc_rows), :]
    part = jnp.sum(
        par_own.astype(jnp.float32) * par_block.astype(jnp.float32), axis=0, keepdims=True
    ) + jnp.sum(ancl_own.astype(jnp.float32) * anc_block.astype(jnp.float32), axis=0, keepdims=True)
    part = jnp.where(row == 0, pivots[...] - part, -part)
    for i in range(part_ref.shape[0]):
        part_ref[i] = part


def local_whole(
    anc_inverse,
    parent_pivinv,
    parent_lower,
    parent_mask,
    leaf_lower_par,
    leaf_lower_anc,
    leaf_mask,
    leaf_pivots,
):
    row_index = lax.axis_index("row")
    row_devices = lax.axis_size("row")
    col_index = lax.axis_index("col")
    anc_rows = anc_inverse.shape[0]
    order_rows = parent_pivinv.shape[0]
    col_width = leaf_pivots.shape[0]
    off_width = parent_lower.shape[1] // 2
    half = anc_rows // 2
    anc_all = anc_rows * row_devices
    order_all = order_rows * row_devices

    sent_width = (row_devices // 2 + 1) * anc_rows
    piece_width = sent_width + order_all + 2 * leaf_lower_par.shape[1]
    piece = pl.pallas_call(
        piece_kernel,
        out_shape=jax.ShapeDtypeStruct((half, piece_width), jnp.bfloat16),
        in_specs=[pl.BlockSpec(memory_space=pltpu.VMEM)] * 4,
        out_specs=pl.BlockSpec(memory_space=pltpu.VMEM),
    )(anc_inverse, parent_lower, leaf_lower_par, leaf_lower_anc)
    full = lax.all_gather(piece, ("row", "col"), axis=0, tiled=True)
    parent_gate = jnp.repeat(parent_mask, BLOCK).astype(jnp.bfloat16)[:, None]
    leaf_gate = jnp.repeat(leaf_mask, BLOCK).astype(jnp.bfloat16)[:, None]
    vmem = pl.BlockSpec(memory_space=pltpu.VMEM)
    flops = 2 * (3 * order_rows * anc_all * order_all + 4 * order_rows * anc_all * col_width)
    block, offdiag_own, par_block, anc_block, parts = pl.pallas_call(
        leaf_kernel,
        out_shape=(
            jax.ShapeDtypeStruct((order_rows, order_all), jnp.float32),
            jax.ShapeDtypeStruct((anc_rows, off_width), jnp.bfloat16),
            jax.ShapeDtypeStruct((order_rows, col_width), jnp.bfloat16),
            jax.ShapeDtypeStruct((anc_rows, col_width), jnp.bfloat16),
            jax.ShapeDtypeStruct((row_devices, 1, col_width), jnp.float32),
        ),
        in_specs=[vmem] * 7,
        out_specs=(vmem,) * 5,
        scratch_shapes=[
            pltpu.VMEM((anc_all, sent_width), jnp.bfloat16),
            pltpu.VMEM((anc_all, anc_all), jnp.bfloat16),
            pltpu.VMEM((anc_all, order_all), jnp.bfloat16),
            pltpu.VMEM((order_all, col_width), jnp.bfloat16),
            pltpu.VMEM((anc_all, col_width), jnp.bfloat16),
            pltpu.VMEM((anc_rows, order_all), jnp.bfloat16),
            pltpu.SemaphoreType.DMA((4,)),
        ],
        cost_estimate=pl.CostEstimate(
            flops=flops, transcendentals=0, bytes_accessed=full.size + 8 * anc_rows * order_all
        ),
    )(
        parent_gate,
        leaf_gate[:order_all],
        leaf_gate[order_all:],
        leaf_pivots[None, :],
        full,
        anc_inverse,
        parent_pivinv,
    )
    density = jnp.sum(lax.all_to_all(parts, "row", 0, 0, tiled=True), axis=0)[0]
    return block, offdiag_own, par_block, anc_block, density


def fits_whole(mesh, anc_rows, order_rows):
    anc_all = anc_rows * mesh.shape["row"]
    return (
        anc_rows == order_rows
        and anc_rows % 128 == 0
        and anc_all * anc_all * 2 <= 16 * 1024 * 1024
    )


def solution(mesh):
    placed = (
        P(("pole", "row"), None),
        P(("pole", "row"), None),
        P(("pole", "row"), None),
        P(),
        P(("pole", "row"), None),
        P(("pole", "row"), None),
        P(),
        P(("pole", "col")),
    )
    placed_out = (
        P(("pole", "row"), None),
        P(("pole", "row"), "col"),
        P(("pole", "row"), "col"),
        P(("pole", "row"), "col"),
        P(("pole", "col")),
    )
    shards = mesh.shape["pole"] * mesh.shape["row"]

    def run(*args):
        anc_rows = args[0].shape[0] // shards
        order_rows = args[1].shape[0] // shards
        body = local_whole if fits_whole(mesh, anc_rows, order_rows) else local
        return jax.shard_map(
            body, mesh=mesh, in_specs=placed, out_specs=placed_out, check_vma=False
        )(*args)

    return run
```

```python
import jax
import jax.numpy as jnp
from jax import lax
from jax.experimental import pallas as pl
from jax.experimental.pallas import tpu as pltpu
from jax.sharding import PartitionSpec as P

BLOCK = 256
ORDER = 1024


def local(
    anc_inverse,
    parent_pivinv,
    parent_lower,
    parent_mask,
    leaf_lower_par,
    leaf_lower_anc,
    leaf_mask,
    leaf_pivots,
):
    row_index = lax.axis_index("row")
    row_devices = lax.axis_size("row")
    col_index = lax.axis_index("col")
    anc_rows = anc_inverse.shape[0]
    order_rows = parent_pivinv.shape[0]
    col_width = leaf_pivots.shape[0]
    parent_gate = lax.dynamic_slice_in_dim(
        jnp.repeat(parent_mask, BLOCK), row_index * anc_rows, anc_rows
    )
    lower_one = parent_lower * parent_gate[:, None].astype(jnp.bfloat16)
    lower_half = lax.dynamic_slice_in_dim(lower_one, col_index * col_width, col_width, 1)
    leaf_gate = jnp.repeat(leaf_mask, BLOCK)
    gate_par = lax.dynamic_slice_in_dim(leaf_gate[:ORDER], row_index * order_rows, order_rows)
    gate_anc = lax.dynamic_slice_in_dim(leaf_gate[ORDER:], row_index * anc_rows, anc_rows)
    leaf_local = jnp.concatenate(
        [
            leaf_lower_par * gate_par[:, None].astype(jnp.bfloat16),
            leaf_lower_anc * gate_anc[:, None].astype(jnp.bfloat16),
        ],
        axis=0,
    )
    leaf_half = lax.dynamic_slice_in_dim(leaf_local, col_index * col_width, col_width, 1)
    columns = anc_inverse
    product = jnp.dot(
        columns,
        lax.all_gather(lower_half, "row", axis=0, tiled=True),
        preferred_element_type=jnp.float32,
    )
    parent_offdiag = (-product).astype(jnp.bfloat16)
    offdiag_rows = lax.all_gather(parent_offdiag, "col", axis=1, tiled=True)
    columns = lower_one
    diag_sums = lax.psum_scatter(
        lax.dot_general(
            columns, offdiag_rows, (((0,), (0,)), ((), ())), preferred_element_type=jnp.float32
        ),
        "row",
        scatter_dimension=0,
        tiled=True,
    )
    parent_block = parent_pivinv - diag_sums
    parent_round = parent_block.astype(jnp.bfloat16)
    mirrored = lax.all_to_all(offdiag_rows, "row", split_axis=1, concat_axis=0, tiled=True).T
    upper_rows = jnp.concatenate(
        [
            parent_round.reshape(order_rows, row_devices, order_rows),
            mirrored.reshape(order_rows, row_devices, anc_rows),
        ],
        axis=2,
    )
    lower_rows = jnp.concatenate(
        [
            offdiag_rows.reshape(anc_rows, row_devices, order_rows),
            anc_inverse.reshape(anc_rows, row_devices, anc_rows),
        ],
        axis=2,
    )
    inverse_rows = jnp.concatenate(
        [upper_rows.reshape(order_rows, -1), lower_rows.reshape(anc_rows, -1)], axis=0
    )
    columns = inverse_rows
    leaf_product = jnp.dot(
        columns,
        lax.all_gather(leaf_half, "row", axis=0, tiled=True),
        preferred_element_type=jnp.float32,
    )
    leaf_result = (-leaf_product).astype(jnp.bfloat16)
    partial_sums = jnp.sum(leaf_half.astype(jnp.float32) * leaf_result.astype(jnp.float32), axis=0)
    density = leaf_pivots - lax.psum(partial_sums, "row")
    return (
        parent_block,
        parent_offdiag,
        leaf_result[:order_rows],
        leaf_result[order_rows:],
        density,
    )


def piece_kernel(anc_hbm, lower_hbm, par_hbm, ancl_hbm, out_ref):
    row, col = lax.axis_index("row"), lax.axis_index("col")
    half = out_ref.shape[0]
    blk = anc_hbm.shape[0]
    blocks = anc_hbm.shape[1] // blk
    sent = blocks // 2 + 1
    rows = pl.ds(pl.multiple_of(col * half, 8), half)
    for k in range(sent):
        start = pl.multiple_of(lax.rem(row + k, blocks) * blk, 128)
        out_ref[:, k * blk : (k + 1) * blk] = anc_hbm[rows, pl.ds(start, blk)]
    at = sent * blk
    for source in (lower_hbm, par_hbm, ancl_hbm):
        width = source.shape[1]
        out_ref[:, at : at + width] = source[rows, :]
        at += width


def leaf_kernel(
    lower_gate, par_gate, anc_gate, pivots, full_hbm, anc_local, pivinv,
    block_ref, offdiag_ref, par_ref, anc_ref, part_ref,
    sent_v, anc_v, lower_v, par_v, ancl_v, rows_v, sem,
):
    row, col = lax.axis_index("row"), lax.axis_index("col")
    anc_all, order_all = anc_v.shape[0], lower_v.shape[1]
    width = par_v.shape[1]
    order_rows, anc_rows = block_ref.shape[0], anc_local.shape[0]
    off_width = offdiag_ref.shape[1]
    sent_width = sent_v.shape[1]
    leaf_at = sent_width + order_all
    leaf_width = (full_hbm.shape[1] - leaf_at) // 2
    chunks = 4
    step = anc_all // chunks
    windows = [
        (pl.ds(sent_width, order_all), lower_v),
        (pl.ds(0, sent_width), sent_v),
        (pl.ds(pl.multiple_of(leaf_at + col * width, 128), width), par_v),
        (pl.ds(pl.multiple_of(leaf_at + leaf_width + col * width, 128), width), ancl_v),
    ]
    copies = [
        [
            pltpu.make_async_copy(
                full_hbm.at[pl.ds(i * step, step), cols],
                target.at[pl.ds(i * step, step), :],
                sem.at[j * chunks + i],
            )
            for i in range(chunks)
        ]
        for j, (cols, target) in enumerate(windows)
    ]
    for copy in copies[0] + copies[1]:
        copy.start()
    gate_row = lower_gate[...]
    gate_col = gate_row.T
    anc_here = anc_local[...]
    for copy in copies[0]:
        copy.wait()
    for copy in copies[2] + copies[3]:
        copy.start()
    lower = lower_v[...]
    rows = (-jnp.dot(anc_here * gate_col, lower, preferred_element_type=jnp.float32)).astype(
        jnp.bfloat16
    )
    rows_v[...] = rows
    offdiag_ref[...] = rows_v[:, pl.ds(pl.multiple_of(col * off_width, 128), off_width)]
    for copy in copies[1]:
        copy.wait()
    blocks = anc_all // anc_rows
    sent = sent_width // anc_rows
    for p in range(blocks):
        rows_p = slice(p * anc_rows, (p + 1) * anc_rows)
        first = min(sent, blocks - p)
        anc_v[rows_p, p * anc_rows : (p + first) * anc_rows] = sent_v[rows_p, : first * anc_rows]
        if first < sent:
            anc_v[rows_p, : (sent - first) * anc_rows] = sent_v[rows_p, first * anc_rows : sent_width]
        for q in range(blocks):
            k = (q - p) % blocks
            if k >= sent:
                k = (p - q) % blocks
                part = sent_v[q * anc_rows : (q + 1) * anc_rows, k * anc_rows : (k + 1) * anc_rows]
                anc_v[rows_p, q * anc_rows : (q + 1) * anc_rows] = (
                    part.astype(jnp.float32).T.astype(jnp.bfloat16)
                )
    lower_cols = lower_v[:, pl.ds(pl.multiple_of(row * order_rows, 128), order_rows)] * gate_row
    offdiag_t = (
        -jnp.dot(lower_cols.T, anc_v[...], preferred_element_type=jnp.float32)
    ).astype(jnp.bfloat16)
    block = pivinv[...] - jnp.dot(offdiag_t * gate_col, lower, preferred_element_type=jnp.float32)
    block_ref[...] = block
    for copy in copies[2] + copies[3]:
        copy.wait()
    par_v[...] = par_v[...] * par_gate[...]
    ancl_v[...] = ancl_v[...] * anc_gate[...]
    par, ancl = par_v[...], ancl_v[...]
    upper = jnp.dot(
        block.astype(jnp.bfloat16), par, preferred_element_type=jnp.float32
    ) + jnp.dot(offdiag_t, ancl, preferred_element_type=jnp.float32)
    par_block = (-upper).astype(jnp.bfloat16)
    lower_sum = jnp.dot(rows, par, preferred_element_type=jnp.float32) + jnp.dot(
        anc_local[...], ancl, preferred_element_type=jnp.float32
    )
    anc_block = (-lower_sum).astype(jnp.bfloat16)
    par_ref[...] = par_block
    anc_ref[...] = anc_block
    par_own = par_v[pl.ds(pl.multiple_of(row * order_rows, 8), order_rows), :]
    ancl_own = ancl_v[pl.ds(pl.multiple_of(row * anc_rows, 8), anc_rows), :]
    part = jnp.sum(
        par_own.astype(jnp.float32) * par_block.astype(jnp.float32), axis=0, keepdims=True
    ) + jnp.sum(ancl_own.astype(jnp.float32) * anc_block.astype(jnp.float32), axis=0, keepdims=True)
    part = jnp.where(row == 0, pivots[...] - part, -part)
    for i in range(part_ref.shape[0]):
        part_ref[i] = part


def local_whole(
    anc_inverse,
    parent_pivinv,
    parent_lower,
    parent_mask,
    leaf_lower_par,
    leaf_lower_anc,
    leaf_mask,
    leaf_pivots,
):
    row_index = lax.axis_index("row")
    row_devices = lax.axis_size("row")
    col_index = lax.axis_index("col")
    anc_rows = anc_inverse.shape[0]
    order_rows = parent_pivinv.shape[0]
    col_width = leaf_pivots.shape[0]
    off_width = parent_lower.shape[1] // 2
    half = anc_rows // 2
    anc_all = anc_rows * row_devices
    order_all = order_rows * row_devices

    sent_width = (row_devices // 2 + 1) * anc_rows
    piece_width = sent_width + order_all + 2 * leaf_lower_par.shape[1]
    piece = pl.pallas_call(
        piece_kernel,
        out_shape=jax.ShapeDtypeStruct((half, piece_width), jnp.bfloat16),
        in_specs=[pl.BlockSpec(memory_space=pltpu.VMEM)] * 4,
        out_specs=pl.BlockSpec(memory_space=pltpu.VMEM),
    )(anc_inverse, parent_lower, leaf_lower_par, leaf_lower_anc)
    full = lax.all_gather(piece, ("row", "col"), axis=0, tiled=True)
    parent_gate = jnp.repeat(parent_mask, BLOCK).astype(jnp.bfloat16)[:, None]
    leaf_gate = jnp.repeat(leaf_mask, BLOCK).astype(jnp.bfloat16)[:, None]
    vmem = pl.BlockSpec(memory_space=pltpu.VMEM)
    flops = 2 * (3 * order_rows * anc_all * order_all + 4 * order_rows * anc_all * col_width)
    block, offdiag_own, par_block, anc_block, parts = pl.pallas_call(
        leaf_kernel,
        out_shape=(
            jax.ShapeDtypeStruct((order_rows, order_all), jnp.float32),
            jax.ShapeDtypeStruct((anc_rows, off_width), jnp.bfloat16),
            jax.ShapeDtypeStruct((order_rows, col_width), jnp.bfloat16),
            jax.ShapeDtypeStruct((anc_rows, col_width), jnp.bfloat16),
            jax.ShapeDtypeStruct((row_devices, 1, col_width), jnp.float32),
        ),
        in_specs=[vmem] * 4
        + [pl.BlockSpec(memory_space=pl.ANY)]
        + [vmem] * 2,
        out_specs=(vmem,) * 5,
        scratch_shapes=[
            pltpu.VMEM((anc_all, sent_width), jnp.bfloat16),
            pltpu.VMEM((anc_all, anc_all), jnp.bfloat16),
            pltpu.VMEM((anc_all, order_all), jnp.bfloat16),
            pltpu.VMEM((order_all, col_width), jnp.bfloat16),
            pltpu.VMEM((anc_all, col_width), jnp.bfloat16),
            pltpu.VMEM((anc_rows, order_all), jnp.bfloat16),
            pltpu.SemaphoreType.DMA((16,)),
        ],
        cost_estimate=pl.CostEstimate(
            flops=flops, transcendentals=0, bytes_accessed=full.size + 8 * anc_rows * order_all
        ),
    )(
        parent_gate,
        leaf_gate[:order_all],
        leaf_gate[order_all:],
        leaf_pivots[None, :],
        full,
        anc_inverse,
        parent_pivinv,
    )
    density = jnp.sum(lax.all_to_all(parts, "row", 0, 0, tiled=True), axis=0)[0]
    return block, offdiag_own, par_block, anc_block, density


def fits_whole(mesh, anc_rows, order_rows):
    anc_all = anc_rows * mesh.shape["row"]
    return (
        anc_rows == order_rows
        and anc_rows % 128 == 0
        and anc_all * anc_all * 2 <= 16 * 1024 * 1024
    )


def solution(mesh):
    placed = (
        P(("pole", "row"), None),
        P(("pole", "row"), None),
        P(("pole", "row"), None),
        P(),
        P(("pole", "row"), None),
        P(("pole", "row"), None),
        P(),
        P(("pole", "col")),
    )
    placed_out = (
        P(("pole", "row"), None),
        P(("pole", "row"), "col"),
        P(("pole", "row"), "col"),
        P(("pole", "row"), "col"),
        P(("pole", "col")),
    )
    shards = mesh.shape["pole"] * mesh.shape["row"]

    def run(*args):
        anc_rows = args[0].shape[0] // shards
        order_rows = args[1].shape[0] // shards
        body = local_whole if fits_whole(mesh, anc_rows, order_rows) else local
        return jax.shard_map(
            body, mesh=mesh, in_specs=placed, out_specs=placed_out, check_vma=False
        )(*args)

    return run
```

```python
import jax
import jax.numpy as jnp
from jax import lax
from jax.experimental import pallas as pl
from jax.experimental.pallas import tpu as pltpu
from jax.sharding import PartitionSpec as P

BLOCK = 256
ORDER = 1024


def local(
    anc_inverse,
    parent_pivinv,
    parent_lower,
    parent_mask,
    leaf_lower_par,
    leaf_lower_anc,
    leaf_mask,
    leaf_pivots,
):
    row_index = lax.axis_index("row")
    row_devices = lax.axis_size("row")
    col_index = lax.axis_index("col")
    anc_rows = anc_inverse.shape[0]
    order_rows = parent_pivinv.shape[0]
    col_width = leaf_pivots.shape[0]
    parent_gate = lax.dynamic_slice_in_dim(
        jnp.repeat(parent_mask, BLOCK), row_index * anc_rows, anc_rows
    )
    lower_one = parent_lower * parent_gate[:, None].astype(jnp.bfloat16)
    lower_half = lax.dynamic_slice_in_dim(lower_one, col_index * col_width, col_width, 1)
    leaf_gate = jnp.repeat(leaf_mask, BLOCK)
    gate_par = lax.dynamic_slice_in_dim(leaf_gate[:ORDER], row_index * order_rows, order_rows)
    gate_anc = lax.dynamic_slice_in_dim(leaf_gate[ORDER:], row_index * anc_rows, anc_rows)
    leaf_local = jnp.concatenate(
        [
            leaf_lower_par * gate_par[:, None].astype(jnp.bfloat16),
            leaf_lower_anc * gate_anc[:, None].astype(jnp.bfloat16),
        ],
        axis=0,
    )
    leaf_half = lax.dynamic_slice_in_dim(leaf_local, col_index * col_width, col_width, 1)
    columns = anc_inverse
    product = jnp.dot(
        columns,
        lax.all_gather(lower_half, "row", axis=0, tiled=True),
        preferred_element_type=jnp.float32,
    )
    parent_offdiag = (-product).astype(jnp.bfloat16)
    offdiag_rows = lax.all_gather(parent_offdiag, "col", axis=1, tiled=True)
    columns = lower_one
    diag_sums = lax.psum_scatter(
        lax.dot_general(
            columns, offdiag_rows, (((0,), (0,)), ((), ())), preferred_element_type=jnp.float32
        ),
        "row",
        scatter_dimension=0,
        tiled=True,
    )
    parent_block = parent_pivinv - diag_sums
    parent_round = parent_block.astype(jnp.bfloat16)
    mirrored = lax.all_to_all(offdiag_rows, "row", split_axis=1, concat_axis=0, tiled=True).T
    upper_rows = jnp.concatenate(
        [
            parent_round.reshape(order_rows, row_devices, order_rows),
            mirrored.reshape(order_rows, row_devices, anc_rows),
        ],
        axis=2,
    )
    lower_rows = jnp.concatenate(
        [
            offdiag_rows.reshape(anc_rows, row_devices, order_rows),
            anc_inverse.reshape(anc_rows, row_devices, anc_rows),
        ],
        axis=2,
    )
    inverse_rows = jnp.concatenate(
        [upper_rows.reshape(order_rows, -1), lower_rows.reshape(anc_rows, -1)], axis=0
    )
    columns = inverse_rows
    leaf_product = jnp.dot(
        columns,
        lax.all_gather(leaf_half, "row", axis=0, tiled=True),
        preferred_element_type=jnp.float32,
    )
    leaf_result = (-leaf_product).astype(jnp.bfloat16)
    partial_sums = jnp.sum(leaf_half.astype(jnp.float32) * leaf_result.astype(jnp.float32), axis=0)
    density = leaf_pivots - lax.psum(partial_sums, "row")
    return (
        parent_block,
        parent_offdiag,
        leaf_result[:order_rows],
        leaf_result[order_rows:],
        density,
    )


def piece_kernel(anc_hbm, lower_hbm, par_hbm, ancl_hbm, out_ref):
    row, col = lax.axis_index("row"), lax.axis_index("col")
    half = out_ref.shape[0]
    blk = anc_hbm.shape[0]
    blocks = anc_hbm.shape[1] // blk
    sent = blocks // 2 + 1
    rows = pl.ds(pl.multiple_of(col * half, 8), half)
    for k in range(sent):
        start = pl.multiple_of(lax.rem(row + k, blocks) * blk, 128)
        out_ref[:, k * blk : (k + 1) * blk] = anc_hbm[rows, pl.ds(start, blk)]
    at = sent * blk
    for source in (lower_hbm, par_hbm, ancl_hbm):
        width = source.shape[1]
        out_ref[:, at : at + width] = source[rows, :]
        at += width


def leaf_kernel(
    gate_col, par_col_ref, anc_col_ref, par_own_gate, anc_own_gate, pivots, full_hbm, anc_local, pivinv,
    block_ref, offdiag_ref, par_ref, anc_ref, part_ref,
    sent_v, anc_v, lower_v, par_v, ancl_v, rows_v, sem,
):
    row, col = lax.axis_index("row"), lax.axis_index("col")
    anc_all, order_all = anc_v.shape[0], lower_v.shape[1]
    width = par_v.shape[1]
    order_rows, anc_rows = block_ref.shape[0], anc_local.shape[0]
    off_width = offdiag_ref.shape[1]
    sent_width = sent_v.shape[1]
    leaf_at = sent_width + order_all
    leaf_width = (full_hbm.shape[1] - leaf_at) // 2
    copies = [
        pltpu.make_async_copy(full_hbm.at[:, pl.ds(sent_width, order_all)], lower_v, sem.at[1]),
        pltpu.make_async_copy(full_hbm.at[:, pl.ds(0, sent_width)], sent_v, sem.at[0]),
        pltpu.make_async_copy(
            full_hbm.at[:, pl.ds(pl.multiple_of(leaf_at + col * width, 128), width)], par_v, sem.at[2]
        ),
        pltpu.make_async_copy(
            full_hbm.at[:, pl.ds(pl.multiple_of(leaf_at + leaf_width + col * width, 128), width)],
            ancl_v,
            sem.at[3],
        ),
    ]
    copies[0].start()
    copies[1].start()
    gate_col = gate_col[...]
    anc_here = anc_local[...]
    copies[0].wait()
    copies[2].start()
    copies[3].start()
    lower = lower_v[...]
    rows = (-jnp.dot(anc_here * gate_col, lower, preferred_element_type=jnp.float32)).astype(
        jnp.bfloat16
    )
    rows_v[...] = rows
    offdiag_ref[...] = rows_v[:, pl.ds(pl.multiple_of(col * off_width, 128), off_width)]
    copies[1].wait()
    blocks = anc_all // anc_rows
    sent = sent_width // anc_rows
    for p in range(blocks):
        rows_p = slice(p * anc_rows, (p + 1) * anc_rows)
        first = min(sent, blocks - p)
        anc_v[rows_p, p * anc_rows : (p + first) * anc_rows] = sent_v[rows_p, : first * anc_rows]
        if first < sent:
            anc_v[rows_p, : (sent - first) * anc_rows] = sent_v[rows_p, first * anc_rows : sent_width]
        for q in range(blocks):
            k = (q - p) % blocks
            if k >= sent:
                k = (p - q) % blocks
                part = sent_v[q * anc_rows : (q + 1) * anc_rows, k * anc_rows : (k + 1) * anc_rows]
                anc_v[rows_p, q * anc_rows : (q + 1) * anc_rows] = (
                    part.astype(jnp.float32).T.astype(jnp.bfloat16)
                )
    lower_cols = lower_v[:, pl.ds(pl.multiple_of(row * order_rows, 128), order_rows)]
    offdiag_t = (
        -jnp.dot(lower_cols.T * gate_col, anc_v[...], preferred_element_type=jnp.float32)
    ).astype(jnp.bfloat16)
    block = pivinv[...] - jnp.dot(offdiag_t * gate_col, lower, preferred_element_type=jnp.float32)
    block_ref[...] = block
    copies[2].wait()
    copies[3].wait()
    par_col, anc_col = par_col_ref[...], anc_col_ref[...]
    par, ancl = par_v[...], ancl_v[...]
    upper = jnp.dot(
        block.astype(jnp.bfloat16) * par_col, par, preferred_element_type=jnp.float32
    ) + jnp.dot(offdiag_t * anc_col, ancl, preferred_element_type=jnp.float32)
    par_block = (-upper).astype(jnp.bfloat16)
    lower_sum = jnp.dot(rows * par_col, par, preferred_element_type=jnp.float32) + jnp.dot(
        anc_here * anc_col, ancl, preferred_element_type=jnp.float32
    )
    anc_block = (-lower_sum).astype(jnp.bfloat16)
    par_ref[...] = par_block
    anc_ref[...] = anc_block
    par_own = par_v[pl.ds(pl.multiple_of(row * order_rows, 8), order_rows), :] * par_own_gate[...]
    ancl_own = ancl_v[pl.ds(pl.multiple_of(row * anc_rows, 8), anc_rows), :] * anc_own_gate[...]
    part = jnp.sum(
        par_own.astype(jnp.float32) * par_block.astype(jnp.float32), axis=0, keepdims=True
    ) + jnp.sum(ancl_own.astype(jnp.float32) * anc_block.astype(jnp.float32), axis=0, keepdims=True)
    part = jnp.where(row == 0, pivots[...] - part, -part)
    for i in range(part_ref.shape[0]):
        part_ref[i] = part


def local_whole(
    anc_inverse,
    parent_pivinv,
    parent_lower,
    parent_mask,
    leaf_lower_par,
    leaf_lower_anc,
    leaf_mask,
    leaf_pivots,
):
    row_index = lax.axis_index("row")
    row_devices = lax.axis_size("row")
    col_index = lax.axis_index("col")
    anc_rows = anc_inverse.shape[0]
    order_rows = parent_pivinv.shape[0]
    col_width = leaf_pivots.shape[0]
    off_width = parent_lower.shape[1] // 2
    half = anc_rows // 2
    anc_all = anc_rows * row_devices
    order_all = order_rows * row_devices

    sent_width = (row_devices // 2 + 1) * anc_rows
    piece_width = sent_width + order_all + 2 * leaf_lower_par.shape[1]
    piece = pl.pallas_call(
        piece_kernel,
        out_shape=jax.ShapeDtypeStruct((half, piece_width), jnp.bfloat16),
        in_specs=[pl.BlockSpec(memory_space=pltpu.VMEM)] * 4,
        out_specs=pl.BlockSpec(memory_space=pltpu.VMEM),
    )(anc_inverse, parent_lower, leaf_lower_par, leaf_lower_anc)
    full = lax.all_gather(piece, ("row", "col"), axis=0, tiled=True)
    parent_gate = jnp.repeat(parent_mask, BLOCK).astype(jnp.bfloat16)[:, None]
    leaf_gate = jnp.repeat(leaf_mask, BLOCK).astype(jnp.bfloat16)[:, None]
    vmem = pl.BlockSpec(memory_space=pltpu.VMEM)
    flops = 2 * (3 * order_rows * anc_all * order_all + 4 * order_rows * anc_all * col_width)
    block, offdiag_own, par_block, anc_block, parts = pl.pallas_call(
        leaf_kernel,
        out_shape=(
            jax.ShapeDtypeStruct((order_rows, order_all), jnp.float32),
            jax.ShapeDtypeStruct((anc_rows, off_width), jnp.bfloat16),
            jax.ShapeDtypeStruct((order_rows, col_width), jnp.bfloat16),
            jax.ShapeDtypeStruct((anc_rows, col_width), jnp.bfloat16),
            jax.ShapeDtypeStruct((row_devices, 1, col_width), jnp.float32),
        ),
        in_specs=[vmem] * 6
        + [pl.BlockSpec(memory_space=pl.ANY)]
        + [vmem] * 2,
        out_specs=(vmem,) * 5,
        scratch_shapes=[
            pltpu.VMEM((anc_all, sent_width), jnp.bfloat16),
            pltpu.VMEM((anc_all, anc_all), jnp.bfloat16),
            pltpu.VMEM((anc_all, order_all), jnp.bfloat16),
            pltpu.VMEM((order_all, col_width), jnp.bfloat16),
            pltpu.VMEM((anc_all, col_width), jnp.bfloat16),
            pltpu.VMEM((anc_rows, order_all), jnp.bfloat16),
            pltpu.SemaphoreType.DMA((4,)),
        ],
        cost_estimate=pl.CostEstimate(
            flops=flops, transcendentals=0, bytes_accessed=full.size + 8 * anc_rows * order_all
        ),
    )(
        parent_gate.T,
        leaf_gate[:order_all].T,
        leaf_gate[order_all:].T,
        lax.dynamic_slice_in_dim(leaf_gate[:order_all], row_index * order_rows, order_rows),
        lax.dynamic_slice_in_dim(leaf_gate[order_all:], row_index * anc_rows, anc_rows),
        leaf_pivots[None, :],
        full,
        anc_inverse,
        parent_pivinv,
    )
    density = jnp.sum(lax.all_to_all(parts, "row", 0, 0, tiled=True), axis=0)[0]
    return block, offdiag_own, par_block, anc_block, density


def fits_whole(mesh, anc_rows, order_rows):
    anc_all = anc_rows * mesh.shape["row"]
    return (
        anc_rows == order_rows
        and anc_rows % 128 == 0
        and anc_all * anc_all * 2 <= 16 * 1024 * 1024
    )


def solution(mesh):
    placed = (
        P(("pole", "row"), None),
        P(("pole", "row"), None),
        P(("pole", "row"), None),
        P(),
        P(("pole", "row"), None),
        P(("pole", "row"), None),
        P(),
        P(("pole", "col")),
    )
    placed_out = (
        P(("pole", "row"), None),
        P(("pole", "row"), "col"),
        P(("pole", "row"), "col"),
        P(("pole", "row"), "col"),
        P(("pole", "col")),
    )
    shards = mesh.shape["pole"] * mesh.shape["row"]

    def run(*args):
        anc_rows = args[0].shape[0] // shards
        order_rows = args[1].shape[0] // shards
        body = local_whole if fits_whole(mesh, anc_rows, order_rows) else local
        return jax.shard_map(
            body, mesh=mesh, in_specs=placed, out_specs=placed_out, check_vma=False
        )(*args)

    return run
```

```python
import jax
import jax.numpy as jnp
from jax import lax
from jax.experimental import pallas as pl
from jax.experimental.pallas import tpu as pltpu
from jax.sharding import PartitionSpec as P

BLOCK = 256
ORDER = 1024


def local(
    anc_inverse,
    parent_pivinv,
    parent_lower,
    parent_mask,
    leaf_lower_par,
    leaf_lower_anc,
    leaf_mask,
    leaf_pivots,
):
    row_index = lax.axis_index("row")
    row_devices = lax.axis_size("row")
    col_index = lax.axis_index("col")
    anc_rows = anc_inverse.shape[0]
    order_rows = parent_pivinv.shape[0]
    col_width = leaf_pivots.shape[0]
    parent_gate = lax.dynamic_slice_in_dim(
        jnp.repeat(parent_mask, BLOCK), row_index * anc_rows, anc_rows
    )
    lower_one = parent_lower * parent_gate[:, None].astype(jnp.bfloat16)
    lower_half = lax.dynamic_slice_in_dim(lower_one, col_index * col_width, col_width, 1)
    leaf_gate = jnp.repeat(leaf_mask, BLOCK)
    gate_par = lax.dynamic_slice_in_dim(leaf_gate[:ORDER], row_index * order_rows, order_rows)
    gate_anc = lax.dynamic_slice_in_dim(leaf_gate[ORDER:], row_index * anc_rows, anc_rows)
    leaf_local = jnp.concatenate(
        [
            leaf_lower_par * gate_par[:, None].astype(jnp.bfloat16),
            leaf_lower_anc * gate_anc[:, None].astype(jnp.bfloat16),
        ],
        axis=0,
    )
    leaf_half = lax.dynamic_slice_in_dim(leaf_local, col_index * col_width, col_width, 1)
    columns = anc_inverse
    product = jnp.dot(
        columns,
        lax.all_gather(lower_half, "row", axis=0, tiled=True),
        preferred_element_type=jnp.float32,
    )
    parent_offdiag = (-product).astype(jnp.bfloat16)
    offdiag_rows = lax.all_gather(parent_offdiag, "col", axis=1, tiled=True)
    columns = lower_one
    diag_sums = lax.psum_scatter(
        lax.dot_general(
            columns, offdiag_rows, (((0,), (0,)), ((), ())), preferred_element_type=jnp.float32
        ),
        "row",
        scatter_dimension=0,
        tiled=True,
    )
    parent_block = parent_pivinv - diag_sums
    parent_round = parent_block.astype(jnp.bfloat16)
    mirrored = lax.all_to_all(offdiag_rows, "row", split_axis=1, concat_axis=0, tiled=True).T
    upper_rows = jnp.concatenate(
        [
            parent_round.reshape(order_rows, row_devices, order_rows),
            mirrored.reshape(order_rows, row_devices, anc_rows),
        ],
        axis=2,
    )
    lower_rows = jnp.concatenate(
        [
            offdiag_rows.reshape(anc_rows, row_devices, order_rows),
            anc_inverse.reshape(anc_rows, row_devices, anc_rows),
        ],
        axis=2,
    )
    inverse_rows = jnp.concatenate(
        [upper_rows.reshape(order_rows, -1), lower_rows.reshape(anc_rows, -1)], axis=0
    )
    columns = inverse_rows
    leaf_product = jnp.dot(
        columns,
        lax.all_gather(leaf_half, "row", axis=0, tiled=True),
        preferred_element_type=jnp.float32,
    )
    leaf_result = (-leaf_product).astype(jnp.bfloat16)
    partial_sums = jnp.sum(leaf_half.astype(jnp.float32) * leaf_result.astype(jnp.float32), axis=0)
    density = leaf_pivots - lax.psum(partial_sums, "row")
    return (
        parent_block,
        parent_offdiag,
        leaf_result[:order_rows],
        leaf_result[order_rows:],
        density,
    )


def piece_kernel(anc_hbm, lower_hbm, par_hbm, ancl_hbm, out_ref):
    row, col = lax.axis_index("row"), lax.axis_index("col")
    half = out_ref.shape[0]
    blk = anc_hbm.shape[0]
    blocks = anc_hbm.shape[1] // blk
    sent = blocks // 2 + 1
    rows = pl.ds(pl.multiple_of(col * half, 8), half)
    for k in range(sent):
        start = pl.multiple_of(lax.rem(row + k, blocks) * blk, 128)
        out_ref[:, k * blk : (k + 1) * blk] = anc_hbm[rows, pl.ds(start, blk)]
    at = sent * blk
    for source in (lower_hbm, par_hbm, ancl_hbm):
        width = source.shape[1]
        out_ref[:, at : at + width] = source[rows, :]
        at += width


def leaf_kernel(
    gate_col, par_col_ref, anc_col_ref, par_own_gate, anc_own_gate, pivots, full_hbm, anc_local, pivinv,
    block_ref, offdiag_ref, par_ref, anc_ref, part_ref,
    sent_v, anc_v, lower_v, par_v, ancl_v, rows_v, pivinv_v, sem,
):
    row, col = lax.axis_index("row"), lax.axis_index("col")
    anc_all, order_all = anc_v.shape[0], lower_v.shape[1]
    width = par_v.shape[1]
    order_rows, anc_rows = block_ref.shape[0], anc_local.shape[0]
    off_width = offdiag_ref.shape[1]
    sent_width = sent_v.shape[1]
    leaf_at = sent_width + order_all
    leaf_width = (full_hbm.shape[1] - leaf_at) // 2
    copies = [
        pltpu.make_async_copy(full_hbm.at[:, pl.ds(sent_width, order_all)], lower_v, sem.at[1]),
        pltpu.make_async_copy(full_hbm.at[:, pl.ds(0, sent_width)], sent_v, sem.at[0]),
        pltpu.make_async_copy(
            full_hbm.at[:, pl.ds(pl.multiple_of(leaf_at + col * width, 128), width)], par_v, sem.at[2]
        ),
        pltpu.make_async_copy(
            full_hbm.at[:, pl.ds(pl.multiple_of(leaf_at + leaf_width + col * width, 128), width)],
            ancl_v,
            sem.at[3],
        ),
    ]
    pivinv_copy = pltpu.make_async_copy(pivinv, pivinv_v, sem.at[4])
    pivinv_copy.start()
    copies[0].start()
    copies[1].start()
    gate_col = gate_col[...]
    anc_here = anc_local[...]
    copies[0].wait()
    copies[2].start()
    copies[3].start()
    lower = lower_v[...]
    rows = (-jnp.dot(anc_here * gate_col, lower, preferred_element_type=jnp.float32)).astype(
        jnp.bfloat16
    )
    rows_v[...] = rows
    offdiag_ref[...] = rows_v[:, pl.ds(pl.multiple_of(col * off_width, 128), off_width)]
    copies[1].wait()
    blocks = anc_all // anc_rows
    sent = sent_width // anc_rows
    for p in range(blocks):
        rows_p = slice(p * anc_rows, (p + 1) * anc_rows)
        first = min(sent, blocks - p)
        anc_v[rows_p, p * anc_rows : (p + first) * anc_rows] = sent_v[rows_p, : first * anc_rows]
        if first < sent:
            anc_v[rows_p, : (sent - first) * anc_rows] = sent_v[rows_p, first * anc_rows : sent_width]
        for q in range(blocks):
            k = (q - p) % blocks
            if k >= sent:
                k = (p - q) % blocks
                part = sent_v[q * anc_rows : (q + 1) * anc_rows, k * anc_rows : (k + 1) * anc_rows]
                anc_v[rows_p, q * anc_rows : (q + 1) * anc_rows] = (
                    part.astype(jnp.float32).T.astype(jnp.bfloat16)
                )
    lower_cols = lower_v[:, pl.ds(pl.multiple_of(row * order_rows, 128), order_rows)]
    offdiag_t = (
        -jnp.dot(lower_cols.T * gate_col, anc_v[...], preferred_element_type=jnp.float32)
    ).astype(jnp.bfloat16)
    pivinv_copy.wait()
    block = pivinv_v[...] - jnp.dot(offdiag_t * gate_col, lower, preferred_element_type=jnp.float32)
    block_ref[...] = block
    copies[2].wait()
    copies[3].wait()
    par_col, anc_col = par_col_ref[...], anc_col_ref[...]
    par, ancl = par_v[...], ancl_v[...]
    upper = jnp.dot(
        block.astype(jnp.bfloat16) * par_col, par, preferred_element_type=jnp.float32
    ) + jnp.dot(offdiag_t * anc_col, ancl, preferred_element_type=jnp.float32)
    par_block = (-upper).astype(jnp.bfloat16)
    lower_sum = jnp.dot(rows * par_col, par, preferred_element_type=jnp.float32) + jnp.dot(
        anc_here * anc_col, ancl, preferred_element_type=jnp.float32
    )
    anc_block = (-lower_sum).astype(jnp.bfloat16)
    par_ref[...] = par_block
    anc_ref[...] = anc_block
    par_own = par_v[pl.ds(pl.multiple_of(row * order_rows, 8), order_rows), :] * par_own_gate[...]
    ancl_own = ancl_v[pl.ds(pl.multiple_of(row * anc_rows, 8), anc_rows), :] * anc_own_gate[...]
    part = jnp.sum(
        par_own.astype(jnp.float32) * par_block.astype(jnp.float32), axis=0, keepdims=True
    ) + jnp.sum(ancl_own.astype(jnp.float32) * anc_block.astype(jnp.float32), axis=0, keepdims=True)
    part = jnp.where(row == 0, pivots[...] - part, -part)
    for i in range(part_ref.shape[0]):
        part_ref[i] = part


def local_whole(
    anc_inverse,
    parent_pivinv,
    parent_lower,
    parent_mask,
    leaf_lower_par,
    leaf_lower_anc,
    leaf_mask,
    leaf_pivots,
):
    row_index = lax.axis_index("row")
    row_devices = lax.axis_size("row")
    col_index = lax.axis_index("col")
    anc_rows = anc_inverse.shape[0]
    order_rows = parent_pivinv.shape[0]
    col_width = leaf_pivots.shape[0]
    off_width = parent_lower.shape[1] // 2
    half = anc_rows // 2
    anc_all = anc_rows * row_devices
    order_all = order_rows * row_devices

    sent_width = (row_devices // 2 + 1) * anc_rows
    piece_width = sent_width + order_all + 2 * leaf_lower_par.shape[1]
    piece = pl.pallas_call(
        piece_kernel,
        out_shape=jax.ShapeDtypeStruct((half, piece_width), jnp.bfloat16),
        in_specs=[pl.BlockSpec(memory_space=pltpu.VMEM)] * 4,
        out_specs=pl.BlockSpec(memory_space=pltpu.VMEM),
    )(anc_inverse, parent_lower, leaf_lower_par, leaf_lower_anc)
    full = lax.all_gather(piece, ("row", "col"), axis=0, tiled=True)
    parent_gate = jnp.repeat(parent_mask, BLOCK).astype(jnp.bfloat16)[:, None]
    leaf_gate = jnp.repeat(leaf_mask, BLOCK).astype(jnp.bfloat16)[:, None]
    vmem = pl.BlockSpec(memory_space=pltpu.VMEM)
    flops = 2 * (3 * order_rows * anc_all * order_all + 4 * order_rows * anc_all * col_width)
    block, offdiag_own, par_block, anc_block, parts = pl.pallas_call(
        leaf_kernel,
        out_shape=(
            jax.ShapeDtypeStruct((order_rows, order_all), jnp.float32),
            jax.ShapeDtypeStruct((anc_rows, off_width), jnp.bfloat16),
            jax.ShapeDtypeStruct((order_rows, col_width), jnp.bfloat16),
            jax.ShapeDtypeStruct((anc_rows, col_width), jnp.bfloat16),
            jax.ShapeDtypeStruct((row_devices, 1, col_width), jnp.float32),
        ),
        in_specs=[vmem] * 6
        + [pl.BlockSpec(memory_space=pl.ANY), vmem, pl.BlockSpec(memory_space=pl.ANY)],
        out_specs=(vmem,) * 5,
        scratch_shapes=[
            pltpu.VMEM((anc_all, sent_width), jnp.bfloat16),
            pltpu.VMEM((anc_all, anc_all), jnp.bfloat16),
            pltpu.VMEM((anc_all, order_all), jnp.bfloat16),
            pltpu.VMEM((order_all, col_width), jnp.bfloat16),
            pltpu.VMEM((anc_all, col_width), jnp.bfloat16),
            pltpu.VMEM((anc_rows, order_all), jnp.bfloat16),
            pltpu.VMEM((order_rows, order_all), jnp.float32),
            pltpu.SemaphoreType.DMA((5,)),
        ],
        cost_estimate=pl.CostEstimate(
            flops=flops, transcendentals=0, bytes_accessed=full.size + 8 * anc_rows * order_all
        ),
    )(
        parent_gate.T,
        leaf_gate[:order_all].T,
        leaf_gate[order_all:].T,
        lax.dynamic_slice_in_dim(leaf_gate[:order_all], row_index * order_rows, order_rows),
        lax.dynamic_slice_in_dim(leaf_gate[order_all:], row_index * anc_rows, anc_rows),
        leaf_pivots[None, :],
        full,
        anc_inverse,
        parent_pivinv,
    )
    density = jnp.sum(lax.all_to_all(parts, "row", 0, 0, tiled=True), axis=0)[0]
    return block, offdiag_own, par_block, anc_block, density


def fits_whole(mesh, anc_rows, order_rows):
    anc_all = anc_rows * mesh.shape["row"]
    return (
        anc_rows == order_rows
        and anc_rows % 128 == 0
        and anc_all * anc_all * 2 <= 16 * 1024 * 1024
    )


def solution(mesh):
    placed = (
        P(("pole", "row"), None),
        P(("pole", "row"), None),
        P(("pole", "row"), None),
        P(),
        P(("pole", "row"), None),
        P(("pole", "row"), None),
        P(),
        P(("pole", "col")),
    )
    placed_out = (
        P(("pole", "row"), None),
        P(("pole", "row"), "col"),
        P(("pole", "row"), "col"),
        P(("pole", "row"), "col"),
        P(("pole", "col")),
    )
    shards = mesh.shape["pole"] * mesh.shape["row"]

    def run(*args):
        anc_rows = args[0].shape[0] // shards
        order_rows = args[1].shape[0] // shards
        body = local_whole if fits_whole(mesh, anc_rows, order_rows) else local
        return jax.shard_map(
            body, mesh=mesh, in_specs=placed, out_specs=placed_out, check_vma=False
        )(*args)

    return run
```

```python
import jax
import jax.numpy as jnp
from jax import lax
from jax.experimental import pallas as pl
from jax.experimental.pallas import tpu as pltpu
from jax.sharding import PartitionSpec as P

BLOCK = 256
ORDER = 1024


def local(
    anc_inverse,
    parent_pivinv,
    parent_lower,
    parent_mask,
    leaf_lower_par,
    leaf_lower_anc,
    leaf_mask,
    leaf_pivots,
):
    row_index = lax.axis_index("row")
    row_devices = lax.axis_size("row")
    col_index = lax.axis_index("col")
    anc_rows = anc_inverse.shape[0]
    order_rows = parent_pivinv.shape[0]
    col_width = leaf_pivots.shape[0]
    parent_gate = lax.dynamic_slice_in_dim(
        jnp.repeat(parent_mask, BLOCK), row_index * anc_rows, anc_rows
    )
    lower_one = parent_lower * parent_gate[:, None].astype(jnp.bfloat16)
    lower_half = lax.dynamic_slice_in_dim(lower_one, col_index * col_width, col_width, 1)
    leaf_gate = jnp.repeat(leaf_mask, BLOCK)
    gate_par = lax.dynamic_slice_in_dim(leaf_gate[:ORDER], row_index * order_rows, order_rows)
    gate_anc = lax.dynamic_slice_in_dim(leaf_gate[ORDER:], row_index * anc_rows, anc_rows)
    leaf_local = jnp.concatenate(
        [
            leaf_lower_par * gate_par[:, None].astype(jnp.bfloat16),
            leaf_lower_anc * gate_anc[:, None].astype(jnp.bfloat16),
        ],
        axis=0,
    )
    leaf_half = lax.dynamic_slice_in_dim(leaf_local, col_index * col_width, col_width, 1)
    columns = anc_inverse
    product = jnp.dot(
        columns,
        lax.all_gather(lower_half, "row", axis=0, tiled=True),
        preferred_element_type=jnp.float32,
    )
    parent_offdiag = (-product).astype(jnp.bfloat16)
    offdiag_rows = lax.all_gather(parent_offdiag, "col", axis=1, tiled=True)
    columns = lower_one
    diag_sums = lax.psum_scatter(
        lax.dot_general(
            columns, offdiag_rows, (((0,), (0,)), ((), ())), preferred_element_type=jnp.float32
        ),
        "row",
        scatter_dimension=0,
        tiled=True,
    )
    parent_block = parent_pivinv - diag_sums
    parent_round = parent_block.astype(jnp.bfloat16)
    mirrored = lax.all_to_all(offdiag_rows, "row", split_axis=1, concat_axis=0, tiled=True).T
    upper_rows = jnp.concatenate(
        [
            parent_round.reshape(order_rows, row_devices, order_rows),
            mirrored.reshape(order_rows, row_devices, anc_rows),
        ],
        axis=2,
    )
    lower_rows = jnp.concatenate(
        [
            offdiag_rows.reshape(anc_rows, row_devices, order_rows),
            anc_inverse.reshape(anc_rows, row_devices, anc_rows),
        ],
        axis=2,
    )
    inverse_rows = jnp.concatenate(
        [upper_rows.reshape(order_rows, -1), lower_rows.reshape(anc_rows, -1)], axis=0
    )
    columns = inverse_rows
    leaf_product = jnp.dot(
        columns,
        lax.all_gather(leaf_half, "row", axis=0, tiled=True),
        preferred_element_type=jnp.float32,
    )
    leaf_result = (-leaf_product).astype(jnp.bfloat16)
    partial_sums = jnp.sum(leaf_half.astype(jnp.float32) * leaf_result.astype(jnp.float32), axis=0)
    density = leaf_pivots - lax.psum(partial_sums, "row")
    return (
        parent_block,
        parent_offdiag,
        leaf_result[:order_rows],
        leaf_result[order_rows:],
        density,
    )


def piece_kernel(anc_hbm, lower_hbm, par_hbm, ancl_hbm, out_ref):
    row, col = lax.axis_index("row"), lax.axis_index("col")
    half = out_ref.shape[0]
    blk = anc_hbm.shape[0]
    blocks = anc_hbm.shape[1] // blk
    sent = blocks // 2 + 1
    rows = pl.ds(pl.multiple_of(col * half, 8), half)
    for k in range(sent):
        start = pl.multiple_of(lax.rem(row + k, blocks) * blk, 128)
        out_ref[:, k * blk : (k + 1) * blk] = anc_hbm[rows, pl.ds(start, blk)]
    at = sent * blk
    for source in (lower_hbm, par_hbm, ancl_hbm):
        width = source.shape[1]
        out_ref[:, at : at + width] = source[rows, :]
        at += width


def leaf_kernel(
    gate_col, par_col_ref, anc_col_ref, par_own_gate, anc_own_gate, pivots, full_hbm, anc_local, pivinv,
    block_ref, offdiag_ref, par_ref, anc_ref, part_ref,
    sent_v, anc_v, lower_v, par_v, ancl_v, rows_v, block_v, sem,
):
    row, col = lax.axis_index("row"), lax.axis_index("col")
    anc_all, order_all = anc_v.shape[0], lower_v.shape[1]
    width = par_v.shape[1]
    order_rows, anc_rows = block_ref.shape[0], anc_local.shape[0]
    off_width = offdiag_ref.shape[1]
    sent_width = sent_v.shape[1]
    leaf_at = sent_width + order_all
    leaf_width = (full_hbm.shape[1] - leaf_at) // 2
    copies = [
        pltpu.make_async_copy(full_hbm.at[:, pl.ds(sent_width, order_all)], lower_v, sem.at[1]),
        pltpu.make_async_copy(full_hbm.at[:, pl.ds(0, sent_width)], sent_v, sem.at[0]),
        pltpu.make_async_copy(
            full_hbm.at[:, pl.ds(pl.multiple_of(leaf_at + col * width, 128), width)], par_v, sem.at[2]
        ),
        pltpu.make_async_copy(
            full_hbm.at[:, pl.ds(pl.multiple_of(leaf_at + leaf_width + col * width, 128), width)],
            ancl_v,
            sem.at[3],
        ),
    ]
    copies[0].start()
    copies[1].start()
    gate_col = gate_col[...]
    anc_here = anc_local[...]
    copies[0].wait()
    copies[2].start()
    copies[3].start()
    lower = lower_v[...]
    rows = (-jnp.dot(anc_here * gate_col, lower, preferred_element_type=jnp.float32)).astype(
        jnp.bfloat16
    )
    rows_v[...] = rows
    offdiag_ref[...] = rows_v[:, pl.ds(pl.multiple_of(col * off_width, 128), off_width)]
    copies[1].wait()
    blocks = anc_all // anc_rows
    sent = sent_width // anc_rows
    for p in range(blocks):
        rows_p = slice(p * anc_rows, (p + 1) * anc_rows)
        first = min(sent, blocks - p)
        anc_v[rows_p, p * anc_rows : (p + first) * anc_rows] = sent_v[rows_p, : first * anc_rows]
        if first < sent:
            anc_v[rows_p, : (sent - first) * anc_rows] = sent_v[rows_p, first * anc_rows : sent_width]
        for q in range(blocks):
            k = (q - p) % blocks
            if k >= sent:
                k = (p - q) % blocks
                part = sent_v[q * anc_rows : (q + 1) * anc_rows, k * anc_rows : (k + 1) * anc_rows]
                anc_v[rows_p, q * anc_rows : (q + 1) * anc_rows] = (
                    part.astype(jnp.float32).T.astype(jnp.bfloat16)
                )
    lower_cols = lower_v[:, pl.ds(pl.multiple_of(row * order_rows, 128), order_rows)]
    offdiag_t = (
        -jnp.dot(lower_cols.T * gate_col, anc_v[...], preferred_element_type=jnp.float32)
    ).astype(jnp.bfloat16)
    block = pivinv[...] - jnp.dot(offdiag_t * gate_col, lower, preferred_element_type=jnp.float32)
    block_v[...] = block
    block_copy = pltpu.make_async_copy(block_v, block_ref, sem.at[4])
    block_copy.start()
    copies[2].wait()
    copies[3].wait()
    par_col, anc_col = par_col_ref[...], anc_col_ref[...]
    par, ancl = par_v[...], ancl_v[...]
    upper = jnp.dot(
        block.astype(jnp.bfloat16) * par_col, par, preferred_element_type=jnp.float32
    ) + jnp.dot(offdiag_t * anc_col, ancl, preferred_element_type=jnp.float32)
    par_block = (-upper).astype(jnp.bfloat16)
    lower_sum = jnp.dot(rows * par_col, par, preferred_element_type=jnp.float32) + jnp.dot(
        anc_here * anc_col, ancl, preferred_element_type=jnp.float32
    )
    anc_block = (-lower_sum).astype(jnp.bfloat16)
    par_ref[...] = par_block
    anc_ref[...] = anc_block
    par_own = par_v[pl.ds(pl.multiple_of(row * order_rows, 8), order_rows), :] * par_own_gate[...]
    ancl_own = ancl_v[pl.ds(pl.multiple_of(row * anc_rows, 8), anc_rows), :] * anc_own_gate[...]
    part = jnp.sum(
        par_own.astype(jnp.float32) * par_block.astype(jnp.float32), axis=0, keepdims=True
    ) + jnp.sum(ancl_own.astype(jnp.float32) * anc_block.astype(jnp.float32), axis=0, keepdims=True)
    part = jnp.where(row == 0, pivots[...] - part, -part)
    for i in range(part_ref.shape[0]):
        part_ref[i] = part
    block_copy.wait()


def local_whole(
    anc_inverse,
    parent_pivinv,
    parent_lower,
    parent_mask,
    leaf_lower_par,
    leaf_lower_anc,
    leaf_mask,
    leaf_pivots,
):
    row_index = lax.axis_index("row")
    row_devices = lax.axis_size("row")
    col_index = lax.axis_index("col")
    anc_rows = anc_inverse.shape[0]
    order_rows = parent_pivinv.shape[0]
    col_width = leaf_pivots.shape[0]
    off_width = parent_lower.shape[1] // 2
    half = anc_rows // 2
    anc_all = anc_rows * row_devices
    order_all = order_rows * row_devices

    sent_width = (row_devices // 2 + 1) * anc_rows
    piece_width = sent_width + order_all + 2 * leaf_lower_par.shape[1]
    piece = pl.pallas_call(
        piece_kernel,
        out_shape=jax.ShapeDtypeStruct((half, piece_width), jnp.bfloat16),
        in_specs=[pl.BlockSpec(memory_space=pltpu.VMEM)] * 4,
        out_specs=pl.BlockSpec(memory_space=pltpu.VMEM),
    )(anc_inverse, parent_lower, leaf_lower_par, leaf_lower_anc)
    full = lax.all_gather(piece, ("row", "col"), axis=0, tiled=True)
    parent_gate = jnp.repeat(parent_mask, BLOCK).astype(jnp.bfloat16)[:, None]
    leaf_gate = jnp.repeat(leaf_mask, BLOCK).astype(jnp.bfloat16)[:, None]
    vmem = pl.BlockSpec(memory_space=pltpu.VMEM)
    flops = 2 * (3 * order_rows * anc_all * order_all + 4 * order_rows * anc_all * col_width)
    block, offdiag_own, par_block, anc_block, parts = pl.pallas_call(
        leaf_kernel,
        out_shape=(
            jax.ShapeDtypeStruct((order_rows, order_all), jnp.float32),
            jax.ShapeDtypeStruct((anc_rows, off_width), jnp.bfloat16),
            jax.ShapeDtypeStruct((order_rows, col_width), jnp.bfloat16),
            jax.ShapeDtypeStruct((anc_rows, col_width), jnp.bfloat16),
            jax.ShapeDtypeStruct((row_devices, 1, col_width), jnp.float32),
        ),
        in_specs=[vmem] * 6
        + [pl.BlockSpec(memory_space=pl.ANY)]
        + [vmem] * 2,
        out_specs=(pl.BlockSpec(memory_space=pl.ANY),) + (vmem,) * 4,
        scratch_shapes=[
            pltpu.VMEM((anc_all, sent_width), jnp.bfloat16),
            pltpu.VMEM((anc_all, anc_all), jnp.bfloat16),
            pltpu.VMEM((anc_all, order_all), jnp.bfloat16),
            pltpu.VMEM((order_all, col_width), jnp.bfloat16),
            pltpu.VMEM((anc_all, col_width), jnp.bfloat16),
            pltpu.VMEM((anc_rows, order_all), jnp.bfloat16),
            pltpu.VMEM((order_rows, order_all), jnp.float32),
            pltpu.SemaphoreType.DMA((5,)),
        ],
        cost_estimate=pl.CostEstimate(
            flops=flops, transcendentals=0, bytes_accessed=full.size + 8 * anc_rows * order_all
        ),
    )(
        parent_gate.T,
        leaf_gate[:order_all].T,
        leaf_gate[order_all:].T,
        lax.dynamic_slice_in_dim(leaf_gate[:order_all], row_index * order_rows, order_rows),
        lax.dynamic_slice_in_dim(leaf_gate[order_all:], row_index * anc_rows, anc_rows),
        leaf_pivots[None, :],
        full,
        anc_inverse,
        parent_pivinv,
    )
    density = jnp.sum(lax.all_to_all(parts, "row", 0, 0, tiled=True), axis=0)[0]
    return block, offdiag_own, par_block, anc_block, density


def fits_whole(mesh, anc_rows, order_rows):
    anc_all = anc_rows * mesh.shape["row"]
    return (
        anc_rows == order_rows
        and anc_rows % 128 == 0
        and anc_all * anc_all * 2 <= 16 * 1024 * 1024
    )


def solution(mesh):
    placed = (
        P(("pole", "row"), None),
        P(("pole", "row"), None),
        P(("pole", "row"), None),
        P(),
        P(("pole", "row"), None),
        P(("pole", "row"), None),
        P(),
        P(("pole", "col")),
    )
    placed_out = (
        P(("pole", "row"), None),
        P(("pole", "row"), "col"),
        P(("pole", "row"), "col"),
        P(("pole", "row"), "col"),
        P(("pole", "col")),
    )
    shards = mesh.shape["pole"] * mesh.shape["row"]

    def run(*args):
        anc_rows = args[0].shape[0] // shards
        order_rows = args[1].shape[0] // shards
        body = local_whole if fits_whole(mesh, anc_rows, order_rows) else local
        return jax.shard_map(
            body, mesh=mesh, in_specs=placed, out_specs=placed_out, check_vma=False
        )(*args)

    return run
```

```python
import jax
import jax.numpy as jnp
from jax import lax
from jax.experimental import pallas as pl
from jax.experimental.pallas import tpu as pltpu
from jax.sharding import PartitionSpec as P

BLOCK = 256
ORDER = 1024


def local(
    anc_inverse,
    parent_pivinv,
    parent_lower,
    parent_mask,
    leaf_lower_par,
    leaf_lower_anc,
    leaf_mask,
    leaf_pivots,
):
    row_index = lax.axis_index("row")
    row_devices = lax.axis_size("row")
    col_index = lax.axis_index("col")
    anc_rows = anc_inverse.shape[0]
    order_rows = parent_pivinv.shape[0]
    col_width = leaf_pivots.shape[0]
    parent_gate = lax.dynamic_slice_in_dim(
        jnp.repeat(parent_mask, BLOCK), row_index * anc_rows, anc_rows
    )
    lower_one = parent_lower * parent_gate[:, None].astype(jnp.bfloat16)
    lower_half = lax.dynamic_slice_in_dim(lower_one, col_index * col_width, col_width, 1)
    leaf_gate = jnp.repeat(leaf_mask, BLOCK)
    gate_par = lax.dynamic_slice_in_dim(leaf_gate[:ORDER], row_index * order_rows, order_rows)
    gate_anc = lax.dynamic_slice_in_dim(leaf_gate[ORDER:], row_index * anc_rows, anc_rows)
    leaf_local = jnp.concatenate(
        [
            leaf_lower_par * gate_par[:, None].astype(jnp.bfloat16),
            leaf_lower_anc * gate_anc[:, None].astype(jnp.bfloat16),
        ],
        axis=0,
    )
    leaf_half = lax.dynamic_slice_in_dim(leaf_local, col_index * col_width, col_width, 1)
    columns = anc_inverse
    product = jnp.dot(
        columns,
        lax.all_gather(lower_half, "row", axis=0, tiled=True),
        preferred_element_type=jnp.float32,
    )
    parent_offdiag = (-product).astype(jnp.bfloat16)
    offdiag_rows = lax.all_gather(parent_offdiag, "col", axis=1, tiled=True)
    columns = lower_one
    diag_sums = lax.psum_scatter(
        lax.dot_general(
            columns, offdiag_rows, (((0,), (0,)), ((), ())), preferred_element_type=jnp.float32
        ),
        "row",
        scatter_dimension=0,
        tiled=True,
    )
    parent_block = parent_pivinv - diag_sums
    parent_round = parent_block.astype(jnp.bfloat16)
    mirrored = lax.all_to_all(offdiag_rows, "row", split_axis=1, concat_axis=0, tiled=True).T
    upper_rows = jnp.concatenate(
        [
            parent_round.reshape(order_rows, row_devices, order_rows),
            mirrored.reshape(order_rows, row_devices, anc_rows),
        ],
        axis=2,
    )
    lower_rows = jnp.concatenate(
        [
            offdiag_rows.reshape(anc_rows, row_devices, order_rows),
            anc_inverse.reshape(anc_rows, row_devices, anc_rows),
        ],
        axis=2,
    )
    inverse_rows = jnp.concatenate(
        [upper_rows.reshape(order_rows, -1), lower_rows.reshape(anc_rows, -1)], axis=0
    )
    columns = inverse_rows
    leaf_product = jnp.dot(
        columns,
        lax.all_gather(leaf_half, "row", axis=0, tiled=True),
        preferred_element_type=jnp.float32,
    )
    leaf_result = (-leaf_product).astype(jnp.bfloat16)
    partial_sums = jnp.sum(leaf_half.astype(jnp.float32) * leaf_result.astype(jnp.float32), axis=0)
    density = leaf_pivots - lax.psum(partial_sums, "row")
    return (
        parent_block,
        parent_offdiag,
        leaf_result[:order_rows],
        leaf_result[order_rows:],
        density,
    )


def piece_kernel(anc_hbm, lower_hbm, par_hbm, ancl_hbm, out_ref):
    row, col = lax.axis_index("row"), lax.axis_index("col")
    half = out_ref.shape[0]
    blk = anc_hbm.shape[0]
    blocks = anc_hbm.shape[1] // blk
    sent = blocks // 2 + 1
    rows = pl.ds(pl.multiple_of(col * half, 8), half)
    for k in range(sent):
        start = pl.multiple_of(lax.rem(row + k, blocks) * blk, 128)
        out_ref[:, k * blk : (k + 1) * blk] = anc_hbm[rows, pl.ds(start, blk)]
    at = sent * blk
    for source in (lower_hbm, par_hbm, ancl_hbm):
        width = source.shape[1]
        out_ref[:, at : at + width] = source[rows, :]
        at += width


def leaf_kernel(
    gate_col, par_col_ref, anc_col_ref, par_own_gate, anc_own_gate, pivots, full_hbm, pivinv,
    block_ref, offdiag_ref, par_ref, anc_ref, part_ref,
    sent_v, anc_v, lower_v, par_v, ancl_v, rows_v, sem,
):
    row, col = lax.axis_index("row"), lax.axis_index("col")
    anc_all, order_all = anc_v.shape[0], lower_v.shape[1]
    width = par_v.shape[1]
    order_rows, anc_rows = block_ref.shape[0], anc_ref.shape[0]
    off_width = offdiag_ref.shape[1]
    sent_width = sent_v.shape[1]
    leaf_at = sent_width + order_all
    leaf_width = (full_hbm.shape[1] - leaf_at) // 2
    copies = [
        pltpu.make_async_copy(full_hbm.at[:, pl.ds(sent_width, order_all)], lower_v, sem.at[1]),
        pltpu.make_async_copy(full_hbm.at[:, pl.ds(0, sent_width)], sent_v, sem.at[0]),
        pltpu.make_async_copy(
            full_hbm.at[:, pl.ds(pl.multiple_of(leaf_at + col * width, 128), width)], par_v, sem.at[2]
        ),
        pltpu.make_async_copy(
            full_hbm.at[:, pl.ds(pl.multiple_of(leaf_at + leaf_width + col * width, 128), width)],
            ancl_v,
            sem.at[3],
        ),
    ]
    copies[0].start()
    copies[1].start()
    gate_col = gate_col[...]
    copies[0].wait()
    copies[2].start()
    copies[3].start()
    copies[1].wait()
    blocks = anc_all // anc_rows
    sent = sent_width // anc_rows
    for p in range(blocks):
        rows_p = slice(p * anc_rows, (p + 1) * anc_rows)
        first = min(sent, blocks - p)
        anc_v[rows_p, p * anc_rows : (p + first) * anc_rows] = sent_v[rows_p, : first * anc_rows]
        if first < sent:
            anc_v[rows_p, : (sent - first) * anc_rows] = sent_v[rows_p, first * anc_rows : sent_width]
        for q in range(blocks):
            k = (q - p) % blocks
            if k >= sent:
                k = (p - q) % blocks
                part = sent_v[q * anc_rows : (q + 1) * anc_rows, k * anc_rows : (k + 1) * anc_rows]
                anc_v[rows_p, q * anc_rows : (q + 1) * anc_rows] = (
                    part.astype(jnp.float32).T.astype(jnp.bfloat16)
                )
    anc_here = anc_v[pl.ds(pl.multiple_of(row * anc_rows, 8), anc_rows), :]
    lower = lower_v[...]
    rows = (-jnp.dot(anc_here * gate_col, lower, preferred_element_type=jnp.float32)).astype(
        jnp.bfloat16
    )
    rows_v[...] = rows
    offdiag_ref[...] = rows_v[:, pl.ds(pl.multiple_of(col * off_width, 128), off_width)]
    lower_cols = lower_v[:, pl.ds(pl.multiple_of(row * order_rows, 128), order_rows)]
    offdiag_t = (
        -jnp.dot(lower_cols.T * gate_col, anc_v[...], preferred_element_type=jnp.float32)
    ).astype(jnp.bfloat16)
    block = pivinv[...] - jnp.dot(offdiag_t * gate_col, lower, preferred_element_type=jnp.float32)
    block_ref[...] = block
    copies[2].wait()
    copies[3].wait()
    par_col, anc_col = par_col_ref[...], anc_col_ref[...]
    par, ancl = par_v[...], ancl_v[...]
    upper = jnp.dot(
        block.astype(jnp.bfloat16) * par_col, par, preferred_element_type=jnp.float32
    ) + jnp.dot(offdiag_t * anc_col, ancl, preferred_element_type=jnp.float32)
    par_block = (-upper).astype(jnp.bfloat16)
    lower_sum = jnp.dot(rows * par_col, par, preferred_element_type=jnp.float32) + jnp.dot(
        anc_here * anc_col, ancl, preferred_element_type=jnp.float32
    )
    anc_block = (-lower_sum).astype(jnp.bfloat16)
    par_ref[...] = par_block
    anc_ref[...] = anc_block
    par_own = par_v[pl.ds(pl.multiple_of(row * order_rows, 8), order_rows), :] * par_own_gate[...]
    ancl_own = ancl_v[pl.ds(pl.multiple_of(row * anc_rows, 8), anc_rows), :] * anc_own_gate[...]
    part = jnp.sum(
        par_own.astype(jnp.float32) * par_block.astype(jnp.float32), axis=0, keepdims=True
    ) + jnp.sum(ancl_own.astype(jnp.float32) * anc_block.astype(jnp.float32), axis=0, keepdims=True)
    part = jnp.where(row == 0, pivots[...] - part, -part)
    for i in range(part_ref.shape[0]):
        part_ref[i] = part


def local_whole(
    anc_inverse,
    parent_pivinv,
    parent_lower,
    parent_mask,
    leaf_lower_par,
    leaf_lower_anc,
    leaf_mask,
    leaf_pivots,
):
    row_index = lax.axis_index("row")
    row_devices = lax.axis_size("row")
    col_index = lax.axis_index("col")
    anc_rows = anc_inverse.shape[0]
    order_rows = parent_pivinv.shape[0]
    col_width = leaf_pivots.shape[0]
    off_width = parent_lower.shape[1] // 2
    half = anc_rows // 2
    anc_all = anc_rows * row_devices
    order_all = order_rows * row_devices

    sent_width = (row_devices // 2 + 1) * anc_rows
    piece_width = sent_width + order_all + 2 * leaf_lower_par.shape[1]
    piece = pl.pallas_call(
        piece_kernel,
        out_shape=jax.ShapeDtypeStruct((half, piece_width), jnp.bfloat16),
        in_specs=[pl.BlockSpec(memory_space=pltpu.VMEM)] * 4,
        out_specs=pl.BlockSpec(memory_space=pltpu.VMEM),
    )(anc_inverse, parent_lower, leaf_lower_par, leaf_lower_anc)
    full = lax.all_gather(piece, ("row", "col"), axis=0, tiled=True)
    parent_gate = jnp.repeat(parent_mask, BLOCK).astype(jnp.bfloat16)[:, None]
    leaf_gate = jnp.repeat(leaf_mask, BLOCK).astype(jnp.bfloat16)[:, None]
    vmem = pl.BlockSpec(memory_space=pltpu.VMEM)
    flops = 2 * (3 * order_rows * anc_all * order_all + 4 * order_rows * anc_all * col_width)
    block, offdiag_own, par_block, anc_block, parts = pl.pallas_call(
        leaf_kernel,
        out_shape=(
            jax.ShapeDtypeStruct((order_rows, order_all), jnp.float32),
            jax.ShapeDtypeStruct((anc_rows, off_width), jnp.bfloat16),
            jax.ShapeDtypeStruct((order_rows, col_width), jnp.bfloat16),
            jax.ShapeDtypeStruct((anc_rows, col_width), jnp.bfloat16),
            jax.ShapeDtypeStruct((row_devices, 1, col_width), jnp.float32),
        ),
        in_specs=[vmem] * 6
        + [pl.BlockSpec(memory_space=pl.ANY)]
        + [vmem],
        out_specs=(vmem,) * 5,
        scratch_shapes=[
            pltpu.VMEM((anc_all, sent_width), jnp.bfloat16),
            pltpu.VMEM((anc_all, anc_all), jnp.bfloat16),
            pltpu.VMEM((anc_all, order_all), jnp.bfloat16),
            pltpu.VMEM((order_all, col_width), jnp.bfloat16),
            pltpu.VMEM((anc_all, col_width), jnp.bfloat16),
            pltpu.VMEM((anc_rows, order_all), jnp.bfloat16),
            pltpu.SemaphoreType.DMA((4,)),
        ],
        cost_estimate=pl.CostEstimate(
            flops=flops, transcendentals=0, bytes_accessed=full.size + 8 * anc_rows * order_all
        ),
    )(
        parent_gate.T,
        leaf_gate[:order_all].T,
        leaf_gate[order_all:].T,
        lax.dynamic_slice_in_dim(leaf_gate[:order_all], row_index * order_rows, order_rows),
        lax.dynamic_slice_in_dim(leaf_gate[order_all:], row_index * anc_rows, anc_rows),
        leaf_pivots[None, :],
        full,
        parent_pivinv,
    )
    density = jnp.sum(lax.all_to_all(parts, "row", 0, 0, tiled=True), axis=0)[0]
    return block, offdiag_own, par_block, anc_block, density


def fits_whole(mesh, anc_rows, order_rows):
    anc_all = anc_rows * mesh.shape["row"]
    return (
        anc_rows == order_rows
        and anc_rows % 128 == 0
        and anc_all * anc_all * 2 <= 16 * 1024 * 1024
    )


def solution(mesh):
    placed = (
        P(("pole", "row"), None),
        P(("pole", "row"), None),
        P(("pole", "row"), None),
        P(),
        P(("pole", "row"), None),
        P(("pole", "row"), None),
        P(),
        P(("pole", "col")),
    )
    placed_out = (
        P(("pole", "row"), None),
        P(("pole", "row"), "col"),
        P(("pole", "row"), "col"),
        P(("pole", "row"), "col"),
        P(("pole", "col")),
    )
    shards = mesh.shape["pole"] * mesh.shape["row"]

    def run(*args):
        anc_rows = args[0].shape[0] // shards
        order_rows = args[1].shape[0] // shards
        body = local_whole if fits_whole(mesh, anc_rows, order_rows) else local
        return jax.shard_map(
            body, mesh=mesh, in_specs=placed, out_specs=placed_out, check_vma=False
        )(*args)

    return run
```

```python
import jax
import jax.numpy as jnp
from jax import lax
from jax.experimental import pallas as pl
from jax.experimental.pallas import tpu as pltpu
from jax.sharding import PartitionSpec as P

BLOCK = 256
ORDER = 1024


def local(
    anc_inverse,
    parent_pivinv,
    parent_lower,
    parent_mask,
    leaf_lower_par,
    leaf_lower_anc,
    leaf_mask,
    leaf_pivots,
):
    row_index = lax.axis_index("row")
    row_devices = lax.axis_size("row")
    col_index = lax.axis_index("col")
    anc_rows = anc_inverse.shape[0]
    order_rows = parent_pivinv.shape[0]
    col_width = leaf_pivots.shape[0]
    parent_gate = lax.dynamic_slice_in_dim(
        jnp.repeat(parent_mask, BLOCK), row_index * anc_rows, anc_rows
    )
    lower_one = parent_lower * parent_gate[:, None].astype(jnp.bfloat16)
    lower_half = lax.dynamic_slice_in_dim(lower_one, col_index * col_width, col_width, 1)
    leaf_gate = jnp.repeat(leaf_mask, BLOCK)
    gate_par = lax.dynamic_slice_in_dim(leaf_gate[:ORDER], row_index * order_rows, order_rows)
    gate_anc = lax.dynamic_slice_in_dim(leaf_gate[ORDER:], row_index * anc_rows, anc_rows)
    leaf_local = jnp.concatenate(
        [
            leaf_lower_par * gate_par[:, None].astype(jnp.bfloat16),
            leaf_lower_anc * gate_anc[:, None].astype(jnp.bfloat16),
        ],
        axis=0,
    )
    leaf_half = lax.dynamic_slice_in_dim(leaf_local, col_index * col_width, col_width, 1)
    columns = anc_inverse
    product = jnp.dot(
        columns,
        lax.all_gather(lower_half, "row", axis=0, tiled=True),
        preferred_element_type=jnp.float32,
    )
    parent_offdiag = (-product).astype(jnp.bfloat16)
    offdiag_rows = lax.all_gather(parent_offdiag, "col", axis=1, tiled=True)
    columns = lower_one
    diag_sums = lax.psum_scatter(
        lax.dot_general(
            columns, offdiag_rows, (((0,), (0,)), ((), ())), preferred_element_type=jnp.float32
        ),
        "row",
        scatter_dimension=0,
        tiled=True,
    )
    parent_block = parent_pivinv - diag_sums
    parent_round = parent_block.astype(jnp.bfloat16)
    mirrored = lax.all_to_all(offdiag_rows, "row", split_axis=1, concat_axis=0, tiled=True).T
    upper_rows = jnp.concatenate(
        [
            parent_round.reshape(order_rows, row_devices, order_rows),
            mirrored.reshape(order_rows, row_devices, anc_rows),
        ],
        axis=2,
    )
    lower_rows = jnp.concatenate(
        [
            offdiag_rows.reshape(anc_rows, row_devices, order_rows),
            anc_inverse.reshape(anc_rows, row_devices, anc_rows),
        ],
        axis=2,
    )
    inverse_rows = jnp.concatenate(
        [upper_rows.reshape(order_rows, -1), lower_rows.reshape(anc_rows, -1)], axis=0
    )
    columns = inverse_rows
    leaf_product = jnp.dot(
        columns,
        lax.all_gather(leaf_half, "row", axis=0, tiled=True),
        preferred_element_type=jnp.float32,
    )
    leaf_result = (-leaf_product).astype(jnp.bfloat16)
    partial_sums = jnp.sum(leaf_half.astype(jnp.float32) * leaf_result.astype(jnp.float32), axis=0)
    density = leaf_pivots - lax.psum(partial_sums, "row")
    return (
        parent_block,
        parent_offdiag,
        leaf_result[:order_rows],
        leaf_result[order_rows:],
        density,
    )


def piece_kernel(parent_mask, leaf_mask, anc_hbm, lower_hbm, par_hbm, ancl_hbm, out_ref):
    row, col = lax.axis_index("row"), lax.axis_index("col")
    half = out_ref.shape[0]
    blk = anc_hbm.shape[0]
    blocks = anc_hbm.shape[1] // blk
    sent = blocks // 2 + 1
    rows = pl.ds(pl.multiple_of(col * half, 8), half)
    for k in range(sent):
        start = pl.multiple_of(lax.rem(row + k, blocks) * blk, 128)
        out_ref[:, k * blk : (k + 1) * blk] = anc_hbm[rows, pl.ds(start, blk)]
    at = sent * blk
    first_row = row * blk + col * half
    order_blocks = par_hbm.shape[0] * blocks // BLOCK
    gates = (
        parent_mask[first_row // BLOCK],
        leaf_mask[first_row // BLOCK],
        leaf_mask[order_blocks + first_row // BLOCK],
    )
    for source, gate in zip((lower_hbm, par_hbm, ancl_hbm), gates):
        width = source.shape[1]
        out_ref[:, at : at + width] = source[rows, :] * gate.astype(jnp.float32).astype(jnp.bfloat16)
        at += width


def leaf_kernel(
    pivots, full_hbm, anc_local, pivinv,
    block_ref, offdiag_ref, par_ref, anc_ref, part_ref,
    sent_v, anc_v, lower_v, par_v, ancl_v, rows_v, sem,
):
    row, col = lax.axis_index("row"), lax.axis_index("col")
    anc_all, order_all = anc_v.shape[0], lower_v.shape[1]
    width = par_v.shape[1]
    order_rows, anc_rows = block_ref.shape[0], anc_local.shape[0]
    off_width = offdiag_ref.shape[1]
    sent_width = sent_v.shape[1]
    leaf_at = sent_width + order_all
    leaf_width = (full_hbm.shape[1] - leaf_at) // 2
    copies = [
        pltpu.make_async_copy(full_hbm.at[:, pl.ds(sent_width, order_all)], lower_v, sem.at[1]),
        pltpu.make_async_copy(full_hbm.at[:, pl.ds(0, sent_width)], sent_v, sem.at[0]),
        pltpu.make_async_copy(
            full_hbm.at[:, pl.ds(pl.multiple_of(leaf_at + col * width, 128), width)], par_v, sem.at[2]
        ),
        pltpu.make_async_copy(
            full_hbm.at[:, pl.ds(pl.multiple_of(leaf_at + leaf_width + col * width, 128), width)],
            ancl_v,
            sem.at[3],
        ),
    ]
    copies[0].start()
    copies[1].start()
    anc_here = anc_local[...]
    copies[0].wait()
    copies[2].start()
    copies[3].start()
    lower = lower_v[...]
    rows = (-jnp.dot(anc_here, lower, preferred_element_type=jnp.float32)).astype(
        jnp.bfloat16
    )
    rows_v[...] = rows
    offdiag_ref[...] = rows_v[:, pl.ds(pl.multiple_of(col * off_width, 128), off_width)]
    copies[1].wait()
    blocks = anc_all // anc_rows
    sent = sent_width // anc_rows
    for p in range(blocks):
        rows_p = slice(p * anc_rows, (p + 1) * anc_rows)
        first = min(sent, blocks - p)
        anc_v[rows_p, p * anc_rows : (p + first) * anc_rows] = sent_v[rows_p, : first * anc_rows]
        if first < sent:
            anc_v[rows_p, : (sent - first) * anc_rows] = sent_v[rows_p, first * anc_rows : sent_width]
        for q in range(blocks):
            k = (q - p) % blocks
            if k >= sent:
                k = (p - q) % blocks
                part = sent_v[q * anc_rows : (q + 1) * anc_rows, k * anc_rows : (k + 1) * anc_rows]
                anc_v[rows_p, q * anc_rows : (q + 1) * anc_rows] = (
                    part.astype(jnp.float32).T.astype(jnp.bfloat16)
                )
    lower_cols = lower_v[:, pl.ds(pl.multiple_of(row * order_rows, 128), order_rows)]
    offdiag_t = (
        -jnp.dot(lower_cols.T, anc_v[...], preferred_element_type=jnp.float32)
    ).astype(jnp.bfloat16)
    block = pivinv[...] - jnp.dot(offdiag_t, lower, preferred_element_type=jnp.float32)
    block_ref[...] = block
    copies[2].wait()
    copies[3].wait()
    par, ancl = par_v[...], ancl_v[...]
    upper = jnp.dot(
        block.astype(jnp.bfloat16), par, preferred_element_type=jnp.float32
    ) + jnp.dot(offdiag_t, ancl, preferred_element_type=jnp.float32)
    par_block = (-upper).astype(jnp.bfloat16)
    lower_sum = jnp.dot(rows, par, preferred_element_type=jnp.float32) + jnp.dot(
        anc_here, ancl, preferred_element_type=jnp.float32
    )
    anc_block = (-lower_sum).astype(jnp.bfloat16)
    par_ref[...] = par_block
    anc_ref[...] = anc_block
    par_own = par_v[pl.ds(pl.multiple_of(row * order_rows, 8), order_rows), :]
    ancl_own = ancl_v[pl.ds(pl.multiple_of(row * anc_rows, 8), anc_rows), :]
    part = jnp.sum(
        par_own.astype(jnp.float32) * par_block.astype(jnp.float32), axis=0, keepdims=True
    ) + jnp.sum(ancl_own.astype(jnp.float32) * anc_block.astype(jnp.float32), axis=0, keepdims=True)
    part = jnp.where(row == 0, pivots[...] - part, -part)
    for i in range(part_ref.shape[0]):
        part_ref[i] = part


def local_whole(
    anc_inverse,
    parent_pivinv,
    parent_lower,
    parent_mask,
    leaf_lower_par,
    leaf_lower_anc,
    leaf_mask,
    leaf_pivots,
):
    row_index = lax.axis_index("row")
    row_devices = lax.axis_size("row")
    col_index = lax.axis_index("col")
    anc_rows = anc_inverse.shape[0]
    order_rows = parent_pivinv.shape[0]
    col_width = leaf_pivots.shape[0]
    off_width = parent_lower.shape[1] // 2
    half = anc_rows // 2
    anc_all = anc_rows * row_devices
    order_all = order_rows * row_devices

    sent_width = (row_devices // 2 + 1) * anc_rows
    piece_width = sent_width + order_all + 2 * leaf_lower_par.shape[1]
    piece = pl.pallas_call(
        piece_kernel,
        out_shape=jax.ShapeDtypeStruct((half, piece_width), jnp.bfloat16),
        in_specs=[pl.BlockSpec(memory_space=pltpu.SMEM)] * 2
        + [pl.BlockSpec(memory_space=pltpu.VMEM)] * 4,
        out_specs=pl.BlockSpec(memory_space=pltpu.VMEM),
    )(parent_mask, leaf_mask, anc_inverse, parent_lower, leaf_lower_par, leaf_lower_anc)
    full = lax.all_gather(piece, ("row", "col"), axis=0, tiled=True)
    parent_gate = jnp.repeat(parent_mask, BLOCK).astype(jnp.bfloat16)[:, None]
    leaf_gate = jnp.repeat(leaf_mask, BLOCK).astype(jnp.bfloat16)[:, None]
    vmem = pl.BlockSpec(memory_space=pltpu.VMEM)
    flops = 2 * (3 * order_rows * anc_all * order_all + 4 * order_rows * anc_all * col_width)
    block, offdiag_own, par_block, anc_block, parts = pl.pallas_call(
        leaf_kernel,
        out_shape=(
            jax.ShapeDtypeStruct((order_rows, order_all), jnp.float32),
            jax.ShapeDtypeStruct((anc_rows, off_width), jnp.bfloat16),
            jax.ShapeDtypeStruct((order_rows, col_width), jnp.bfloat16),
            jax.ShapeDtypeStruct((anc_rows, col_width), jnp.bfloat16),
            jax.ShapeDtypeStruct((row_devices, 1, col_width), jnp.float32),
        ),
        in_specs=[vmem]
        + [pl.BlockSpec(memory_space=pl.ANY)]
        + [vmem] * 2,
        out_specs=(vmem,) * 5,
        scratch_shapes=[
            pltpu.VMEM((anc_all, sent_width), jnp.bfloat16),
            pltpu.VMEM((anc_all, anc_all), jnp.bfloat16),
            pltpu.VMEM((anc_all, order_all), jnp.bfloat16),
            pltpu.VMEM((order_all, col_width), jnp.bfloat16),
            pltpu.VMEM((anc_all, col_width), jnp.bfloat16),
            pltpu.VMEM((anc_rows, order_all), jnp.bfloat16),
            pltpu.SemaphoreType.DMA((4,)),
        ],
        cost_estimate=pl.CostEstimate(
            flops=flops, transcendentals=0, bytes_accessed=full.size + 8 * anc_rows * order_all
        ),
    )(
        leaf_pivots[None, :],
        full,
        anc_inverse,
        parent_pivinv,
    )
    density = jnp.sum(lax.all_to_all(parts, "row", 0, 0, tiled=True), axis=0)[0]
    return block, offdiag_own, par_block, anc_block, density


def fits_whole(mesh, anc_rows, order_rows):
    anc_all = anc_rows * mesh.shape["row"]
    return (
        anc_rows == order_rows
        and anc_rows % 128 == 0
        and BLOCK % (anc_rows // 2) == 0
        and anc_all * anc_all * 2 <= 16 * 1024 * 1024
    )


def solution(mesh):
    placed = (
        P(("pole", "row"), None),
        P(("pole", "row"), None),
        P(("pole", "row"), None),
        P(),
        P(("pole", "row"), None),
        P(("pole", "row"), None),
        P(),
        P(("pole", "col")),
    )
    placed_out = (
        P(("pole", "row"), None),
        P(("pole", "row"), "col"),
        P(("pole", "row"), "col"),
        P(("pole", "row"), "col"),
        P(("pole", "col")),
    )
    shards = mesh.shape["pole"] * mesh.shape["row"]

    def run(*args):
        anc_rows = args[0].shape[0] // shards
        order_rows = args[1].shape[0] // shards
        body = local_whole if fits_whole(mesh, anc_rows, order_rows) else local
        return jax.shard_map(
            body, mesh=mesh, in_specs=placed, out_specs=placed_out, check_vma=False
        )(*args)

    return run
```
